32 devices in a mesh: rec: 4 (over y, x), seq: 8 (over z, core).
Axes of the slice: x: 2, y: 2, z: 4, core: 2. Of those that a mesh axis runs over, the one named last changes fastest.
Arguments:
- owned_rows: bfloat16 [4, 2048, 1024], P('rec', 'seq'), may hold values from -20 to 20
- seq_position: int32 [4, 2048], P('rec', 'seq'), may hold values from 0 to 2047, as said below
- head_weights: bfloat16 [1024, 8, 128], replicated, may hold values from -0.1875 to 0.1875
- key_blocks: int32 [1, 16, 8], replicated, may hold values from 0 to 15, as said below
- key_counts: int32 [1, 16], replicated, may hold values from 1 to 8, as said below
- out_grad: bfloat16 [4, 8, 2048, 64], P('rec', None, 'seq'), may hold values from -6 to 6
Outputs:
- attention: bfloat16 [4, 8, 2048, 64], P('rec', None, 'seq')
- seq_grad: bfloat16 [4, 2048, 1024], P('rec', 'seq')
- weight_grad: float32 [1024, 8, 128], P(('rec', 'seq'))
The draws below stay inside these ranges and needn't reach their ends.
Inputs may be any that keep to these rules, and one draw needn't show every extreme that they name: `seq_position`: in each recording every position appears once. The rows of one index of seq go to each index of seq (positions p with the same p // 256) between 1 and 63 times, and in every recording some index sends exactly 63 rows to some index. `key_blocks`: each list holds 8 different block numbers of the same spatial group, the query block's own number first; only the first key_counts entries are used. `key_counts`: every spatial group has a query block that uses all 8 listed blocks.
All inputs are finite; a program needn't handle non-finite values.
Results may differ from the reference program's by a relative error of at most 0.012.
Values may be sent and summed in bfloat16 or wider, within the bound.
No kernel may reach another device: no remote copies, remote signals or barrier semaphores. Data moves between devices by JAX's collectives and lax.ppermute only.
A program may use at most 64 MiB of HBM per device.

```python
import jax
import jax.numpy as jnp
from jax import lax

D = 1024
HEADS = 8
HDIM = 64
TOK_DEV = 256
BLOCK = 128
KB = 8
RECS = 4
VIS = 2048
GROUPS = 1
PART = 256
GSEQ = 2048
QB = 16
N_SEQ = 8


def draw_owned_rows(key, part):
    first_key = jax.random.fold_in(key, 0)
    return jnp.clip(jax.random.normal(first_key, (RECS, VIS, D), jnp.float32), -6.0, 6.0).astype(jnp.bfloat16)


def one_layout(subkey):
    first_key, second_key, third_key, fourth_key = jax.random.split(subkey, 4)
    average = TOK_DEV // N_SEQ
    halves = N_SEQ // 2
    first_runs = jax.random.randint(first_key, (halves,), 1, 2 * average)
    first_runs = first_runs.at[0].set(1)
    second_runs = 2 * average - first_runs
    run_lengths = jnp.stack([first_runs, second_runs], axis=1).reshape(-1)
    run_ends = jnp.cumsum(run_lengths)
    slots = jnp.arange(TOK_DEV, dtype=jnp.int32)
    run_of_slot = jnp.sum((slots[:, None] >= run_ends[None, :]).astype(jnp.int32), axis=1)
    shifts = jax.random.permutation(second_key, N_SEQ)
    relabel = jax.random.permutation(third_key, N_SEQ)
    holders = jnp.arange(N_SEQ, dtype=jnp.int32)
    owner_of = relabel[(holders[:, None] + shifts[run_of_slot][None, :]) % N_SEQ]
    positions = holders[:, None] * TOK_DEV + slots[None, :]
    shuffle = jax.random.permutation(fourth_key, VIS)
    ranking = owner_of.reshape(-1).astype(jnp.int32) * VIS + shuffle.astype(jnp.int32)
    order = jnp.argsort(ranking)
    return positions.reshape(-1)[order].astype(jnp.int32)


def draw_seq_position(key, part):
    record_keys = jax.vmap(lambda number: jax.random.fold_in(key, number))(jnp.arange(RECS))
    return jax.vmap(one_layout)(record_keys)


def draw_key_blocks(key, part):
    row_keys = jax.random.split(jax.random.fold_in(key, 11), GROUPS * QB)

    def one_list(row_key):
        return jax.random.permutation(row_key, QB - 1)[:KB - 1] + 1
    offsets = jax.vmap(one_list)(row_keys).reshape(GROUPS, QB, KB - 1)
    offsets = jnp.concatenate([jnp.zeros((GROUPS, QB, 1), jnp.int32), offsets.astype(jnp.int32)], axis=2)
    own = jnp.arange(QB, dtype=jnp.int32)[None, :, None]
    return ((own + offsets) % QB).astype(jnp.int32)


def draw_key_counts(key, part):
    first_key, second_key, third_key = jax.random.split(jax.random.fold_in(key, 23), 3)
    levels = jax.random.randint(first_key, (GROUPS, 1), 1, KB + 1)
    counts = jax.random.randint(second_key, (GROUPS, QB), 1, levels + 1)
    full_at = jax.random.randint(third_key, (GROUPS,), 0, QB)
    counts = counts.at[jnp.arange(GROUPS), full_at].set(KB)
    return counts.astype(jnp.int32)


def shard_levels(own_key, extent, cuts, smallest, largest):
    loudness, own = 1.0, jax.random.fold_in(own_key, 6)
    for axis_at, parts in cuts:
        draws = jnp.exp(jax.random.uniform(jax.random.fold_in(own, axis_at), (parts,), jnp.float32, smallest / len(cuts), largest / len(cuts)))
        loudness = loudness * jnp.repeat(draws, extent[axis_at] // parts).reshape([-1 if axis == axis_at else 1 for axis in range(len(extent))])
    return loudness


def bell_draw(own_key, shape, deviation, bound, shards=(), held_as=jnp.bfloat16):
    gain = shard_levels(own_key, shape, shards, -0.22, 0.18) if shards else 1.0
    values = jax.random.normal(own_key, shape, jnp.float32) * deviation * gain
    return jnp.minimum(jnp.maximum(values, -bound), bound).astype(held_as)


def setup_inputs(seed: int = 0) -> dict:
    streams_of = jax.random.split(jax.random.key(seed), 7)
    return {
        "owned_rows": draw_owned_rows(jax.random.fold_in(streams_of[6], 71), 0),
        "seq_position": draw_seq_position(jax.random.fold_in(streams_of[6], 71), 0),
        "head_weights": bell_draw(streams_of[2], (D, HEADS, 2 * HDIM), D ** -0.5, 0.1875),
        "key_blocks": draw_key_blocks(jax.random.fold_in(streams_of[6], 71), 0),
        "key_counts": draw_key_counts(jax.random.fold_in(streams_of[6], 71), 0),
        "out_grad": bell_draw(streams_of[5], (RECS, HEADS, VIS, HDIM), 1.0, 6.0, ((0, 4), (2, 8))),
    }


def to_groups(values):
    width = values.shape[2]
    shaped = values.reshape(N_SEQ, GROUPS, PART, HEADS, width)
    shaped = jnp.transpose(shaped, (3, 1, 0, 2, 4))
    return shaped.reshape(HEADS * GROUPS, GSEQ, width)


def from_groups(values):
    width = values.shape[2]
    shaped = values.reshape(HEADS, GROUPS, N_SEQ, PART, width)
    shaped = jnp.transpose(shaped, (2, 1, 3, 0, 4))
    return shaped.reshape(VIS, HEADS, width)


def attend_block(shared, values, grad_rows, lists, counts):
    scale = HDIM ** -0.5
    key_tiles = shared.reshape(QB, BLOCK, HDIM).astype(jnp.float32)
    value_tiles = values.reshape(QB, BLOCK, HDIM).astype(jnp.float32)
    grad_tiles = grad_rows.reshape(QB, BLOCK, HDIM).astype(jnp.float32)

    def advance(carry, number):
        acc_keys, acc_values = carry
        query = key_tiles[number]
        upstream = grad_tiles[number]
        chosen = lists[number]
        near_keys = key_tiles[chosen].reshape(KB * BLOCK, HDIM)
        near_values = value_tiles[chosen].reshape(KB * BLOCK, HDIM)
        usable = jnp.repeat(jnp.arange(KB) < counts[number], BLOCK)[None, :]
        scores = scale * jnp.einsum("qc,kc->qk", query, near_keys)
        scores = jnp.where(usable, scores, -jnp.inf)
        peak = jnp.max(scores, axis=1, keepdims=True)
        weights = jnp.where(usable, jnp.exp(scores - peak), 0.0)
        probs = weights / jnp.sum(weights, axis=1, keepdims=True)
        probs_low = probs.astype(jnp.bfloat16).astype(jnp.float32)
        mixed = jnp.einsum("qk,kc->qc", probs_low, near_values).astype(jnp.bfloat16)
        dprobs = jnp.einsum("qc,kc->qk", upstream, near_values)
        inner = jnp.sum(probs * dprobs, axis=1, keepdims=True)
        dscores = (scale * probs * (dprobs - inner)).astype(jnp.bfloat16).astype(jnp.float32)
        dquery = jnp.einsum("qk,kc->qc", dscores, near_keys)
        dkeys = jnp.einsum("qk,qc->kc", dscores, query).reshape(KB, BLOCK, HDIM)
        dvalues = jnp.einsum("qk,qc->kc", probs_low, upstream).reshape(KB, BLOCK, HDIM)
        return (acc_keys.at[chosen].add(dkeys), acc_values.at[chosen].add(dvalues)), (mixed, dquery)

    zeros = jnp.zeros((QB, BLOCK, HDIM), jnp.float32)
    (acc_keys, acc_values), (mixed, dquery) = lax.scan(advance, (zeros, zeros), jnp.arange(QB))
    grad_qk = (dquery.reshape(GSEQ, HDIM) + acc_keys.reshape(GSEQ, HDIM)).astype(jnp.bfloat16)
    grad_v = acc_values.reshape(GSEQ, HDIM).astype(jnp.bfloat16)
    return mixed.reshape(GSEQ, HDIM), jnp.concatenate([grad_qk, grad_v], axis=1)


def reference(owned_rows, seq_position, head_weights, key_blocks, key_counts, out_grad):
    weights_f = head_weights.astype(jnp.float32)
    owners = jnp.arange(HEADS * GROUPS) % GROUPS
    lists_all = key_blocks[owners]
    counts_all = key_counts[owners]

    def one_recording(record):
        rows, places, upstream = record
        tokens = jnp.zeros((VIS, D), jnp.bfloat16).at[places].set(rows)
        proj = jnp.einsum("td,dhc->thc", tokens.astype(jnp.float32), weights_f).astype(jnp.bfloat16)
        grouped = to_groups(proj)
        grad_grouped = to_groups(jnp.transpose(upstream, (1, 0, 2)))

        def per_item(item):
            both, grad_rows, lists, counts = item
            return attend_block(both[:, :HDIM], both[:, HDIM:], grad_rows, lists, counts)

        mixed, grads = lax.map(per_item, (grouped, grad_grouped, lists_all, counts_all))
        output = jnp.transpose(from_groups(mixed), (1, 0, 2))
        grad_proj = from_groups(grads)
        grad_tokens = jnp.einsum("thc,dhc->td", grad_proj.astype(jnp.float32), weights_f).astype(jnp.bfloat16)
        term = jnp.einsum("td,thc->dhc", tokens.astype(jnp.float32), grad_proj.astype(jnp.float32))
        return output, grad_tokens, term

    outputs, grad_tokens, terms = lax.map(one_recording, (owned_rows, seq_position, out_grad))
    return outputs, grad_tokens, jnp.sum(terms, axis=0)
```

```python
import jax
import jax.numpy as jnp
from jax import lax
from jax.sharding import PartitionSpec as P
from jax.experimental import pallas as pl
from jax.experimental.pallas import tpu as pltpu

BLOCK = 128


def attention_kernel(lists_ref, counts_ref, both_ref, grad_ref, out_ref, back_ref, acc_ref):
    nblocks, listed = lists_ref.shape
    depth = grad_ref.shape[1]
    scale = depth ** (-0.5)
    acc_ref[...] = jnp.zeros(acc_ref.shape, jnp.float32)
    col_block = lax.broadcasted_iota(jnp.int32, (BLOCK, listed * BLOCK), 1) // BLOCK
    trans_a = (((0,), (0,)), ((), ()))
    trans_b = (((1,), (1,)), ((), ()))

    def one_block(a, carry):
        start = pl.multiple_of(a * BLOCK, BLOCK)
        own = both_ref[pl.ds(start, BLOCK), :]
        query = own[:, :depth]
        upstream = grad_ref[pl.ds(start, BLOCK), :]
        active = counts_ref[a]
        picks = [jnp.clip(lists_ref[a, j], 0, nblocks - 1) for j in range(listed)]
        tiles = [both_ref[pl.ds(pl.multiple_of(b * BLOCK, BLOCK), BLOCK), :] for b in picks]
        keys = [t[:, :depth] for t in tiles]
        values = [t[:, depth:] for t in tiles]
        scores = jnp.concatenate(
            [lax.dot_general(query, k, trans_b, preferred_element_type=jnp.float32) for k in keys],
            axis=1,
        ) * scale
        usable = col_block < active
        scores = jnp.where(usable, scores, -jnp.inf)
        peak = jnp.max(scores, axis=1, keepdims=True)
        weights = jnp.where(usable, jnp.exp(scores - peak), 0.0)
        probs = weights / jnp.sum(weights, axis=1, keepdims=True)
        probs_low = probs.astype(jnp.bfloat16)
        dprobs = jnp.concatenate(
            [lax.dot_general(upstream, v, trans_b, preferred_element_type=jnp.float32) for v in values],
            axis=1,
        )
        inner = jnp.sum(probs * dprobs, axis=1, keepdims=True)
        dscores = (scale * probs * (dprobs - inner)).astype(jnp.bfloat16)
        mixed = jnp.zeros((BLOCK, depth), jnp.float32)
        dquery = jnp.zeros((BLOCK, depth), jnp.float32)
        for j in range(listed):
            cols = slice(j * BLOCK, (j + 1) * BLOCK)
            mixed = mixed + jnp.dot(probs_low[:, cols], values[j], preferred_element_type=jnp.float32)
            dquery = dquery + jnp.dot(dscores[:, cols], keys[j], preferred_element_type=jnp.float32)
        out_ref[pl.ds(start, BLOCK), :] = mixed.astype(out_ref.dtype)
        for j in range(listed):
            cols = slice(j * BLOCK, (j + 1) * BLOCK)
            dkeys = lax.dot_general(dscores[:, cols], query, trans_a, preferred_element_type=jnp.float32)
            dvalues = lax.dot_general(probs_low[:, cols], upstream, trans_a, preferred_element_type=jnp.float32)
            if j == 0:
                dkeys = dkeys + dquery

            @pl.when(j < active)
            def _():
                rows = pl.ds(pl.multiple_of(picks[j] * BLOCK, BLOCK), BLOCK)
                acc_ref[rows, :] += jnp.concatenate([dkeys, dvalues], axis=1)

        return carry

    lax.fori_loop(0, nblocks, one_block, 0)
    back_ref[...] = acc_ref[...].astype(back_ref.dtype)


def attend_group(both, grad_rows, lists, counts):
    total, width = both.shape
    depth = grad_rows.shape[1]
    smem = pltpu.MemorySpace.SMEM
    vmem = pltpu.MemorySpace.VMEM
    return pl.pallas_call(
        attention_kernel,
        out_shape=(
            jax.ShapeDtypeStruct((total, depth), jnp.bfloat16),
            jax.ShapeDtypeStruct((total, width), jnp.bfloat16),
        ),
        in_specs=[
            pl.BlockSpec(memory_space=smem),
            pl.BlockSpec(memory_space=smem),
            pl.BlockSpec(memory_space=vmem),
            pl.BlockSpec(memory_space=vmem),
        ],
        out_specs=(pl.BlockSpec(memory_space=vmem), pl.BlockSpec(memory_space=vmem)),
        scratch_shapes=[pltpu.VMEM((total, width), jnp.float32)],
    )(lists, counts, both, grad_rows)


def local(owned_rows, seq_position, head_weights, key_blocks, key_counts, out_grad):
    seq_count = lax.axis_size("seq")
    my_index = lax.axis_index("seq")
    tokens_here = owned_rows.shape[1]
    width = owned_rows.shape[2]
    heads = head_weights.shape[1]
    depth = head_weights.shape[2] // 2
    groups = seq_count // heads
    portion = tokens_here // groups
    room = 2 * tokens_here // seq_count - 1
    rows_here = owned_rows[0]
    targets = seq_position[0]
    holders = targets // tokens_here
    order_ids = jnp.arange(tokens_here)
    earlier = order_ids[None, :] < order_ids[:, None]
    same_holder = holders[:, None] == holders[None, :]
    ranked = jnp.sum((earlier & same_holder).astype(jnp.int32), axis=1)
    slot_ids = holders * room + ranked
    outgoing = jnp.zeros((seq_count * room, width), rows_here.dtype).at[slot_ids].set(rows_here)
    outgoing = outgoing.reshape(seq_count, room, width)
    labels = (
        jnp.full((seq_count * room,), -1, jnp.int32)
        .at[slot_ids]
        .set(targets)
        .reshape(seq_count, room)
    )
    arrived, arrived_pos = (
        lax.all_to_all(outgoing, "seq", split_axis=0, concat_axis=0, tiled=True),
        lax.all_to_all(labels, "seq", split_axis=0, concat_axis=0, tiled=True),
    )
    local_ids = jnp.where(
        arrived_pos >= 0, arrived_pos - my_index * tokens_here, tokens_here
    ).reshape(-1)
    tokens = (
        jnp.zeros((tokens_here, width), rows_here.dtype)
        .at[local_ids]
        .set(arrived.reshape(-1, width), mode="drop")
    )
    proj = jnp.einsum(
        "td,dhc->htc", tokens, head_weights, preferred_element_type=jnp.float32
    ).astype(jnp.bfloat16)
    sending = proj.reshape(seq_count, portion * 2 * depth)
    upstream = out_grad[0].reshape(seq_count, portion * depth)
    got, got_grad = (
        lax.all_to_all(sending, "seq", split_axis=0, concat_axis=0, tiled=True),
        lax.all_to_all(upstream, "seq", split_axis=0, concat_axis=0, tiled=True),
    )
    gathered = got.reshape(seq_count * portion, 2 * depth)
    grad_rows = got_grad.reshape(seq_count * portion, depth)
    group = my_index % groups
    mixed, grad_both = attend_group(gathered, grad_rows, key_blocks[group], key_counts[group])
    back_out, back_grad = (
        lax.all_to_all(
            mixed.reshape(seq_count, portion * depth),
            "seq",
            split_axis=0,
            concat_axis=0,
            tiled=True,
        ),
        lax.all_to_all(
            grad_both.reshape(seq_count, portion * 2 * depth),
            "seq",
            split_axis=0,
            concat_axis=0,
            tiled=True,
        ),
    )
    attention = back_out.reshape(heads, tokens_here, depth)[None]
    grad_proj = back_grad.reshape(heads, tokens_here, 2 * depth)
    seq_grad = jnp.einsum(
        "htc,dhc->td", grad_proj, head_weights, preferred_element_type=jnp.float32
    ).astype(jnp.bfloat16)[None]
    weight_grad = lax.psum_scatter(
        jnp.einsum("td,htc->dhc", tokens, grad_proj, preferred_element_type=jnp.float32),
        ("rec", "seq"),
        scatter_dimension=0,
        tiled=True,
    )
    return (attention, seq_grad, weight_grad)


def solution(mesh):
    placed = (P("rec", "seq", None), P("rec", "seq"), P(), P(), P(), P("rec", None, "seq", None))
    return jax.shard_map(
        local,
        mesh=mesh,
        in_specs=placed,
        out_specs=(
            P("rec", None, "seq", None),
            P("rec", "seq", None),
            P(("rec", "seq"), None, None),
        ),
        check_vma=False,
    )
```

```python
import jax
import jax.numpy as jnp
from jax import lax
from jax.sharding import PartitionSpec as P
from jax.experimental import pallas as pl
from jax.experimental.pallas import tpu as pltpu

BLOCK = 128


def attention_kernel(lists_ref, counts_ref, both_ref, grad_ref, out_ref, back_ref, acc_ref):
    nblocks, listed = lists_ref.shape
    depth = grad_ref.shape[1]
    scale = depth ** (-0.5)
    acc_ref[...] = jnp.zeros(acc_ref.shape, jnp.float32)
    col_block = lax.broadcasted_iota(jnp.int32, (BLOCK, listed * BLOCK), 1) // BLOCK
    trans_a = (((0,), (0,)), ((), ()))
    trans_b = (((1,), (1,)), ((), ()))

    def one_block(a, carry):
        start = pl.multiple_of(a * BLOCK, BLOCK)
        own = both_ref[pl.ds(start, BLOCK), :]
        query = own[:, :depth]
        upstream = grad_ref[pl.ds(start, BLOCK), :]
        active = counts_ref[a]
        picks = [jnp.clip(lists_ref[a, j], 0, nblocks - 1) for j in range(listed)]
        tiles = [both_ref[pl.ds(pl.multiple_of(b * BLOCK, BLOCK), BLOCK), :] for b in picks]
        keys = [t[:, :depth] for t in tiles]
        values = [t[:, depth:] for t in tiles]
        scores = jnp.concatenate(
            [lax.dot_general(query, k, trans_b, preferred_element_type=jnp.float32) for k in keys],
            axis=1,
        ) * scale
        usable = col_block < active
        scores = jnp.where(usable, scores, -jnp.inf)
        peak = jnp.max(scores, axis=1, keepdims=True)
        weights = jnp.where(usable, jnp.exp(scores - peak), 0.0)
        probs = weights / jnp.sum(weights, axis=1, keepdims=True)
        probs_low = probs.astype(jnp.bfloat16)
        dprobs = jnp.concatenate(
            [lax.dot_general(upstream, v, trans_b, preferred_element_type=jnp.float32) for v in values],
            axis=1,
        )
        inner = jnp.sum(probs * dprobs, axis=1, keepdims=True)
        dscores = (scale * probs * (dprobs - inner)).astype(jnp.bfloat16)
        mixed = jnp.zeros((BLOCK, depth), jnp.float32)
        dquery = jnp.zeros((BLOCK, depth), jnp.float32)
        for j in range(listed):
            cols = slice(j * BLOCK, (j + 1) * BLOCK)
            mixed = mixed + jnp.dot(probs_low[:, cols], values[j], preferred_element_type=jnp.float32)
            dquery = dquery + jnp.dot(dscores[:, cols], keys[j], preferred_element_type=jnp.float32)
        out_ref[pl.ds(start, BLOCK), :] = mixed.astype(out_ref.dtype)
        for j in range(listed):
            cols = slice(j * BLOCK, (j + 1) * BLOCK)
            dkeys = lax.dot_general(dscores[:, cols], query, trans_a, preferred_element_type=jnp.float32)
            dvalues = lax.dot_general(probs_low[:, cols], upstream, trans_a, preferred_element_type=jnp.float32)
            if j == 0:
                dkeys = dkeys + dquery

            @pl.when(j < active)
            def _():
                rows = pl.ds(pl.multiple_of(picks[j] * BLOCK, BLOCK), BLOCK)
                acc_ref[rows, :] += jnp.concatenate([dkeys, dvalues], axis=1)

        return carry

    lax.fori_loop(0, nblocks, one_block, 0)
    back_ref[...] = acc_ref[...].astype(back_ref.dtype)


def attend_group(both, grad_rows, lists, counts):
    total, width = both.shape
    depth = grad_rows.shape[1]
    smem = pltpu.MemorySpace.SMEM
    vmem = pltpu.MemorySpace.VMEM
    return pl.pallas_call(
        attention_kernel,
        out_shape=(
            jax.ShapeDtypeStruct((total, depth), jnp.bfloat16),
            jax.ShapeDtypeStruct((total, width), jnp.bfloat16),
        ),
        in_specs=[
            pl.BlockSpec(memory_space=smem),
            pl.BlockSpec(memory_space=smem),
            pl.BlockSpec(memory_space=vmem),
            pl.BlockSpec(memory_space=vmem),
        ],
        out_specs=(pl.BlockSpec(memory_space=vmem), pl.BlockSpec(memory_space=vmem)),
        scratch_shapes=[pltpu.VMEM((total, width), jnp.float32)],
    )(lists, counts, both, grad_rows)


def local(owned_rows, seq_position, head_weights, key_blocks, key_counts, out_grad):
    seq_count = lax.axis_size("seq")
    my_index = lax.axis_index("seq")
    tokens_here = owned_rows.shape[1]
    width = owned_rows.shape[2]
    heads = head_weights.shape[1]
    depth = head_weights.shape[2] // 2
    groups = seq_count // heads
    portion = tokens_here // groups
    room = 2 * tokens_here // seq_count - 1
    rows_here = owned_rows[0]
    targets = seq_position[0]
    if groups == 1:
        owned_all = lax.all_gather(rows_here, "seq", axis=0, tiled=True)
        places_all = lax.all_gather(targets, "seq", axis=0, tiled=True)
    holders = targets // tokens_here
    order_ids = jnp.arange(tokens_here)
    earlier = order_ids[None, :] < order_ids[:, None]
    same_holder = holders[:, None] == holders[None, :]
    ranked = jnp.sum((earlier & same_holder).astype(jnp.int32), axis=1)
    slot_ids = holders * room + ranked
    outgoing = jnp.zeros((seq_count * room, width), rows_here.dtype).at[slot_ids].set(rows_here)
    outgoing = outgoing.reshape(seq_count, room, width)
    labels = (
        jnp.full((seq_count * room,), -1, jnp.int32)
        .at[slot_ids]
        .set(targets)
        .reshape(seq_count, room)
    )
    arrived, arrived_pos = (
        lax.all_to_all(outgoing, "seq", split_axis=0, concat_axis=0, tiled=True),
        lax.all_to_all(labels, "seq", split_axis=0, concat_axis=0, tiled=True),
    )
    local_ids = jnp.where(
        arrived_pos >= 0, arrived_pos - my_index * tokens_here, tokens_here
    ).reshape(-1)
    tokens = (
        jnp.zeros((tokens_here, width), rows_here.dtype)
        .at[local_ids]
        .set(arrived.reshape(-1, width), mode="drop")
    )
    proj = jnp.einsum(
        "td,dhc->htc", tokens, head_weights, preferred_element_type=jnp.float32
    ).astype(jnp.bfloat16)
    sending = proj.reshape(seq_count, portion * 2 * depth)
    upstream = out_grad[0].reshape(seq_count, portion * depth)
    got, got_grad = (
        lax.all_to_all(sending, "seq", split_axis=0, concat_axis=0, tiled=True),
        lax.all_to_all(upstream, "seq", split_axis=0, concat_axis=0, tiled=True),
    )
    gathered = got.reshape(seq_count * portion, 2 * depth)
    grad_rows = got_grad.reshape(seq_count * portion, depth)
    group = my_index % groups
    mixed, grad_both = attend_group(gathered, grad_rows, key_blocks[group], key_counts[group])
    back_out, back_grad = (
        lax.all_to_all(
            mixed.reshape(seq_count, portion * depth),
            "seq",
            split_axis=0,
            concat_axis=0,
            tiled=True,
        ),
        lax.all_to_all(
            grad_both.reshape(seq_count, portion * 2 * depth),
            "seq",
            split_axis=0,
            concat_axis=0,
            tiled=True,
        ),
    )
    attention = back_out.reshape(heads, tokens_here, depth)[None]
    grad_proj = back_grad.reshape(heads, tokens_here, 2 * depth)
    seq_grad = jnp.einsum(
        "htc,dhc->td", grad_proj, head_weights, preferred_element_type=jnp.float32
    ).astype(jnp.bfloat16)[None]
    if groups == 1:
        rec_count = lax.axis_size("rec")
        rows_out = width // (rec_count * seq_count)
        head_grad = grad_both[places_all]
        partial = jnp.einsum(
            "od,oc->dc", owned_all, head_grad, preferred_element_type=jnp.float32
        )
        summed = lax.psum_scatter(partial, "rec", scatter_dimension=0, tiled=True)
        spread = lax.all_to_all(
            summed.reshape(seq_count, rows_out, 2 * depth),
            "seq",
            split_axis=0,
            concat_axis=0,
            tiled=True,
        )
        weight_grad = jnp.transpose(spread, (1, 0, 2))
    else:
        weight_grad = lax.psum_scatter(
            jnp.einsum("td,htc->dhc", tokens, grad_proj, preferred_element_type=jnp.float32),
            ("rec", "seq"),
            scatter_dimension=0,
            tiled=True,
        )
    return (attention, seq_grad, weight_grad)


def solution(mesh):
    placed = (P("rec", "seq", None), P("rec", "seq"), P(), P(), P(), P("rec", None, "seq", None))
    return jax.shard_map(
        local,
        mesh=mesh,
        in_specs=placed,
        out_specs=(
            P("rec", None, "seq", None),
            P("rec", "seq", None),
            P(("rec", "seq"), None, None),
        ),
        check_vma=False,
    )
```

```python
import jax
import jax.numpy as jnp
from jax import lax
from jax.sharding import PartitionSpec as P
from jax.experimental import pallas as pl
from jax.experimental.pallas import tpu as pltpu

BLOCK = 128


def attention_kernel(lists_ref, counts_ref, both_ref, grad_ref, out_ref, back_ref, acc_ref):
    nblocks, listed = lists_ref.shape
    depth = grad_ref.shape[1]
    scale = depth ** (-0.5)
    acc_ref[...] = jnp.zeros(acc_ref.shape, jnp.float32)
    col_block = lax.broadcasted_iota(jnp.int32, (BLOCK, listed * BLOCK), 1) // BLOCK
    trans_a = (((0,), (0,)), ((), ()))
    trans_b = (((1,), (1,)), ((), ()))

    def one_block(a, carry):
        start = pl.multiple_of(a * BLOCK, BLOCK)
        own = both_ref[pl.ds(start, BLOCK), :]
        query = own[:, :depth]
        upstream = grad_ref[pl.ds(start, BLOCK), :]
        active = counts_ref[a]
        picks = [jnp.clip(lists_ref[a, j], 0, nblocks - 1) for j in range(listed)]
        tiles = [both_ref[pl.ds(pl.multiple_of(b * BLOCK, BLOCK), BLOCK), :] for b in picks]
        keys = [t[:, :depth] for t in tiles]
        values = [t[:, depth:] for t in tiles]
        scores = jnp.concatenate(
            [lax.dot_general(query, k, trans_b, preferred_element_type=jnp.float32) for k in keys],
            axis=1,
        ) * scale
        usable = col_block < active
        scores = jnp.where(usable, scores, -jnp.inf)
        peak = jnp.max(scores, axis=1, keepdims=True)
        weights = jnp.where(usable, jnp.exp(scores - peak), 0.0)
        probs = weights / jnp.sum(weights, axis=1, keepdims=True)
        probs_low = probs.astype(jnp.bfloat16)
        dprobs = jnp.concatenate(
            [lax.dot_general(upstream, v, trans_b, preferred_element_type=jnp.float32) for v in values],
            axis=1,
        )
        inner = jnp.sum(probs * dprobs, axis=1, keepdims=True)
        dscores = (scale * probs * (dprobs - inner)).astype(jnp.bfloat16)
        mixed = jnp.zeros((BLOCK, depth), jnp.float32)
        dquery = jnp.zeros((BLOCK, depth), jnp.float32)
        for j in range(listed):
            cols = slice(j * BLOCK, (j + 1) * BLOCK)
            mixed = mixed + jnp.dot(probs_low[:, cols], values[j], preferred_element_type=jnp.float32)
            dquery = dquery + jnp.dot(dscores[:, cols], keys[j], preferred_element_type=jnp.float32)
        out_ref[pl.ds(start, BLOCK), :] = mixed.astype(out_ref.dtype)
        for j in range(listed):
            cols = slice(j * BLOCK, (j + 1) * BLOCK)
            dkeys = lax.dot_general(dscores[:, cols], query, trans_a, preferred_element_type=jnp.float32)
            dvalues = lax.dot_general(probs_low[:, cols], upstream, trans_a, preferred_element_type=jnp.float32)
            if j == 0:
                dkeys = dkeys + dquery

            @pl.when(j < active)
            def _():
                rows = pl.ds(pl.multiple_of(picks[j] * BLOCK, BLOCK), BLOCK)
                acc_ref[rows, :] += jnp.concatenate([dkeys, dvalues], axis=1)

        return carry

    lax.fori_loop(0, nblocks, one_block, 0)
    back_ref[...] = acc_ref[...].astype(back_ref.dtype)


def attend_group(both, grad_rows, lists, counts):
    total, width = both.shape
    depth = grad_rows.shape[1]
    smem = pltpu.MemorySpace.SMEM
    vmem = pltpu.MemorySpace.VMEM
    return pl.pallas_call(
        attention_kernel,
        out_shape=(
            jax.ShapeDtypeStruct((total, depth), jnp.bfloat16),
            jax.ShapeDtypeStruct((total, width), jnp.bfloat16),
        ),
        in_specs=[
            pl.BlockSpec(memory_space=smem),
            pl.BlockSpec(memory_space=smem),
            pl.BlockSpec(memory_space=vmem),
            pl.BlockSpec(memory_space=vmem),
        ],
        out_specs=(pl.BlockSpec(memory_space=vmem), pl.BlockSpec(memory_space=vmem)),
        scratch_shapes=[pltpu.VMEM((total, width), jnp.float32)],
    )(lists, counts, both, grad_rows)


def route_tokens(rows_here, targets, seq_count, my_index):
    tokens_here, width = rows_here.shape
    room = 2 * tokens_here // seq_count - 1
    holders = targets // tokens_here
    order_ids = jnp.arange(tokens_here)
    earlier = order_ids[None, :] < order_ids[:, None]
    same_holder = holders[:, None] == holders[None, :]
    ranked = jnp.sum((earlier & same_holder).astype(jnp.int32), axis=1)
    slot_ids = holders * room + ranked
    outgoing = jnp.zeros((seq_count * room, width), rows_here.dtype).at[slot_ids].set(rows_here)
    outgoing = outgoing.reshape(seq_count, room, width)
    labels = (
        jnp.full((seq_count * room,), -1, jnp.int32)
        .at[slot_ids]
        .set(targets)
        .reshape(seq_count, room)
    )
    arrived, arrived_pos = (
        lax.all_to_all(outgoing, "seq", split_axis=0, concat_axis=0, tiled=True),
        lax.all_to_all(labels, "seq", split_axis=0, concat_axis=0, tiled=True),
    )
    local_ids = jnp.where(
        arrived_pos >= 0, arrived_pos - my_index * tokens_here, tokens_here
    ).reshape(-1)
    return (
        jnp.zeros((tokens_here, width), rows_here.dtype)
        .at[local_ids]
        .set(arrived.reshape(-1, width), mode="drop")
    )


def local(owned_rows, seq_position, head_weights, key_blocks, key_counts, out_grad):
    seq_count = lax.axis_size("seq")
    rec_count = lax.axis_size("rec")
    my_index = lax.axis_index("seq")
    tokens_here = owned_rows.shape[1]
    width = owned_rows.shape[2]
    heads = head_weights.shape[1]
    depth = head_weights.shape[2] // 2
    groups = seq_count // heads
    portion = tokens_here // groups
    rows_here = owned_rows[0]
    targets = seq_position[0]
    group = my_index % groups
    upstream = out_grad[0].reshape(seq_count, portion * depth)
    got_grad = lax.all_to_all(upstream, "seq", split_axis=0, concat_axis=0, tiled=True)
    grad_rows = got_grad.reshape(seq_count * portion, depth)
    if groups == 1:
        owned_all = lax.all_gather(rows_here, "seq", axis=0, tiled=True)
        places_all = lax.all_gather(targets, "seq", axis=0, tiled=True)
        head_w = lax.dynamic_index_in_dim(head_weights, my_index // groups, axis=1, keepdims=False)
        proj_owned = jnp.dot(owned_all, head_w, preferred_element_type=jnp.float32).astype(
            jnp.bfloat16
        )
        gathered = (
            jnp.zeros(proj_owned.shape, proj_owned.dtype)
            .at[places_all]
            .set(proj_owned, unique_indices=True)
        )
    else:
        tokens = route_tokens(rows_here, targets, seq_count, my_index)
        proj = jnp.einsum(
            "td,dhc->htc", tokens, head_weights, preferred_element_type=jnp.float32
        ).astype(jnp.bfloat16)
        sending = proj.reshape(seq_count, portion * 2 * depth)
        got = lax.all_to_all(sending, "seq", split_axis=0, concat_axis=0, tiled=True)
        gathered = got.reshape(seq_count * portion, 2 * depth)
    mixed, grad_both = attend_group(gathered, grad_rows, key_blocks[group], key_counts[group])
    back_out, back_grad = (
        lax.all_to_all(
            mixed.reshape(seq_count, portion * depth),
            "seq",
            split_axis=0,
            concat_axis=0,
            tiled=True,
        ),
        lax.all_to_all(
            grad_both.reshape(seq_count, portion * 2 * depth),
            "seq",
            split_axis=0,
            concat_axis=0,
            tiled=True,
        ),
    )
    attention = back_out.reshape(heads, tokens_here, depth)[None]
    grad_proj = back_grad.reshape(heads, tokens_here, 2 * depth)
    seq_grad = jnp.einsum(
        "htc,dhc->td", grad_proj, head_weights, preferred_element_type=jnp.float32
    ).astype(jnp.bfloat16)[None]
    if groups == 1:
        rows_out = width // (rec_count * seq_count)
        head_grad = grad_both[places_all]
        partial = jnp.einsum(
            "od,oc->dc", owned_all, head_grad, preferred_element_type=jnp.float32
        )
        summed = lax.psum_scatter(partial, "rec", scatter_dimension=0, tiled=True)
        spread = lax.all_to_all(
            summed.reshape(seq_count, rows_out, 2 * depth),
            "seq",
            split_axis=0,
            concat_axis=0,
            tiled=True,
        )
        weight_grad = jnp.transpose(spread, (1, 0, 2))
    else:
        weight_grad = lax.psum_scatter(
            jnp.einsum("td,htc->dhc", tokens, grad_proj, preferred_element_type=jnp.float32),
            ("rec", "seq"),
            scatter_dimension=0,
            tiled=True,
        )
    return (attention, seq_grad, weight_grad)


def solution(mesh):
    placed = (P("rec", "seq", None), P("rec", "seq"), P(), P(), P(), P("rec", None, "seq", None))
    return jax.shard_map(
        local,
        mesh=mesh,
        in_specs=placed,
        out_specs=(
            P("rec", None, "seq", None),
            P("rec", "seq", None),
            P(("rec", "seq"), None, None),
        ),
        check_vma=False,
    )
```

```python
import jax
import jax.numpy as jnp
from jax import lax
from jax.sharding import PartitionSpec as P
from jax.experimental import pallas as pl
from jax.experimental.pallas import tpu as pltpu

BLOCK = 128


def attention_kernel(lists_ref, counts_ref, both_ref, grad_ref, out_ref, back_ref, acc_ref):
    nblocks, listed = lists_ref.shape
    depth = grad_ref.shape[1]
    scale = depth ** (-0.5)
    acc_ref[...] = jnp.zeros(acc_ref.shape, jnp.float32)
    col_block = lax.broadcasted_iota(jnp.int32, (BLOCK, listed * BLOCK), 1) // BLOCK
    trans_a = (((0,), (0,)), ((), ()))
    trans_b = (((1,), (1,)), ((), ()))

    def one_block(a, carry):
        start = pl.multiple_of(a * BLOCK, BLOCK)
        own = both_ref[pl.ds(start, BLOCK), :]
        query = own[:, :depth]
        upstream = grad_ref[pl.ds(start, BLOCK), :]
        active = counts_ref[a]
        picks = [jnp.clip(lists_ref[a, j], 0, nblocks - 1) for j in range(listed)]
        tiles = [both_ref[pl.ds(pl.multiple_of(b * BLOCK, BLOCK), BLOCK), :] for b in picks]
        keys = [t[:, :depth] for t in tiles]
        values = [t[:, depth:] for t in tiles]
        scores = jnp.concatenate(
            [lax.dot_general(query, k, trans_b, preferred_element_type=jnp.float32) for k in keys],
            axis=1,
        ) * scale
        usable = col_block < active
        scores = jnp.where(usable, scores, -jnp.inf)
        peak = jnp.max(scores, axis=1, keepdims=True)
        weights = jnp.where(usable, jnp.exp(scores - peak), 0.0)
        probs = weights / jnp.sum(weights, axis=1, keepdims=True)
        probs_low = probs.astype(jnp.bfloat16)
        dprobs = jnp.concatenate(
            [lax.dot_general(upstream, v, trans_b, preferred_element_type=jnp.float32) for v in values],
            axis=1,
        )
        inner = jnp.sum(probs * dprobs, axis=1, keepdims=True)
        dscores = (scale * probs * (dprobs - inner)).astype(jnp.bfloat16)
        mixed = jnp.zeros((BLOCK, depth), jnp.float32)
        dquery = jnp.zeros((BLOCK, depth), jnp.float32)
        for j in range(listed):
            cols = slice(j * BLOCK, (j + 1) * BLOCK)
            mixed = mixed + jnp.dot(probs_low[:, cols], values[j], preferred_element_type=jnp.float32)
            dquery = dquery + jnp.dot(dscores[:, cols], keys[j], preferred_element_type=jnp.float32)
        out_ref[pl.ds(start, BLOCK), :] = mixed.astype(out_ref.dtype)
        for j in range(listed):
            cols = slice(j * BLOCK, (j + 1) * BLOCK)
            dkeys = lax.dot_general(dscores[:, cols], query, trans_a, preferred_element_type=jnp.float32)
            dvalues = lax.dot_general(probs_low[:, cols], upstream, trans_a, preferred_element_type=jnp.float32)
            if j == 0:
                dkeys = dkeys + dquery

            @pl.when(j < active)
            def _():
                rows = pl.ds(pl.multiple_of(picks[j] * BLOCK, BLOCK), BLOCK)
                acc_ref[rows, :] += jnp.concatenate([dkeys, dvalues], axis=1)

        return carry

    lax.fori_loop(0, nblocks, one_block, 0)
    back_ref[...] = acc_ref[...].astype(back_ref.dtype)


def attend_group(both, grad_rows, lists, counts):
    total, width = both.shape
    depth = grad_rows.shape[1]
    smem = pltpu.MemorySpace.SMEM
    vmem = pltpu.MemorySpace.VMEM
    return pl.pallas_call(
        attention_kernel,
        out_shape=(
            jax.ShapeDtypeStruct((total, depth), jnp.bfloat16),
            jax.ShapeDtypeStruct((total, width), jnp.bfloat16),
        ),
        in_specs=[
            pl.BlockSpec(memory_space=smem),
            pl.BlockSpec(memory_space=smem),
            pl.BlockSpec(memory_space=vmem),
            pl.BlockSpec(memory_space=vmem),
        ],
        out_specs=(pl.BlockSpec(memory_space=vmem), pl.BlockSpec(memory_space=vmem)),
        scratch_shapes=[pltpu.VMEM((total, width), jnp.float32)],
    )(lists, counts, both, grad_rows)


def route_tokens(rows_here, targets, seq_count, my_index):
    tokens_here, width = rows_here.shape
    room = 2 * tokens_here // seq_count - 1
    holders = targets // tokens_here
    order_ids = jnp.arange(tokens_here)
    earlier = order_ids[None, :] < order_ids[:, None]
    same_holder = holders[:, None] == holders[None, :]
    ranked = jnp.sum((earlier & same_holder).astype(jnp.int32), axis=1)
    slot_ids = holders * room + ranked
    outgoing = jnp.zeros((seq_count * room, width), rows_here.dtype).at[slot_ids].set(rows_here)
    outgoing = outgoing.reshape(seq_count, room, width)
    labels = (
        jnp.full((seq_count * room,), -1, jnp.int32)
        .at[slot_ids]
        .set(targets)
        .reshape(seq_count, room)
    )
    arrived, arrived_pos = (
        lax.all_to_all(outgoing, "seq", split_axis=0, concat_axis=0, tiled=True),
        lax.all_to_all(labels, "seq", split_axis=0, concat_axis=0, tiled=True),
    )
    local_ids = jnp.where(
        arrived_pos >= 0, arrived_pos - my_index * tokens_here, tokens_here
    ).reshape(-1)
    return (
        jnp.zeros((tokens_here, width), rows_here.dtype)
        .at[local_ids]
        .set(arrived.reshape(-1, width), mode="drop")
    )


def local(owned_rows, seq_position, head_weights, key_blocks, key_counts, out_grad):
    seq_count = lax.axis_size("seq")
    rec_count = lax.axis_size("rec")
    my_index = lax.axis_index("seq")
    tokens_here = owned_rows.shape[1]
    width = owned_rows.shape[2]
    heads = head_weights.shape[1]
    depth = head_weights.shape[2] // 2
    groups = seq_count // heads
    portion = tokens_here // groups
    rows_here = owned_rows[0]
    targets = seq_position[0]
    group = my_index % groups
    upstream = out_grad[0].reshape(seq_count, portion * depth)
    got_grad = lax.all_to_all(upstream, "seq", split_axis=0, concat_axis=0, tiled=True)
    grad_rows = got_grad.reshape(seq_count * portion, depth)
    if groups == 1:
        owned_all = lax.all_gather(rows_here, "seq", axis=0, tiled=True)
        places_all = lax.all_to_all(
            jnp.broadcast_to(targets[None], (seq_count, tokens_here)),
            "seq",
            split_axis=0,
            concat_axis=0,
            tiled=True,
        ).reshape(-1)
        proj_mine = jnp.einsum(
            "td,dhc->htc", rows_here, head_weights, preferred_element_type=jnp.float32
        ).astype(jnp.bfloat16)
        proj_owned = lax.all_to_all(
            proj_mine, "seq", split_axis=0, concat_axis=0, tiled=True
        ).reshape(seq_count * tokens_here, 2 * depth)
        gathered = (
            jnp.zeros(proj_owned.shape, proj_owned.dtype)
            .at[places_all]
            .set(proj_owned, unique_indices=True)
        )
    else:
        tokens = route_tokens(rows_here, targets, seq_count, my_index)
        proj = jnp.einsum(
            "td,dhc->htc", tokens, head_weights, preferred_element_type=jnp.float32
        ).astype(jnp.bfloat16)
        sending = proj.reshape(seq_count, portion * 2 * depth)
        got = lax.all_to_all(sending, "seq", split_axis=0, concat_axis=0, tiled=True)
        gathered = got.reshape(seq_count * portion, 2 * depth)
    mixed, grad_both = attend_group(gathered, grad_rows, key_blocks[group], key_counts[group])
    back_out, back_grad = (
        lax.all_to_all(
            mixed.reshape(seq_count, portion * depth),
            "seq",
            split_axis=0,
            concat_axis=0,
            tiled=True,
        ),
        lax.all_to_all(
            grad_both.reshape(seq_count, portion * 2 * depth),
            "seq",
            split_axis=0,
            concat_axis=0,
            tiled=True,
        ),
    )
    attention = back_out.reshape(heads, tokens_here, depth)[None]
    grad_proj = back_grad.reshape(heads, tokens_here, 2 * depth)
    seq_grad = jnp.einsum(
        "htc,dhc->td", grad_proj, head_weights, preferred_element_type=jnp.float32
    ).astype(jnp.bfloat16)[None]
    if groups == 1:
        rows_out = width // (rec_count * seq_count)
        head_grad = grad_both[places_all]
        partial = jnp.einsum(
            "od,oc->dc", owned_all, head_grad, preferred_element_type=jnp.float32
        )
        summed = lax.psum_scatter(partial, "rec", scatter_dimension=0, tiled=True)
        spread = lax.all_to_all(
            summed.reshape(seq_count, rows_out, 2 * depth),
            "seq",
            split_axis=0,
            concat_axis=0,
            tiled=True,
        )
        weight_grad = jnp.transpose(spread, (1, 0, 2))
    else:
        weight_grad = lax.psum_scatter(
            jnp.einsum("td,htc->dhc", tokens, grad_proj, preferred_element_type=jnp.float32),
            ("rec", "seq"),
            scatter_dimension=0,
            tiled=True,
        )
    return (attention, seq_grad, weight_grad)


def solution(mesh):
    placed = (P("rec", "seq", None), P("rec", "seq"), P(), P(), P(), P("rec", None, "seq", None))
    return jax.shard_map(
        local,
        mesh=mesh,
        in_specs=placed,
        out_specs=(
            P("rec", None, "seq", None),
            P("rec", "seq", None),
            P(("rec", "seq"), None, None),
        ),
        check_vma=False,
    )
```

```python
import jax
import jax.numpy as jnp
from jax import lax
from jax.sharding import PartitionSpec as P
from jax.experimental import pallas as pl
from jax.experimental.pallas import tpu as pltpu

BLOCK = 128


def attention_kernel(lists_ref, counts_ref, both_ref, grad_ref, out_ref, back_ref, acc_ref):
    nblocks, listed = lists_ref.shape
    depth = grad_ref.shape[1]
    scale = depth ** (-0.5)
    acc_ref[...] = jnp.zeros(acc_ref.shape, jnp.float32)
    col_block = lax.broadcasted_iota(jnp.int32, (BLOCK, listed * BLOCK), 1) // BLOCK
    trans_a = (((0,), (0,)), ((), ()))
    trans_b = (((1,), (1,)), ((), ()))

    def one_block(a, carry):
        start = pl.multiple_of(a * BLOCK, BLOCK)
        own = both_ref[pl.ds(start, BLOCK), :]
        query = own[:, :depth]
        upstream = grad_ref[pl.ds(start, BLOCK), :]
        active = counts_ref[a]
        picks = [jnp.clip(lists_ref[a, j], 0, nblocks - 1) for j in range(listed)]
        tiles = [both_ref[pl.ds(pl.multiple_of(b * BLOCK, BLOCK), BLOCK), :] for b in picks]
        keys = [t[:, :depth] for t in tiles]
        values = [t[:, depth:] for t in tiles]
        scores = jnp.concatenate(
            [lax.dot_general(query, k, trans_b, preferred_element_type=jnp.float32) for k in keys],
            axis=1,
        ) * scale
        usable = col_block < active
        scores = jnp.where(usable, scores, -jnp.inf)
        peak = jnp.max(scores, axis=1, keepdims=True)
        weights = jnp.where(usable, jnp.exp(scores - peak), 0.0)
        probs = weights / jnp.sum(weights, axis=1, keepdims=True)
        probs_low = probs.astype(jnp.bfloat16)
        dprobs = jnp.concatenate(
            [lax.dot_general(upstream, v, trans_b, preferred_element_type=jnp.float32) for v in values],
            axis=1,
        )
        inner = jnp.sum(probs * dprobs, axis=1, keepdims=True)
        dscores = (scale * probs * (dprobs - inner)).astype(jnp.bfloat16)
        mixed = jnp.zeros((BLOCK, depth), jnp.float32)
        dquery = jnp.zeros((BLOCK, depth), jnp.float32)
        for j in range(listed):
            cols = slice(j * BLOCK, (j + 1) * BLOCK)
            mixed = mixed + jnp.dot(probs_low[:, cols], values[j], preferred_element_type=jnp.float32)
            dquery = dquery + jnp.dot(dscores[:, cols], keys[j], preferred_element_type=jnp.float32)
        out_ref[pl.ds(start, BLOCK), :] = mixed.astype(out_ref.dtype)
        for j in range(listed):
            cols = slice(j * BLOCK, (j + 1) * BLOCK)
            dkeys = lax.dot_general(dscores[:, cols], query, trans_a, preferred_element_type=jnp.float32)
            dvalues = lax.dot_general(probs_low[:, cols], upstream, trans_a, preferred_element_type=jnp.float32)
            if j == 0:
                dkeys = dkeys + dquery

            @pl.when(j < active)
            def _():
                rows = pl.ds(pl.multiple_of(picks[j] * BLOCK, BLOCK), BLOCK)
                acc_ref[rows, :] += jnp.concatenate([dkeys, dvalues], axis=1)

        return carry

    lax.fori_loop(0, nblocks, one_block, 0)
    back_ref[...] = acc_ref[...].astype(back_ref.dtype)


def attend_group(both, grad_rows, lists, counts):
    total, width = both.shape
    depth = grad_rows.shape[1]
    smem = pltpu.MemorySpace.SMEM
    vmem = pltpu.MemorySpace.VMEM
    return pl.pallas_call(
        attention_kernel,
        out_shape=(
            jax.ShapeDtypeStruct((total, depth), jnp.bfloat16),
            jax.ShapeDtypeStruct((total, width), jnp.bfloat16),
        ),
        in_specs=[
            pl.BlockSpec(memory_space=smem),
            pl.BlockSpec(memory_space=smem),
            pl.BlockSpec(memory_space=vmem),
            pl.BlockSpec(memory_space=vmem),
        ],
        out_specs=(pl.BlockSpec(memory_space=vmem), pl.BlockSpec(memory_space=vmem)),
        scratch_shapes=[pltpu.VMEM((total, width), jnp.float32)],
    )(lists, counts, both, grad_rows)


def route_tokens(rows_here, targets, seq_count, my_index):
    tokens_here, width = rows_here.shape
    room = 2 * tokens_here // seq_count - 1
    holders = targets // tokens_here
    order_ids = jnp.arange(tokens_here)
    earlier = order_ids[None, :] < order_ids[:, None]
    same_holder = holders[:, None] == holders[None, :]
    ranked = jnp.sum((earlier & same_holder).astype(jnp.int32), axis=1)
    slot_ids = holders * room + ranked
    outgoing = jnp.zeros((seq_count * room, width), rows_here.dtype).at[slot_ids].set(rows_here)
    outgoing = outgoing.reshape(seq_count, room, width)
    labels = (
        jnp.full((seq_count * room,), -1, jnp.int32)
        .at[slot_ids]
        .set(targets)
        .reshape(seq_count, room)
    )
    arrived, arrived_pos = (
        lax.all_to_all(outgoing, "seq", split_axis=0, concat_axis=0, tiled=True),
        lax.all_to_all(labels, "seq", split_axis=0, concat_axis=0, tiled=True),
    )
    local_ids = jnp.where(
        arrived_pos >= 0, arrived_pos - my_index * tokens_here, tokens_here
    ).reshape(-1)
    return (
        jnp.zeros((tokens_here, width), rows_here.dtype)
        .at[local_ids]
        .set(arrived.reshape(-1, width), mode="drop")
    )


def local(owned_rows, seq_position, head_weights, key_blocks, key_counts, out_grad):
    seq_count = lax.axis_size("seq")
    rec_count = lax.axis_size("rec")
    my_index = lax.axis_index("seq")
    tokens_here = owned_rows.shape[1]
    width = owned_rows.shape[2]
    heads = head_weights.shape[1]
    depth = head_weights.shape[2] // 2
    groups = seq_count // heads
    portion = tokens_here // groups
    rows_here = owned_rows[0]
    targets = seq_position[0]
    group = my_index % groups
    upstream = out_grad[0].reshape(seq_count, portion * depth)
    got_grad = lax.all_to_all(upstream, "seq", split_axis=0, concat_axis=0, tiled=True)
    grad_rows = got_grad.reshape(seq_count * portion, depth)
    if groups == 1:
        places_all = lax.all_to_all(
            jnp.broadcast_to(targets[None], (seq_count, tokens_here)),
            "seq",
            split_axis=0,
            concat_axis=0,
            tiled=True,
        ).reshape(-1)
        proj_mine = jnp.einsum(
            "td,dhc->htc", rows_here, head_weights, preferred_element_type=jnp.float32
        ).astype(jnp.bfloat16)
        proj_owned = lax.all_to_all(
            proj_mine, "seq", split_axis=0, concat_axis=0, tiled=True
        ).reshape(seq_count * tokens_here, 2 * depth)
        later_rows, proj_owned, grad_rows, places_all = lax.optimization_barrier(
            (rows_here, proj_owned, grad_rows, places_all)
        )
        owned_all = lax.all_gather(later_rows, "seq", axis=0, tiled=True)
        gathered = (
            jnp.zeros(proj_owned.shape, proj_owned.dtype)
            .at[places_all]
            .set(proj_owned, unique_indices=True)
        )
    else:
        tokens = route_tokens(rows_here, targets, seq_count, my_index)
        proj = jnp.einsum(
            "td,dhc->htc", tokens, head_weights, preferred_element_type=jnp.float32
        ).astype(jnp.bfloat16)
        sending = proj.reshape(seq_count, portion * 2 * depth)
        got = lax.all_to_all(sending, "seq", split_axis=0, concat_axis=0, tiled=True)
        gathered = got.reshape(seq_count * portion, 2 * depth)
    mixed, grad_both = attend_group(gathered, grad_rows, key_blocks[group], key_counts[group])
    back_out, back_grad = (
        lax.all_to_all(
            mixed.reshape(seq_count, portion * depth),
            "seq",
            split_axis=0,
            concat_axis=0,
            tiled=True,
        ),
        lax.all_to_all(
            grad_both.reshape(seq_count, portion * 2 * depth),
            "seq",
            split_axis=0,
            concat_axis=0,
            tiled=True,
        ),
    )
    attention = back_out.reshape(heads, tokens_here, depth)[None]
    grad_proj = back_grad.reshape(heads, tokens_here, 2 * depth)
    seq_grad = jnp.einsum(
        "htc,dhc->td", grad_proj, head_weights, preferred_element_type=jnp.float32
    ).astype(jnp.bfloat16)[None]
    if groups == 1:
        rows_out = width // (rec_count * seq_count)
        head_grad = grad_both[places_all]
        partial = jnp.einsum(
            "od,oc->dc", owned_all, head_grad, preferred_element_type=jnp.float32
        )
        summed = lax.psum_scatter(partial, "rec", scatter_dimension=0, tiled=True)
        spread = lax.all_to_all(
            summed.reshape(seq_count, rows_out, 2 * depth),
            "seq",
            split_axis=0,
            concat_axis=0,
            tiled=True,
        )
        weight_grad = jnp.transpose(spread, (1, 0, 2))
    else:
        weight_grad = lax.psum_scatter(
            jnp.einsum("td,htc->dhc", tokens, grad_proj, preferred_element_type=jnp.float32),
            ("rec", "seq"),
            scatter_dimension=0,
            tiled=True,
        )
    return (attention, seq_grad, weight_grad)


def solution(mesh):
    placed = (P("rec", "seq", None), P("rec", "seq"), P(), P(), P(), P("rec", None, "seq", None))
    return jax.shard_map(
        local,
        mesh=mesh,
        in_specs=placed,
        out_specs=(
            P("rec", None, "seq", None),
            P("rec", "seq", None),
            P(("rec", "seq"), None, None),
        ),
        check_vma=False,
    )
```

```python
import jax
import jax.numpy as jnp
from jax import lax
from jax.sharding import PartitionSpec as P
from jax.experimental import pallas as pl
from jax.experimental.pallas import tpu as pltpu

BLOCK = 128


def attention_kernel(lists_ref, counts_ref, both_ref, grad_ref, out_ref, back_ref, acc_ref):
    nblocks, listed = lists_ref.shape
    depth = grad_ref.shape[1]
    scale = depth ** (-0.5)
    acc_ref[...] = jnp.zeros(acc_ref.shape, jnp.float32)
    col_block = lax.broadcasted_iota(jnp.int32, (BLOCK, listed * BLOCK), 1) // BLOCK
    trans_a = (((0,), (0,)), ((), ()))
    trans_b = (((1,), (1,)), ((), ()))

    def one_block(a, carry):
        start = pl.multiple_of(a * BLOCK, BLOCK)
        own = both_ref[pl.ds(start, BLOCK), :]
        query = own[:, :depth]
        upstream = grad_ref[pl.ds(start, BLOCK), :]
        active = counts_ref[a]
        picks = [jnp.clip(lists_ref[a, j], 0, nblocks - 1) for j in range(listed)]
        tiles = [both_ref[pl.ds(pl.multiple_of(b * BLOCK, BLOCK), BLOCK), :] for b in picks]
        keys = [t[:, :depth] for t in tiles]
        values = [t[:, depth:] for t in tiles]
        scores = jnp.concatenate(
            [lax.dot_general(query, k, trans_b, preferred_element_type=jnp.float32) for k in keys],
            axis=1,
        ) * scale
        usable = col_block < active
        scores = jnp.where(usable, scores, -jnp.inf)
        peak = jnp.max(scores, axis=1, keepdims=True)
        weights = jnp.where(usable, jnp.exp(scores - peak), 0.0)
        probs = weights / jnp.sum(weights, axis=1, keepdims=True)
        probs_low = probs.astype(jnp.bfloat16)
        dprobs = jnp.concatenate(
            [lax.dot_general(upstream, v, trans_b, preferred_element_type=jnp.float32) for v in values],
            axis=1,
        )
        inner = jnp.sum(probs * dprobs, axis=1, keepdims=True)
        dscores = (scale * probs * (dprobs - inner)).astype(jnp.bfloat16)
        mixed = jnp.zeros((BLOCK, depth), jnp.float32)
        dquery = jnp.zeros((BLOCK, depth), jnp.float32)
        for j in range(listed):
            cols = slice(j * BLOCK, (j + 1) * BLOCK)
            mixed = mixed + jnp.dot(probs_low[:, cols], values[j], preferred_element_type=jnp.float32)
            dquery = dquery + jnp.dot(dscores[:, cols], keys[j], preferred_element_type=jnp.float32)
        out_ref[pl.ds(start, BLOCK), :] = mixed.astype(out_ref.dtype)
        for j in range(listed):
            cols = slice(j * BLOCK, (j + 1) * BLOCK)
            dkeys = lax.dot_general(dscores[:, cols], query, trans_a, preferred_element_type=jnp.float32)
            dvalues = lax.dot_general(probs_low[:, cols], upstream, trans_a, preferred_element_type=jnp.float32)
            if j == 0:
                dkeys = dkeys + dquery

            @pl.when(j < active)
            def _():
                rows = pl.ds(pl.multiple_of(picks[j] * BLOCK, BLOCK), BLOCK)
                acc_ref[rows, :] += jnp.concatenate([dkeys, dvalues], axis=1)

        return carry

    lax.fori_loop(0, nblocks, one_block, 0)
    back_ref[...] = acc_ref[...].astype(back_ref.dtype)


def attend_group(both, grad_rows, lists, counts):
    total, width = both.shape
    depth = grad_rows.shape[1]
    smem = pltpu.MemorySpace.SMEM
    vmem = pltpu.MemorySpace.VMEM
    return pl.pallas_call(
        attention_kernel,
        out_shape=(
            jax.ShapeDtypeStruct((total, depth), jnp.bfloat16),
            jax.ShapeDtypeStruct((total, width), jnp.bfloat16),
        ),
        in_specs=[
            pl.BlockSpec(memory_space=smem),
            pl.BlockSpec(memory_space=smem),
            pl.BlockSpec(memory_space=vmem),
            pl.BlockSpec(memory_space=vmem),
        ],
        out_specs=(pl.BlockSpec(memory_space=vmem), pl.BlockSpec(memory_space=vmem)),
        scratch_shapes=[pltpu.VMEM((total, width), jnp.float32)],
    )(lists, counts, both, grad_rows)


def route_tokens(rows_here, targets, seq_count, my_index):
    tokens_here, width = rows_here.shape
    room = 2 * tokens_here // seq_count - 1
    holders = targets // tokens_here
    order_ids = jnp.arange(tokens_here)
    earlier = order_ids[None, :] < order_ids[:, None]
    same_holder = holders[:, None] == holders[None, :]
    ranked = jnp.sum((earlier & same_holder).astype(jnp.int32), axis=1)
    slot_ids = holders * room + ranked
    outgoing = jnp.zeros((seq_count * room, width), rows_here.dtype).at[slot_ids].set(rows_here)
    outgoing = outgoing.reshape(seq_count, room, width)
    labels = (
        jnp.full((seq_count * room,), -1, jnp.int32)
        .at[slot_ids]
        .set(targets)
        .reshape(seq_count, room)
    )
    arrived, arrived_pos = (
        lax.all_to_all(outgoing, "seq", split_axis=0, concat_axis=0, tiled=True),
        lax.all_to_all(labels, "seq", split_axis=0, concat_axis=0, tiled=True),
    )
    local_ids = jnp.where(
        arrived_pos >= 0, arrived_pos - my_index * tokens_here, tokens_here
    ).reshape(-1)
    return (
        jnp.zeros((tokens_here, width), rows_here.dtype)
        .at[local_ids]
        .set(arrived.reshape(-1, width), mode="drop")
    )


def local(owned_rows, seq_position, head_weights, key_blocks, key_counts, out_grad):
    seq_count = lax.axis_size("seq")
    rec_count = lax.axis_size("rec")
    my_index = lax.axis_index("seq")
    tokens_here = owned_rows.shape[1]
    width = owned_rows.shape[2]
    heads = head_weights.shape[1]
    depth = head_weights.shape[2] // 2
    groups = seq_count // heads
    portion = tokens_here // groups
    rows_here = owned_rows[0]
    targets = seq_position[0]
    group = my_index % groups
    upstream = out_grad[0].reshape(seq_count, portion, depth)
    got_grad = lax.all_to_all(upstream, "seq", split_axis=0, concat_axis=0, tiled=True)
    grad_rows = got_grad.reshape(seq_count * portion, depth)
    if groups == 1:
        places_all = lax.all_to_all(
            jnp.broadcast_to(targets[None], (seq_count, tokens_here)),
            "seq",
            split_axis=0,
            concat_axis=0,
            tiled=True,
        ).reshape(-1)
        proj_mine = jnp.einsum(
            "td,dhc->htc", rows_here, head_weights, preferred_element_type=jnp.float32
        ).astype(jnp.bfloat16)
        proj_owned = lax.all_to_all(
            proj_mine, "seq", split_axis=0, concat_axis=0, tiled=True
        ).reshape(seq_count * tokens_here, 2 * depth)
        later_rows, proj_owned, grad_rows, places_all = lax.optimization_barrier(
            (rows_here, proj_owned, grad_rows, places_all)
        )
        owned_all = lax.all_gather(later_rows, "seq", axis=0, tiled=True)
        gathered = (
            jnp.zeros(proj_owned.shape, proj_owned.dtype)
            .at[places_all]
            .set(proj_owned, unique_indices=True)
        )
    else:
        tokens = route_tokens(rows_here, targets, seq_count, my_index)
        proj = jnp.einsum(
            "td,dhc->htc", tokens, head_weights, preferred_element_type=jnp.float32
        ).astype(jnp.bfloat16)
        sending = proj.reshape(seq_count, portion * 2 * depth)
        got = lax.all_to_all(sending, "seq", split_axis=0, concat_axis=0, tiled=True)
        gathered = got.reshape(seq_count * portion, 2 * depth)
    mixed, grad_both = attend_group(gathered, grad_rows, key_blocks[group], key_counts[group])
    back_out, back_grad = (
        lax.all_to_all(
            mixed.reshape(seq_count, portion, depth),
            "seq",
            split_axis=0,
            concat_axis=0,
            tiled=True,
        ),
        lax.all_to_all(
            grad_both.reshape(seq_count, portion, 2 * depth),
            "seq",
            split_axis=0,
            concat_axis=0,
            tiled=True,
        ),
    )
    attention = back_out.reshape(heads, tokens_here, depth)[None]
    grad_proj = back_grad.reshape(heads, tokens_here, 2 * depth)
    seq_grad = jnp.einsum(
        "htc,dhc->td", grad_proj, head_weights, preferred_element_type=jnp.float32
    ).astype(jnp.bfloat16)[None]
    if groups == 1:
        rows_out = width // (rec_count * seq_count)
        head_grad = grad_both[places_all]
        partial = jnp.einsum(
            "od,oc->dc", owned_all, head_grad, preferred_element_type=jnp.float32
        )
        summed = lax.psum_scatter(partial, "rec", scatter_dimension=0, tiled=True)
        spread = lax.all_to_all(
            summed.reshape(seq_count, rows_out, 2 * depth),
            "seq",
            split_axis=0,
            concat_axis=0,
            tiled=True,
        )
        weight_grad = jnp.transpose(spread, (1, 0, 2))
    else:
        weight_grad = lax.psum_scatter(
            jnp.einsum("td,htc->dhc", tokens, grad_proj, preferred_element_type=jnp.float32),
            ("rec", "seq"),
            scatter_dimension=0,
            tiled=True,
        )
    return (attention, seq_grad, weight_grad)


def solution(mesh):
    placed = (P("rec", "seq", None), P("rec", "seq"), P(), P(), P(), P("rec", None, "seq", None))
    return jax.shard_map(
        local,
        mesh=mesh,
        in_specs=placed,
        out_specs=(
            P("rec", None, "seq", None),
            P("rec", "seq", None),
            P(("rec", "seq"), None, None),
        ),
        check_vma=False,
    )
```

```python
import jax
import jax.numpy as jnp
from jax import lax
from jax.sharding import PartitionSpec as P
from jax.experimental import pallas as pl
from jax.experimental.pallas import tpu as pltpu

BLOCK = 128


def attention_kernel(lists_ref, counts_ref, both_ref, grad_ref, out_ref, back_ref, acc_ref, prob_ref, dprob_ref):
    nblocks, listed = lists_ref.shape
    depth = grad_ref.shape[1]
    scale = depth ** (-0.5)
    acc_ref[...] = jnp.zeros(acc_ref.shape, jnp.float32)
    trans_a = (((0,), (0,)), ((), ()))
    trans_b = (((1,), (1,)), ((), ()))

    def one_block(a, carry):
        start = pl.multiple_of(a * BLOCK, BLOCK)
        query = both_ref[pl.ds(start, BLOCK), :][:, :depth]
        upstream = grad_ref[pl.ds(start, BLOCK), :]
        active = jnp.clip(counts_ref[a], 1, listed)

        def tile(j):
            b = jnp.clip(lists_ref[a, j], 0, nblocks - 1)
            return b, both_ref[pl.ds(pl.multiple_of(b * BLOCK, BLOCK), BLOCK), :]

        def score_pass(j, peak):
            _, both = tile(j)
            scores = lax.dot_general(
                query, both[:, :depth], trans_b, preferred_element_type=jnp.float32
            ) * scale
            prob_ref[j] = scores
            return jnp.maximum(peak, jnp.max(scores, axis=1, keepdims=True))

        peak = lax.fori_loop(
            0, active, score_pass, jnp.full((BLOCK, 1), -jnp.inf, jnp.float32)
        )

        def exp_pass(j, total):
            weights = jnp.exp(prob_ref[j] - peak)
            prob_ref[j] = weights
            return total + jnp.sum(weights, axis=1, keepdims=True)

        total = lax.fori_loop(0, active, exp_pass, jnp.zeros((BLOCK, 1), jnp.float32))

        def value_pass(j, carry):
            mixed, inner = carry
            _, both = tile(j)
            values = both[:, depth:]
            probs = prob_ref[j] / total
            prob_ref[j] = probs
            mixed = mixed + jnp.dot(
                probs.astype(jnp.bfloat16), values, preferred_element_type=jnp.float32
            )
            dprobs = lax.dot_general(upstream, values, trans_b, preferred_element_type=jnp.float32)
            dprob_ref[j] = dprobs
            return mixed, inner + jnp.sum(probs * dprobs, axis=1, keepdims=True)

        mixed, inner = lax.fori_loop(
            0,
            active,
            value_pass,
            (jnp.zeros((BLOCK, depth), jnp.float32), jnp.zeros((BLOCK, 1), jnp.float32)),
        )
        out_ref[pl.ds(start, BLOCK), :] = mixed.astype(out_ref.dtype)

        def grad_pass(j, dquery):
            b, both = tile(j)
            probs = prob_ref[j]
            dscores = (scale * probs * (dprob_ref[j] - inner)).astype(jnp.bfloat16)
            dquery = dquery + jnp.dot(dscores, both[:, :depth], preferred_element_type=jnp.float32)
            dkeys = lax.dot_general(dscores, query, trans_a, preferred_element_type=jnp.float32)
            dvalues = lax.dot_general(
                probs.astype(jnp.bfloat16), upstream, trans_a, preferred_element_type=jnp.float32
            )
            rows = pl.ds(pl.multiple_of(b * BLOCK, BLOCK), BLOCK)
            acc_ref[rows, :] += jnp.concatenate([dkeys, dvalues], axis=1)
            return dquery

        dquery = lax.fori_loop(0, active, grad_pass, jnp.zeros((BLOCK, depth), jnp.float32))
        own = pl.ds(start, BLOCK)
        acc_ref[own, :] += jnp.concatenate([dquery, jnp.zeros_like(dquery)], axis=1)
        return carry

    lax.fori_loop(0, nblocks, one_block, 0)
    back_ref[...] = acc_ref[...].astype(back_ref.dtype)


def attend_group(both, grad_rows, lists, counts):
    total, width = both.shape
    depth = grad_rows.shape[1]
    listed = lists.shape[1]
    smem = pltpu.MemorySpace.SMEM
    vmem = pltpu.MemorySpace.VMEM
    return pl.pallas_call(
        attention_kernel,
        out_shape=(
            jax.ShapeDtypeStruct((total, depth), jnp.bfloat16),
            jax.ShapeDtypeStruct((total, width), jnp.bfloat16),
        ),
        in_specs=[
            pl.BlockSpec(memory_space=smem),
            pl.BlockSpec(memory_space=smem),
            pl.BlockSpec(memory_space=vmem),
            pl.BlockSpec(memory_space=vmem),
        ],
        out_specs=(pl.BlockSpec(memory_space=vmem), pl.BlockSpec(memory_space=vmem)),
        scratch_shapes=[
            pltpu.VMEM((total, width), jnp.float32),
            pltpu.VMEM((listed, BLOCK, BLOCK), jnp.float32),
            pltpu.VMEM((listed, BLOCK, BLOCK), jnp.float32),
        ],
    )(lists, counts, both, grad_rows)


def route_tokens(rows_here, targets, seq_count, my_index):
    tokens_here, width = rows_here.shape
    room = 2 * tokens_here // seq_count - 1
    holders = targets // tokens_here
    order_ids = jnp.arange(tokens_here)
    earlier = order_ids[None, :] < order_ids[:, None]
    same_holder = holders[:, None] == holders[None, :]
    ranked = jnp.sum((earlier & same_holder).astype(jnp.int32), axis=1)
    slot_ids = holders * room + ranked
    outgoing = jnp.zeros((seq_count * room, width), rows_here.dtype).at[slot_ids].set(rows_here)
    outgoing = outgoing.reshape(seq_count, room, width)
    labels = (
        jnp.full((seq_count * room,), -1, jnp.int32)
        .at[slot_ids]
        .set(targets)
        .reshape(seq_count, room)
    )
    arrived, arrived_pos = (
        lax.all_to_all(outgoing, "seq", split_axis=0, concat_axis=0, tiled=True),
        lax.all_to_all(labels, "seq", split_axis=0, concat_axis=0, tiled=True),
    )
    local_ids = jnp.where(
        arrived_pos >= 0, arrived_pos - my_index * tokens_here, tokens_here
    ).reshape(-1)
    return (
        jnp.zeros((tokens_here, width), rows_here.dtype)
        .at[local_ids]
        .set(arrived.reshape(-1, width), mode="drop")
    )


def local(owned_rows, seq_position, head_weights, key_blocks, key_counts, out_grad):
    seq_count = lax.axis_size("seq")
    rec_count = lax.axis_size("rec")
    my_index = lax.axis_index("seq")
    tokens_here = owned_rows.shape[1]
    width = owned_rows.shape[2]
    heads = head_weights.shape[1]
    depth = head_weights.shape[2] // 2
    groups = seq_count // heads
    portion = tokens_here // groups
    rows_here = owned_rows[0]
    targets = seq_position[0]
    group = my_index % groups
    upstream = out_grad[0].reshape(seq_count, portion, depth)
    got_grad = lax.all_to_all(upstream, "seq", split_axis=0, concat_axis=0, tiled=True)
    grad_rows = got_grad.reshape(seq_count * portion, depth)
    if groups == 1:
        places_all = lax.all_to_all(
            jnp.broadcast_to(targets[None], (seq_count, tokens_here)),
            "seq",
            split_axis=0,
            concat_axis=0,
            tiled=True,
        ).reshape(-1)
        proj_mine = jnp.einsum(
            "td,dhc->htc", rows_here, head_weights, preferred_element_type=jnp.float32
        ).astype(jnp.bfloat16)
        proj_owned = lax.all_to_all(
            proj_mine, "seq", split_axis=0, concat_axis=0, tiled=True
        ).reshape(seq_count * tokens_here, 2 * depth)
        later_rows, proj_owned, grad_rows, places_all = lax.optimization_barrier(
            (rows_here, proj_owned, grad_rows, places_all)
        )
        owned_all = lax.all_gather(later_rows, "seq", axis=0, tiled=True)
        gathered = (
            jnp.zeros(proj_owned.shape, proj_owned.dtype)
            .at[places_all]
            .set(proj_owned, unique_indices=True)
        )
    else:
        tokens = route_tokens(rows_here, targets, seq_count, my_index)
        proj = jnp.einsum(
            "td,dhc->htc", tokens, head_weights, preferred_element_type=jnp.float32
        ).astype(jnp.bfloat16)
        sending = proj.reshape(seq_count, portion * 2 * depth)
        got = lax.all_to_all(sending, "seq", split_axis=0, concat_axis=0, tiled=True)
        gathered = got.reshape(seq_count * portion, 2 * depth)
    mixed, grad_both = attend_group(gathered, grad_rows, key_blocks[group], key_counts[group])
    back_out, back_grad = (
        lax.all_to_all(
            mixed.reshape(seq_count, portion, depth),
            "seq",
            split_axis=0,
            concat_axis=0,
            tiled=True,
        ),
        lax.all_to_all(
            grad_both.reshape(seq_count, portion, 2 * depth),
            "seq",
            split_axis=0,
            concat_axis=0,
            tiled=True,
        ),
    )
    attention = back_out.reshape(heads, tokens_here, depth)[None]
    grad_proj = back_grad.reshape(heads, tokens_here, 2 * depth)
    seq_grad = jnp.einsum(
        "htc,dhc->td", grad_proj, head_weights, preferred_element_type=jnp.float32
    ).astype(jnp.bfloat16)[None]
    if groups == 1:
        rows_out = width // (rec_count * seq_count)
        head_grad = grad_both[places_all]
        partial = jnp.einsum(
            "od,oc->dc", owned_all, head_grad, preferred_element_type=jnp.float32
        )
        summed = lax.psum_scatter(partial, "rec", scatter_dimension=0, tiled=True)
        spread = lax.all_to_all(
            summed.reshape(seq_count, rows_out, 2 * depth),
            "seq",
            split_axis=0,
            concat_axis=0,
            tiled=True,
        )
        weight_grad = jnp.transpose(spread, (1, 0, 2))
    else:
        weight_grad = lax.psum_scatter(
            jnp.einsum("td,htc->dhc", tokens, grad_proj, preferred_element_type=jnp.float32),
            ("rec", "seq"),
            scatter_dimension=0,
            tiled=True,
        )
    return (attention, seq_grad, weight_grad)


def solution(mesh):
    placed = (P("rec", "seq", None), P("rec", "seq"), P(), P(), P(), P("rec", None, "seq", None))
    return jax.shard_map(
        local,
        mesh=mesh,
        in_specs=placed,
        out_specs=(
            P("rec", None, "seq", None),
            P("rec", "seq", None),
            P(("rec", "seq"), None, None),
        ),
        check_vma=False,
    )
```

```python
import jax
import jax.numpy as jnp
from jax import lax
from jax.sharding import PartitionSpec as P
from jax.experimental import pallas as pl
from jax.experimental.pallas import tpu as pltpu

BLOCK = 128


def attention_kernel(lists_ref, counts_ref, both_ref, grad_ref, out_ref, back_ref, acc_ref):
    nblocks, listed = lists_ref.shape
    depth = grad_ref.shape[1]
    scale = depth ** (-0.5)
    acc_ref[...] = jnp.zeros(acc_ref.shape, jnp.float32)
    col_block = lax.broadcasted_iota(jnp.int32, (BLOCK, listed * BLOCK), 1) // BLOCK
    trans_a = (((0,), (0,)), ((), ()))
    trans_b = (((1,), (1,)), ((), ()))

    def one_block(a, carry):
        start = pl.multiple_of(a * BLOCK, BLOCK)
        query = both_ref[pl.ds(start, BLOCK), :][:, :depth]
        upstream = grad_ref[pl.ds(start, BLOCK), :]
        active = counts_ref[a]
        picks = [jnp.clip(lists_ref[a, j], 0, nblocks - 1) for j in range(listed)]
        near = jnp.concatenate(
            [both_ref[pl.ds(pl.multiple_of(b * BLOCK, BLOCK), BLOCK), :] for b in picks], axis=0
        )
        keys = near[:, :depth]
        values = near[:, depth:]
        scores = lax.dot_general(query, keys, trans_b, preferred_element_type=jnp.float32) * scale
        usable = col_block < active
        scores = jnp.where(usable, scores, -jnp.inf)
        peak = jnp.max(scores, axis=1, keepdims=True)
        weights = jnp.where(usable, jnp.exp(scores - peak), 0.0)
        probs = weights / jnp.sum(weights, axis=1, keepdims=True)
        probs_low = probs.astype(jnp.bfloat16)
        mixed = jnp.dot(probs_low, values, preferred_element_type=jnp.float32)
        out_ref[pl.ds(start, BLOCK), :] = mixed.astype(out_ref.dtype)
        dprobs = lax.dot_general(upstream, values, trans_b, preferred_element_type=jnp.float32)
        inner = jnp.sum(probs * dprobs, axis=1, keepdims=True)
        dscores = (scale * probs * (dprobs - inner)).astype(jnp.bfloat16)
        dquery = jnp.dot(dscores, keys, preferred_element_type=jnp.float32)
        dkeys = lax.dot_general(dscores, query, trans_a, preferred_element_type=jnp.float32)
        dvalues = lax.dot_general(probs_low, upstream, trans_a, preferred_element_type=jnp.float32)
        both_grads = jnp.concatenate([dkeys, dvalues], axis=1)
        for j in range(listed):
            part = both_grads[j * BLOCK:(j + 1) * BLOCK]
            if j == 0:
                part = part + jnp.concatenate([dquery, jnp.zeros_like(dquery)], axis=1)

            @pl.when(j < active)
            def _():
                rows = pl.ds(pl.multiple_of(picks[j] * BLOCK, BLOCK), BLOCK)
                acc_ref[rows, :] += part

        return carry

    lax.fori_loop(0, nblocks, one_block, 0)
    back_ref[...] = acc_ref[...].astype(back_ref.dtype)


def attend_group(both, grad_rows, lists, counts):
    total, width = both.shape
    depth = grad_rows.shape[1]
    smem = pltpu.MemorySpace.SMEM
    vmem = pltpu.MemorySpace.VMEM
    return pl.pallas_call(
        attention_kernel,
        out_shape=(
            jax.ShapeDtypeStruct((total, depth), jnp.bfloat16),
            jax.ShapeDtypeStruct((total, width), jnp.bfloat16),
        ),
        in_specs=[
            pl.BlockSpec(memory_space=smem),
            pl.BlockSpec(memory_space=smem),
            pl.BlockSpec(memory_space=vmem),
            pl.BlockSpec(memory_space=vmem),
        ],
        out_specs=(pl.BlockSpec(memory_space=vmem), pl.BlockSpec(memory_space=vmem)),
        scratch_shapes=[pltpu.VMEM((total, width), jnp.float32)],
    )(lists, counts, both, grad_rows)


def route_tokens(rows_here, targets, seq_count, my_index):
    tokens_here, width = rows_here.shape
    room = 2 * tokens_here // seq_count - 1
    holders = targets // tokens_here
    order_ids = jnp.arange(tokens_here)
    earlier = order_ids[None, :] < order_ids[:, None]
    same_holder = holders[:, None] == holders[None, :]
    ranked = jnp.sum((earlier & same_holder).astype(jnp.int32), axis=1)
    slot_ids = holders * room + ranked
    outgoing = jnp.zeros((seq_count * room, width), rows_here.dtype).at[slot_ids].set(rows_here)
    outgoing = outgoing.reshape(seq_count, room, width)
    labels = (
        jnp.full((seq_count * room,), -1, jnp.int32)
        .at[slot_ids]
        .set(targets)
        .reshape(seq_count, room)
    )
    arrived, arrived_pos = (
        lax.all_to_all(outgoing, "seq", split_axis=0, concat_axis=0, tiled=True),
        lax.all_to_all(labels, "seq", split_axis=0, concat_axis=0, tiled=True),
    )
    local_ids = jnp.where(
        arrived_pos >= 0, arrived_pos - my_index * tokens_here, tokens_here
    ).reshape(-1)
    return (
        jnp.zeros((tokens_here, width), rows_here.dtype)
        .at[local_ids]
        .set(arrived.reshape(-1, width), mode="drop")
    )


def local(owned_rows, seq_position, head_weights, key_blocks, key_counts, out_grad):
    seq_count = lax.axis_size("seq")
    rec_count = lax.axis_size("rec")
    my_index = lax.axis_index("seq")
    tokens_here = owned_rows.shape[1]
    width = owned_rows.shape[2]
    heads = head_weights.shape[1]
    depth = head_weights.shape[2] // 2
    groups = seq_count // heads
    portion = tokens_here // groups
    rows_here = owned_rows[0]
    targets = seq_position[0]
    group = my_index % groups
    upstream = out_grad[0].reshape(seq_count, portion, depth)
    got_grad = lax.all_to_all(upstream, "seq", split_axis=0, concat_axis=0, tiled=True)
    grad_rows = got_grad.reshape(seq_count * portion, depth)
    if groups == 1:
        places_all = lax.all_to_all(
            jnp.broadcast_to(targets[None], (seq_count, tokens_here)),
            "seq",
            split_axis=0,
            concat_axis=0,
            tiled=True,
        ).reshape(-1)
        proj_mine = jnp.einsum(
            "td,dhc->htc", rows_here, head_weights, preferred_element_type=jnp.float32
        ).astype(jnp.bfloat16)
        proj_owned = lax.all_to_all(
            proj_mine, "seq", split_axis=0, concat_axis=0, tiled=True
        ).reshape(seq_count * tokens_here, 2 * depth)
        later_rows, proj_owned, grad_rows, places_all = lax.optimization_barrier(
            (rows_here, proj_owned, grad_rows, places_all)
        )
        owned_all = lax.all_gather(later_rows, "seq", axis=0, tiled=True)
        gathered = (
            jnp.zeros(proj_owned.shape, proj_owned.dtype)
            .at[places_all]
            .set(proj_owned, unique_indices=True)
        )
    else:
        tokens = route_tokens(rows_here, targets, seq_count, my_index)
        proj = jnp.einsum(
            "td,dhc->htc", tokens, head_weights, preferred_element_type=jnp.float32
        ).astype(jnp.bfloat16)
        sending = proj.reshape(seq_count, portion * 2 * depth)
        got = lax.all_to_all(sending, "seq", split_axis=0, concat_axis=0, tiled=True)
        gathered = got.reshape(seq_count * portion, 2 * depth)
    mixed, grad_both = attend_group(gathered, grad_rows, key_blocks[group], key_counts[group])
    back_out, back_grad = (
        lax.all_to_all(
            mixed.reshape(seq_count, portion, depth),
            "seq",
            split_axis=0,
            concat_axis=0,
            tiled=True,
        ),
        lax.all_to_all(
            grad_both.reshape(seq_count, portion, 2 * depth),
            "seq",
            split_axis=0,
            concat_axis=0,
            tiled=True,
        ),
    )
    attention = back_out.reshape(heads, tokens_here, depth)[None]
    grad_proj = back_grad.reshape(heads, tokens_here, 2 * depth)
    seq_grad = jnp.einsum(
        "htc,dhc->td", grad_proj, head_weights, preferred_element_type=jnp.float32
    ).astype(jnp.bfloat16)[None]
    if groups == 1:
        rows_out = width // (rec_count * seq_count)
        head_grad = grad_both[places_all]
        partial = jnp.einsum(
            "od,oc->dc", owned_all, head_grad, preferred_element_type=jnp.float32
        )
        summed = lax.psum_scatter(partial, "rec", scatter_dimension=0, tiled=True)
        spread = lax.all_to_all(
            summed.reshape(seq_count, rows_out, 2 * depth),
            "seq",
            split_axis=0,
            concat_axis=0,
            tiled=True,
        )
        weight_grad = jnp.transpose(spread, (1, 0, 2))
    else:
        weight_grad = lax.psum_scatter(
            jnp.einsum("td,htc->dhc", tokens, grad_proj, preferred_element_type=jnp.float32),
            ("rec", "seq"),
            scatter_dimension=0,
            tiled=True,
        )
    return (attention, seq_grad, weight_grad)


def solution(mesh):
    placed = (P("rec", "seq", None), P("rec", "seq"), P(), P(), P(), P("rec", None, "seq", None))
    return jax.shard_map(
        local,
        mesh=mesh,
        in_specs=placed,
        out_specs=(
            P("rec", None, "seq", None),
            P("rec", "seq", None),
            P(("rec", "seq"), None, None),
        ),
        check_vma=False,
    )
```

```python
import jax
import jax.numpy as jnp
from jax import lax
from jax.sharding import PartitionSpec as P
from jax.experimental import pallas as pl
from jax.experimental.pallas import tpu as pltpu

BLOCK = 128


def attention_kernel(lists_ref, counts_ref, both_ref, grad_ref, out_ref, back_ref, acc_ref):
    nblocks, listed = lists_ref.shape
    depth = grad_ref.shape[1]
    scale = depth ** (-0.5)
    acc_ref[...] = jnp.zeros(acc_ref.shape, jnp.float32)
    col_block = lax.broadcasted_iota(jnp.int32, (BLOCK, listed * BLOCK), 1) // BLOCK
    trans_a = (((0,), (0,)), ((), ()))
    trans_b = (((1,), (1,)), ((), ()))

    def one_block(a, carry):
        start = pl.multiple_of(a * BLOCK, BLOCK)
        query = both_ref[pl.ds(start, BLOCK), :][:, :depth]
        upstream = grad_ref[pl.ds(start, BLOCK), :]
        active = counts_ref[a]
        picks = [jnp.clip(lists_ref[a, j], 0, nblocks - 1) for j in range(listed)]
        near = jnp.concatenate(
            [both_ref[pl.ds(pl.multiple_of(b * BLOCK, BLOCK), BLOCK), :] for b in picks], axis=0
        )
        keys = near[:, :depth]
        values = near[:, depth:]
        scores = lax.dot_general(query, keys, trans_b, preferred_element_type=jnp.float32) * scale
        usable = col_block < active
        scores = jnp.where(usable, scores, -jnp.inf)
        peak = jnp.max(scores, axis=1, keepdims=True)
        weights = jnp.where(usable, jnp.exp(scores - peak), 0.0)
        probs = weights / jnp.sum(weights, axis=1, keepdims=True)
        probs_low = probs.astype(jnp.bfloat16)
        mixed = jnp.dot(probs_low, values, preferred_element_type=jnp.float32)
        out_ref[pl.ds(start, BLOCK), :] = mixed.astype(out_ref.dtype)
        dprobs = lax.dot_general(upstream, values, trans_b, preferred_element_type=jnp.float32)
        inner = jnp.sum(probs * dprobs, axis=1, keepdims=True)
        dscores = (scale * probs * (dprobs - inner)).astype(jnp.bfloat16)
        dquery = jnp.dot(dscores, keys, preferred_element_type=jnp.float32)
        dkeys = lax.dot_general(dscores, query, trans_a, preferred_element_type=jnp.float32)
        dvalues = lax.dot_general(probs_low, upstream, trans_a, preferred_element_type=jnp.float32)
        both_grads = jnp.concatenate([dkeys, dvalues], axis=1)
        for j in range(listed):
            part = both_grads[j * BLOCK:(j + 1) * BLOCK]
            if j == 0:
                part = part + jnp.concatenate([dquery, jnp.zeros_like(dquery)], axis=1)

            @pl.when(j < active)
            def _():
                rows = pl.ds(pl.multiple_of(picks[j] * BLOCK, BLOCK), BLOCK)
                acc_ref[rows, :] += part

        return carry

    lax.fori_loop(0, nblocks, one_block, 0)
    back_ref[...] = acc_ref[...].astype(back_ref.dtype)


def attend_group(both, grad_rows, lists, counts):
    total, width = both.shape
    depth = grad_rows.shape[1]
    smem = pltpu.MemorySpace.SMEM
    vmem = pltpu.MemorySpace.VMEM
    return pl.pallas_call(
        attention_kernel,
        out_shape=(
            jax.ShapeDtypeStruct((total, depth), jnp.bfloat16),
            jax.ShapeDtypeStruct((total, width), jnp.bfloat16),
        ),
        in_specs=[
            pl.BlockSpec(memory_space=smem),
            pl.BlockSpec(memory_space=smem),
            pl.BlockSpec(memory_space=vmem),
            pl.BlockSpec(memory_space=vmem),
        ],
        out_specs=(pl.BlockSpec(memory_space=vmem), pl.BlockSpec(memory_space=vmem)),
        scratch_shapes=[pltpu.VMEM((total, width), jnp.float32)],
    )(lists, counts, both, grad_rows)


def route_tokens(rows_here, targets, seq_count, my_index):
    tokens_here, width = rows_here.shape
    room = 2 * tokens_here // seq_count - 1
    holders = targets // tokens_here
    order_ids = jnp.arange(tokens_here)
    earlier = order_ids[None, :] < order_ids[:, None]
    same_holder = holders[:, None] == holders[None, :]
    ranked = jnp.sum((earlier & same_holder).astype(jnp.int32), axis=1)
    slot_ids = holders * room + ranked
    outgoing = jnp.zeros((seq_count * room, width), rows_here.dtype).at[slot_ids].set(rows_here)
    outgoing = outgoing.reshape(seq_count, room, width)
    labels = (
        jnp.full((seq_count * room,), -1, jnp.int32)
        .at[slot_ids]
        .set(targets)
        .reshape(seq_count, room)
    )
    arrived, arrived_pos = (
        lax.all_to_all(outgoing, "seq", split_axis=0, concat_axis=0, tiled=True),
        lax.all_to_all(labels, "seq", split_axis=0, concat_axis=0, tiled=True),
    )
    local_ids = jnp.where(
        arrived_pos >= 0, arrived_pos - my_index * tokens_here, tokens_here
    ).reshape(-1)
    return (
        jnp.zeros((tokens_here, width), rows_here.dtype)
        .at[local_ids]
        .set(arrived.reshape(-1, width), mode="drop")
    )


def local(owned_rows, seq_position, head_weights, key_blocks, key_counts, out_grad):
    seq_count = lax.axis_size("seq")
    rec_count = lax.axis_size("rec")
    my_index = lax.axis_index("seq")
    tokens_here = owned_rows.shape[1]
    width = owned_rows.shape[2]
    heads = head_weights.shape[1]
    depth = head_weights.shape[2] // 2
    groups = seq_count // heads
    portion = tokens_here // groups
    rows_here = owned_rows[0]
    targets = seq_position[0]
    group = my_index % groups
    upstream = out_grad[0].reshape(seq_count, portion, depth)
    got_grad = lax.all_to_all(upstream, "seq", split_axis=0, concat_axis=0, tiled=True)
    grad_rows = got_grad.reshape(seq_count * portion, depth)
    if groups == 1:
        places_all = lax.all_to_all(
            jnp.broadcast_to(targets[None], (seq_count, tokens_here)),
            "seq",
            split_axis=0,
            concat_axis=0,
            tiled=True,
        ).reshape(-1)
        proj_mine = jnp.einsum(
            "td,dhc->htc", rows_here, head_weights, preferred_element_type=jnp.float32
        ).astype(jnp.bfloat16)
        proj_owned = lax.all_to_all(
            proj_mine, "seq", split_axis=0, concat_axis=0, tiled=True
        ).reshape(seq_count * tokens_here, 2 * depth)
        later_rows, proj_owned, grad_rows = lax.optimization_barrier(
            (rows_here, proj_owned, grad_rows)
        )
        owned_all = lax.all_gather(later_rows, "seq", axis=0, tiled=True)
        gathered = (
            jnp.zeros(proj_owned.shape, proj_owned.dtype)
            .at[places_all]
            .set(proj_owned, unique_indices=True)
        )
    else:
        tokens = route_tokens(rows_here, targets, seq_count, my_index)
        proj = jnp.einsum(
            "td,dhc->htc", tokens, head_weights, preferred_element_type=jnp.float32
        ).astype(jnp.bfloat16)
        sending = proj.reshape(seq_count, portion * 2 * depth)
        got = lax.all_to_all(sending, "seq", split_axis=0, concat_axis=0, tiled=True)
        gathered = got.reshape(seq_count * portion, 2 * depth)
    mixed, grad_both = attend_group(gathered, grad_rows, key_blocks[group], key_counts[group])
    back_out, back_grad = (
        lax.all_to_all(
            mixed.reshape(seq_count, portion, depth),
            "seq",
            split_axis=0,
            concat_axis=0,
            tiled=True,
        ),
        lax.all_to_all(
            grad_both.reshape(seq_count, portion, 2 * depth),
            "seq",
            split_axis=0,
            concat_axis=0,
            tiled=True,
        ),
    )
    attention = back_out.reshape(heads, tokens_here, depth)[None]
    grad_proj = back_grad.reshape(heads, tokens_here, 2 * depth)
    seq_grad = jnp.einsum(
        "htc,dhc->td", grad_proj, head_weights, preferred_element_type=jnp.float32
    ).astype(jnp.bfloat16)[None]
    if groups == 1:
        rows_out = width // (rec_count * seq_count)
        head_grad = grad_both[places_all]
        partial = jnp.einsum(
            "od,oc->dc", owned_all, head_grad, preferred_element_type=jnp.float32
        )
        summed = lax.psum_scatter(partial, "rec", scatter_dimension=0, tiled=True)
        spread = lax.all_to_all(
            summed.reshape(seq_count, rows_out, 2 * depth),
            "seq",
            split_axis=0,
            concat_axis=0,
            tiled=True,
        )
        weight_grad = jnp.transpose(spread, (1, 0, 2))
    else:
        weight_grad = lax.psum_scatter(
            jnp.einsum("td,htc->dhc", tokens, grad_proj, preferred_element_type=jnp.float32),
            ("rec", "seq"),
            scatter_dimension=0,
            tiled=True,
        )
    return (attention, seq_grad, weight_grad)


def solution(mesh):
    placed = (P("rec", "seq", None), P("rec", "seq"), P(), P(), P(), P("rec", None, "seq", None))
    return jax.shard_map(
        local,
        mesh=mesh,
        in_specs=placed,
        out_specs=(
            P("rec", None, "seq", None),
            P("rec", "seq", None),
            P(("rec", "seq"), None, None),
        ),
        check_vma=False,
    )
```

```python
import jax
import jax.numpy as jnp
from jax import lax
from jax.sharding import PartitionSpec as P
from jax.experimental import pallas as pl
from jax.experimental.pallas import tpu as pltpu

BLOCK = 128


def attention_kernel(lists_ref, counts_ref, both_ref, grad_ref, out_ref, back_ref, acc_ref):
    nblocks, listed = lists_ref.shape
    depth = grad_ref.shape[1]
    scale = depth ** (-0.5)
    acc_ref[...] = jnp.zeros(acc_ref.shape, jnp.float32)
    col_block = lax.broadcasted_iota(jnp.int32, (BLOCK, listed * BLOCK), 1) // BLOCK
    trans_a = (((0,), (0,)), ((), ()))
    trans_b = (((1,), (1,)), ((), ()))

    def one_block(a, carry):
        start = pl.multiple_of(a * BLOCK, BLOCK)
        query = both_ref[pl.ds(start, BLOCK), :][:, :depth]
        upstream = grad_ref[pl.ds(start, BLOCK), :]
        active = counts_ref[a]
        picks = [jnp.clip(lists_ref[a, j], 0, nblocks - 1) for j in range(listed)]
        near = jnp.concatenate(
            [both_ref[pl.ds(pl.multiple_of(b * BLOCK, BLOCK), BLOCK), :] for b in picks], axis=0
        )
        keys = near[:, :depth]
        values = near[:, depth:]
        scores = lax.dot_general(query, keys, trans_b, preferred_element_type=jnp.float32) * scale
        usable = col_block < active
        scores = jnp.where(usable, scores, -jnp.inf)
        peak = jnp.max(scores, axis=1, keepdims=True)
        weights = jnp.where(usable, jnp.exp(scores - peak), 0.0)
        probs = weights / jnp.sum(weights, axis=1, keepdims=True)
        probs_low = probs.astype(jnp.bfloat16)
        mixed = jnp.dot(probs_low, values, preferred_element_type=jnp.float32)
        out_ref[pl.ds(start, BLOCK), :] = mixed.astype(out_ref.dtype)
        dprobs = lax.dot_general(upstream, values, trans_b, preferred_element_type=jnp.float32)
        inner = jnp.sum(probs * dprobs, axis=1, keepdims=True)
        dscores = (scale * probs * (dprobs - inner)).astype(jnp.bfloat16)
        dquery = jnp.dot(dscores, keys, preferred_element_type=jnp.float32)
        dkeys = lax.dot_general(dscores, query, trans_a, preferred_element_type=jnp.float32)
        dvalues = lax.dot_general(probs_low, upstream, trans_a, preferred_element_type=jnp.float32)
        both_grads = jnp.concatenate([dkeys, dvalues], axis=1)
        for j in range(listed):
            part = both_grads[j * BLOCK:(j + 1) * BLOCK]
            if j == 0:
                part = part + jnp.concatenate([dquery, jnp.zeros_like(dquery)], axis=1)

            @pl.when(j < active)
            def _():
                rows = pl.ds(pl.multiple_of(picks[j] * BLOCK, BLOCK), BLOCK)
                acc_ref[rows, :] += part

        return carry

    lax.fori_loop(0, nblocks, one_block, 0)
    back_ref[...] = acc_ref[...].astype(back_ref.dtype)


def attend_group(both, grad_rows, lists, counts):
    total, width = both.shape
    depth = grad_rows.shape[1]
    smem = pltpu.MemorySpace.SMEM
    vmem = pltpu.MemorySpace.VMEM
    return pl.pallas_call(
        attention_kernel,
        out_shape=(
            jax.ShapeDtypeStruct((total, depth), jnp.bfloat16),
            jax.ShapeDtypeStruct((total, width), jnp.bfloat16),
        ),
        in_specs=[
            pl.BlockSpec(memory_space=smem),
            pl.BlockSpec(memory_space=smem),
            pl.BlockSpec(memory_space=vmem),
            pl.BlockSpec(memory_space=vmem),
        ],
        out_specs=(pl.BlockSpec(memory_space=vmem), pl.BlockSpec(memory_space=vmem)),
        scratch_shapes=[pltpu.VMEM((total, width), jnp.float32)],
    )(lists, counts, both, grad_rows)


def route_tokens(rows_here, targets, seq_count, my_index):
    tokens_here, width = rows_here.shape
    room = 2 * tokens_here // seq_count - 1
    holders = targets // tokens_here
    order_ids = jnp.arange(tokens_here)
    earlier = order_ids[None, :] < order_ids[:, None]
    same_holder = holders[:, None] == holders[None, :]
    ranked = jnp.sum((earlier & same_holder).astype(jnp.int32), axis=1)
    slot_ids = holders * room + ranked
    outgoing = jnp.zeros((seq_count * room, width), rows_here.dtype).at[slot_ids].set(rows_here)
    outgoing = outgoing.reshape(seq_count, room, width)
    labels = (
        jnp.full((seq_count * room,), -1, jnp.int32)
        .at[slot_ids]
        .set(targets)
        .reshape(seq_count, room)
    )
    arrived, arrived_pos = (
        lax.all_to_all(outgoing, "seq", split_axis=0, concat_axis=0, tiled=True),
        lax.all_to_all(labels, "seq", split_axis=0, concat_axis=0, tiled=True),
    )
    local_ids = jnp.where(
        arrived_pos >= 0, arrived_pos - my_index * tokens_here, tokens_here
    ).reshape(-1)
    return (
        jnp.zeros((tokens_here, width), rows_here.dtype)
        .at[local_ids]
        .set(arrived.reshape(-1, width), mode="drop")
    )


def local(owned_rows, seq_position, head_weights, key_blocks, key_counts, out_grad):
    seq_count = lax.axis_size("seq")
    rec_count = lax.axis_size("rec")
    my_index = lax.axis_index("seq")
    tokens_here = owned_rows.shape[1]
    width = owned_rows.shape[2]
    heads = head_weights.shape[1]
    depth = head_weights.shape[2] // 2
    groups = seq_count // heads
    portion = tokens_here // groups
    rows_here = owned_rows[0]
    targets = seq_position[0]
    group = my_index % groups
    upstream = out_grad[0].reshape(seq_count, portion, depth)
    got_grad = lax.all_to_all(upstream, "seq", split_axis=0, concat_axis=0, tiled=True)
    grad_rows = got_grad.reshape(seq_count * portion, depth)
    if groups == 1:
        places_all = lax.all_to_all(
            jnp.broadcast_to(targets[None], (seq_count, tokens_here)),
            "seq",
            split_axis=0,
            concat_axis=0,
            tiled=True,
        ).reshape(-1)
        proj_mine = jnp.einsum(
            "td,dhc->htc", rows_here, head_weights, preferred_element_type=jnp.float32
        ).astype(jnp.bfloat16)
        proj_owned = lax.all_to_all(
            proj_mine, "seq", split_axis=0, concat_axis=0, tiled=True
        ).reshape(seq_count * tokens_here, 2 * depth)
        later_rows, proj_owned, grad_rows = lax.optimization_barrier(
            (rows_here, proj_owned, grad_rows)
        )
        owned_all = lax.all_gather(later_rows, "seq", axis=0, tiled=True)
        gathered = (
            jnp.zeros(proj_owned.shape, proj_owned.dtype)
            .at[places_all]
            .set(proj_owned, unique_indices=True)
        )
    else:
        tokens = route_tokens(rows_here, targets, seq_count, my_index)
        proj = jnp.einsum(
            "td,dhc->htc", tokens, head_weights, preferred_element_type=jnp.float32
        ).astype(jnp.bfloat16)
        sending = proj.reshape(seq_count, portion * 2 * depth)
        got = lax.all_to_all(sending, "seq", split_axis=0, concat_axis=0, tiled=True)
        gathered = got.reshape(seq_count * portion, 2 * depth)
    mixed, grad_both = attend_group(gathered, grad_rows, key_blocks[group], key_counts[group])
    back_out, back_grad = (
        lax.all_to_all(
            mixed.reshape(seq_count, portion, depth),
            "seq",
            split_axis=0,
            concat_axis=0,
            tiled=True,
        ),
        lax.all_to_all(
            grad_both.reshape(seq_count, portion, 2 * depth),
            "seq",
            split_axis=0,
            concat_axis=0,
            tiled=True,
        ),
    )
    attention = back_out.reshape(heads, tokens_here, depth)[None]
    grad_proj = back_grad.reshape(heads, tokens_here, 2 * depth)
    seq_grad = jnp.einsum(
        "htc,dhc->td", grad_proj, head_weights, preferred_element_type=jnp.float32
    ).astype(jnp.bfloat16)[None]
    if groups == 1:
        rows_out = width // (rec_count * seq_count)
        head_grad = grad_both[places_all]
        partial = jnp.einsum(
            "od,oc->dc", owned_all, head_grad, preferred_element_type=jnp.float32
        )
        pieces = lax.all_to_all(
            partial.reshape(rec_count, width // rec_count, 2 * depth),
            "rec",
            split_axis=0,
            concat_axis=0,
            tiled=True,
        )
        summed = jnp.sum(pieces, axis=0)
        spread = lax.all_to_all(
            summed.reshape(seq_count, rows_out, 2 * depth),
            "seq",
            split_axis=0,
            concat_axis=0,
            tiled=True,
        )
        weight_grad = jnp.transpose(spread, (1, 0, 2))
    else:
        weight_grad = lax.psum_scatter(
            jnp.einsum("td,htc->dhc", tokens, grad_proj, preferred_element_type=jnp.float32),
            ("rec", "seq"),
            scatter_dimension=0,
            tiled=True,
        )
    return (attention, seq_grad, weight_grad)


def solution(mesh):
    placed = (P("rec", "seq", None), P("rec", "seq"), P(), P(), P(), P("rec", None, "seq", None))
    return jax.shard_map(
        local,
        mesh=mesh,
        in_specs=placed,
        out_specs=(
            P("rec", None, "seq", None),
            P("rec", "seq", None),
            P(("rec", "seq"), None, None),
        ),
        check_vma=False,
    )
```

```python
import jax
import jax.numpy as jnp
from jax import lax
from jax.sharding import PartitionSpec as P
from jax.experimental import pallas as pl
from jax.experimental.pallas import tpu as pltpu

BLOCK = 128


def attention_kernel(lists_ref, counts_ref, both_ref, grad_ref, out_ref, back_ref, acc_ref):
    nblocks, listed = lists_ref.shape
    depth = grad_ref.shape[1]
    scale = depth ** (-0.5)
    acc_ref[...] = jnp.zeros(acc_ref.shape, jnp.float32)
    col_block = lax.broadcasted_iota(jnp.int32, (BLOCK, listed * BLOCK), 1) // BLOCK
    trans_a = (((0,), (0,)), ((), ()))
    trans_b = (((1,), (1,)), ((), ()))

    def one_block(a, carry):
        start = pl.multiple_of(a * BLOCK, BLOCK)
        query = both_ref[pl.ds(start, BLOCK), :][:, :depth]
        upstream = grad_ref[pl.ds(start, BLOCK), :]
        active = counts_ref[a]
        picks = [jnp.clip(lists_ref[a, j], 0, nblocks - 1) for j in range(listed)]
        near = jnp.concatenate(
            [both_ref[pl.ds(pl.multiple_of(b * BLOCK, BLOCK), BLOCK), :] for b in picks], axis=0
        )
        keys = near[:, :depth]
        values = near[:, depth:]
        scores = lax.dot_general(query, keys, trans_b, preferred_element_type=jnp.float32) * scale
        usable = col_block < active
        scores = jnp.where(usable, scores, -jnp.inf)
        peak = jnp.max(scores, axis=1, keepdims=True)
        weights = jnp.where(usable, jnp.exp(scores - peak), 0.0)
        probs = weights / jnp.sum(weights, axis=1, keepdims=True)
        probs_low = probs.astype(jnp.bfloat16)
        mixed = jnp.dot(probs_low, values, preferred_element_type=jnp.float32)
        out_ref[pl.ds(start, BLOCK), :] = mixed.astype(out_ref.dtype)
        dprobs = lax.dot_general(upstream, values, trans_b, preferred_element_type=jnp.float32)
        inner = jnp.sum(probs * dprobs, axis=1, keepdims=True)
        dscores = (scale * probs * (dprobs - inner)).astype(jnp.bfloat16)
        dquery = jnp.dot(dscores, keys, preferred_element_type=jnp.float32)
        dkeys = lax.dot_general(dscores, query, trans_a, preferred_element_type=jnp.float32)
        dvalues = lax.dot_general(probs_low, upstream, trans_a, preferred_element_type=jnp.float32)
        both_grads = jnp.concatenate([dkeys, dvalues], axis=1)
        for j in range(listed):
            part = both_grads[j * BLOCK:(j + 1) * BLOCK]
            if j == 0:
                part = part + jnp.concatenate([dquery, jnp.zeros_like(dquery)], axis=1)

            @pl.when(j < active)
            def _():
                rows = pl.ds(pl.multiple_of(picks[j] * BLOCK, BLOCK), BLOCK)
                acc_ref[rows, :] += part

        return carry

    lax.fori_loop(0, nblocks, one_block, 0)
    back_ref[...] = acc_ref[...].astype(back_ref.dtype)


def attend_group(both, grad_rows, lists, counts):
    total, width = both.shape
    depth = grad_rows.shape[1]
    smem = pltpu.MemorySpace.SMEM
    vmem = pltpu.MemorySpace.VMEM
    return pl.pallas_call(
        attention_kernel,
        out_shape=(
            jax.ShapeDtypeStruct((total, depth), jnp.bfloat16),
            jax.ShapeDtypeStruct((total, width), jnp.bfloat16),
        ),
        in_specs=[
            pl.BlockSpec(memory_space=smem),
            pl.BlockSpec(memory_space=smem),
            pl.BlockSpec(memory_space=vmem),
            pl.BlockSpec(memory_space=vmem),
        ],
        out_specs=(pl.BlockSpec(memory_space=vmem), pl.BlockSpec(memory_space=vmem)),
        scratch_shapes=[pltpu.VMEM((total, width), jnp.float32)],
    )(lists, counts, both, grad_rows)


def route_tokens(rows_here, targets, seq_count, my_index):
    tokens_here, width = rows_here.shape
    room = 2 * tokens_here // seq_count - 1
    holders = targets // tokens_here
    order_ids = jnp.arange(tokens_here)
    earlier = order_ids[None, :] < order_ids[:, None]
    same_holder = holders[:, None] == holders[None, :]
    ranked = jnp.sum((earlier & same_holder).astype(jnp.int32), axis=1)
    slot_ids = holders * room + ranked
    outgoing = jnp.zeros((seq_count * room, width), rows_here.dtype).at[slot_ids].set(rows_here)
    outgoing = outgoing.reshape(seq_count, room, width)
    labels = (
        jnp.full((seq_count * room,), -1, jnp.int32)
        .at[slot_ids]
        .set(targets)
        .reshape(seq_count, room)
    )
    arrived, arrived_pos = (
        lax.all_to_all(outgoing, "seq", split_axis=0, concat_axis=0, tiled=True),
        lax.all_to_all(labels, "seq", split_axis=0, concat_axis=0, tiled=True),
    )
    local_ids = jnp.where(
        arrived_pos >= 0, arrived_pos - my_index * tokens_here, tokens_here
    ).reshape(-1)
    return (
        jnp.zeros((tokens_here, width), rows_here.dtype)
        .at[local_ids]
        .set(arrived.reshape(-1, width), mode="drop")
    )


def local(owned_rows, seq_position, head_weights, key_blocks, key_counts, out_grad):
    seq_count = lax.axis_size("seq")
    rec_count = lax.axis_size("rec")
    my_index = lax.axis_index("seq")
    tokens_here = owned_rows.shape[1]
    width = owned_rows.shape[2]
    heads = head_weights.shape[1]
    depth = head_weights.shape[2] // 2
    groups = seq_count // heads
    portion = tokens_here // groups
    rows_here = owned_rows[0]
    targets = seq_position[0]
    group = my_index % groups
    upstream = out_grad[0].reshape(seq_count, portion, depth)
    got_grad = lax.all_to_all(upstream, "seq", split_axis=0, concat_axis=0, tiled=True)
    grad_rows = got_grad.reshape(seq_count * portion, depth)
    if groups == 1:
        places_all = lax.all_to_all(
            jnp.broadcast_to(targets[None], (seq_count, tokens_here)),
            "seq",
            split_axis=0,
            concat_axis=0,
            tiled=True,
        ).reshape(-1)
        rows_ready, places_all = lax.optimization_barrier((rows_here, places_all))
        proj_mine = jnp.einsum(
            "td,dhc->htc", rows_ready, head_weights, preferred_element_type=jnp.float32
        ).astype(jnp.bfloat16)
        proj_owned = lax.all_to_all(
            proj_mine, "seq", split_axis=0, concat_axis=0, tiled=True
        ).reshape(seq_count * tokens_here, 2 * depth)
        later_rows, proj_owned, grad_rows = lax.optimization_barrier(
            (rows_here, proj_owned, grad_rows)
        )
        owned_all = lax.all_gather(later_rows, "seq", axis=0, tiled=True)
        gathered = (
            jnp.zeros(proj_owned.shape, proj_owned.dtype)
            .at[places_all]
            .set(proj_owned, unique_indices=True)
        )
    else:
        tokens = route_tokens(rows_here, targets, seq_count, my_index)
        proj = jnp.einsum(
            "td,dhc->htc", tokens, head_weights, preferred_element_type=jnp.float32
        ).astype(jnp.bfloat16)
        sending = proj.reshape(seq_count, portion * 2 * depth)
        got = lax.all_to_all(sending, "seq", split_axis=0, concat_axis=0, tiled=True)
        gathered = got.reshape(seq_count * portion, 2 * depth)
    mixed, grad_both = attend_group(gathered, grad_rows, key_blocks[group], key_counts[group])
    back_out, back_grad = (
        lax.all_to_all(
            mixed.reshape(seq_count, portion, depth),
            "seq",
            split_axis=0,
            concat_axis=0,
            tiled=True,
        ),
        lax.all_to_all(
            grad_both.reshape(seq_count, portion, 2 * depth),
            "seq",
            split_axis=0,
            concat_axis=0,
            tiled=True,
        ),
    )
    attention = back_out.reshape(heads, tokens_here, depth)[None]
    grad_proj = back_grad.reshape(heads, tokens_here, 2 * depth)
    seq_grad = jnp.einsum(
        "htc,dhc->td", grad_proj, head_weights, preferred_element_type=jnp.float32
    ).astype(jnp.bfloat16)[None]
    if groups == 1:
        rows_out = width // (rec_count * seq_count)
        head_grad = grad_both[places_all]
        partial = jnp.einsum(
            "od,oc->dc", owned_all, head_grad, preferred_element_type=jnp.float32
        )
        summed = lax.psum_scatter(partial, "rec", scatter_dimension=0, tiled=True)
        spread = lax.all_to_all(
            summed.reshape(seq_count, rows_out, 2 * depth),
            "seq",
            split_axis=0,
            concat_axis=0,
            tiled=True,
        )
        weight_grad = jnp.transpose(spread, (1, 0, 2))
    else:
        weight_grad = lax.psum_scatter(
            jnp.einsum("td,htc->dhc", tokens, grad_proj, preferred_element_type=jnp.float32),
            ("rec", "seq"),
            scatter_dimension=0,
            tiled=True,
        )
    return (attention, seq_grad, weight_grad)


def solution(mesh):
    placed = (P("rec", "seq", None), P("rec", "seq"), P(), P(), P(), P("rec", None, "seq", None))
    return jax.shard_map(
        local,
        mesh=mesh,
        in_specs=placed,
        out_specs=(
            P("rec", None, "seq", None),
            P("rec", "seq", None),
            P(("rec", "seq"), None, None),
        ),
        check_vma=False,
    )
```

```python
import jax
import jax.numpy as jnp
from jax import lax
from jax.sharding import PartitionSpec as P
from jax.experimental import pallas as pl
from jax.experimental.pallas import tpu as pltpu

BLOCK = 128


def attention_kernel(lists_ref, counts_ref, both_ref, grad_ref, out_ref, back_ref, acc_ref):
    nblocks, listed = lists_ref.shape
    depth = grad_ref.shape[1]
    scale = depth ** (-0.5)
    acc_ref[...] = jnp.zeros(acc_ref.shape, jnp.float32)
    col_block = lax.broadcasted_iota(jnp.int32, (BLOCK, listed * BLOCK), 1) // BLOCK
    trans_a = (((0,), (0,)), ((), ()))
    trans_b = (((1,), (1,)), ((), ()))

    def one_block(a, carry):
        start = pl.multiple_of(a * BLOCK, BLOCK)
        query = both_ref[pl.ds(start, BLOCK), :][:, :depth]
        upstream = grad_ref[pl.ds(start, BLOCK), :]
        active = counts_ref[a]
        picks = [jnp.clip(lists_ref[a, j], 0, nblocks - 1) for j in range(listed)]
        near = jnp.concatenate(
            [both_ref[pl.ds(pl.multiple_of(b * BLOCK, BLOCK), BLOCK), :] for b in picks], axis=0
        )
        keys = near[:, :depth]
        values = near[:, depth:]
        scores = lax.dot_general(query, keys, trans_b, preferred_element_type=jnp.float32) * scale
        usable = col_block < active
        scores = jnp.where(usable, scores, -jnp.inf)
        peak = jnp.max(scores, axis=1, keepdims=True)
        weights = jnp.where(usable, jnp.exp(scores - peak), 0.0)
        probs = weights / jnp.sum(weights, axis=1, keepdims=True)
        probs_low = probs.astype(jnp.bfloat16)
        mixed = jnp.dot(probs_low, values, preferred_element_type=jnp.float32)
        out_ref[pl.ds(start, BLOCK), :] = mixed.astype(out_ref.dtype)
        dprobs = lax.dot_general(upstream, values, trans_b, preferred_element_type=jnp.float32)
        inner = jnp.sum(probs * dprobs, axis=1, keepdims=True)
        dscores = (scale * probs * (dprobs - inner)).astype(jnp.bfloat16)
        dquery = jnp.dot(dscores, keys, preferred_element_type=jnp.float32)
        dkeys = lax.dot_general(dscores, query, trans_a, preferred_element_type=jnp.float32)
        dvalues = lax.dot_general(probs_low, upstream, trans_a, preferred_element_type=jnp.float32)
        both_grads = jnp.concatenate([dkeys, dvalues], axis=1)
        for j in range(listed):
            part = both_grads[j * BLOCK:(j + 1) * BLOCK]
            if j == 0:
                part = part + jnp.concatenate([dquery, jnp.zeros_like(dquery)], axis=1)

            @pl.when(j < active)
            def _():
                rows = pl.ds(pl.multiple_of(picks[j] * BLOCK, BLOCK), BLOCK)
                acc_ref[rows, :] += part

        return carry

    lax.fori_loop(0, nblocks, one_block, 0)
    back_ref[...] = acc_ref[...].astype(back_ref.dtype)


def attend_group(both, grad_rows, lists, counts):
    total, width = both.shape
    depth = grad_rows.shape[1]
    smem = pltpu.MemorySpace.SMEM
    vmem = pltpu.MemorySpace.VMEM
    return pl.pallas_call(
        attention_kernel,
        out_shape=(
            jax.ShapeDtypeStruct((total, depth), jnp.bfloat16),
            jax.ShapeDtypeStruct((total, width), jnp.bfloat16),
        ),
        in_specs=[
            pl.BlockSpec(memory_space=smem),
            pl.BlockSpec(memory_space=smem),
            pl.BlockSpec(memory_space=vmem),
            pl.BlockSpec(memory_space=vmem),
        ],
        out_specs=(pl.BlockSpec(memory_space=vmem), pl.BlockSpec(memory_space=vmem)),
        scratch_shapes=[pltpu.VMEM((total, width), jnp.float32)],
    )(lists, counts, both, grad_rows)


def route_tokens(rows_here, targets, seq_count, my_index):
    tokens_here, width = rows_here.shape
    room = 2 * tokens_here // seq_count - 1
    holders = targets // tokens_here
    order_ids = jnp.arange(tokens_here)
    earlier = order_ids[None, :] < order_ids[:, None]
    same_holder = holders[:, None] == holders[None, :]
    ranked = jnp.sum((earlier & same_holder).astype(jnp.int32), axis=1)
    slot_ids = holders * room + ranked
    outgoing = jnp.zeros((seq_count * room, width), rows_here.dtype).at[slot_ids].set(rows_here)
    outgoing = outgoing.reshape(seq_count, room, width)
    labels = (
        jnp.full((seq_count * room,), -1, jnp.int32)
        .at[slot_ids]
        .set(targets)
        .reshape(seq_count, room)
    )
    arrived, arrived_pos = (
        lax.all_to_all(outgoing, "seq", split_axis=0, concat_axis=0, tiled=True),
        lax.all_to_all(labels, "seq", split_axis=0, concat_axis=0, tiled=True),
    )
    local_ids = jnp.where(
        arrived_pos >= 0, arrived_pos - my_index * tokens_here, tokens_here
    ).reshape(-1)
    return (
        jnp.zeros((tokens_here, width), rows_here.dtype)
        .at[local_ids]
        .set(arrived.reshape(-1, width), mode="drop")
    )


def local(owned_rows, seq_position, head_weights, key_blocks, key_counts, out_grad):
    seq_count = lax.axis_size("seq")
    rec_count = lax.axis_size("rec")
    my_index = lax.axis_index("seq")
    tokens_here = owned_rows.shape[1]
    width = owned_rows.shape[2]
    heads = head_weights.shape[1]
    depth = head_weights.shape[2] // 2
    groups = seq_count // heads
    portion = tokens_here // groups
    rows_here = owned_rows[0]
    targets = seq_position[0]
    group = my_index % groups
    upstream = out_grad[0].reshape(seq_count, portion, depth)
    got_grad = lax.all_to_all(upstream, "seq", split_axis=0, concat_axis=0, tiled=True)
    grad_rows = got_grad.reshape(seq_count * portion, depth)
    if groups == 1:
        places_all = lax.all_to_all(
            jnp.broadcast_to(targets[None], (seq_count, tokens_here)),
            "seq",
            split_axis=0,
            concat_axis=0,
            tiled=True,
        ).reshape(-1)
        proj_mine = jnp.einsum(
            "td,dhc->htc", rows_here, head_weights, preferred_element_type=jnp.float32
        ).astype(jnp.bfloat16)
        proj_owned = lax.all_to_all(
            proj_mine, "seq", split_axis=0, concat_axis=0, tiled=True
        ).reshape(seq_count * tokens_here, 2 * depth)
        later_rows, proj_owned, grad_rows = lax.optimization_barrier(
            (rows_here, proj_owned, grad_rows)
        )
        owned_all = lax.all_gather(later_rows, "seq", axis=0, tiled=True)
        slots = jnp.arange(places_all.shape[0], dtype=places_all.dtype)
        placing = (slots[:, None] == places_all[None, :]).astype(jnp.bfloat16)
        gathered = jnp.dot(placing, proj_owned, preferred_element_type=jnp.float32).astype(
            jnp.bfloat16
        )
    else:
        tokens = route_tokens(rows_here, targets, seq_count, my_index)
        proj = jnp.einsum(
            "td,dhc->htc", tokens, head_weights, preferred_element_type=jnp.float32
        ).astype(jnp.bfloat16)
        sending = proj.reshape(seq_count, portion * 2 * depth)
        got = lax.all_to_all(sending, "seq", split_axis=0, concat_axis=0, tiled=True)
        gathered = got.reshape(seq_count * portion, 2 * depth)
    mixed, grad_both = attend_group(gathered, grad_rows, key_blocks[group], key_counts[group])
    back_out, back_grad = (
        lax.all_to_all(
            mixed.reshape(seq_count, portion, depth),
            "seq",
            split_axis=0,
            concat_axis=0,
            tiled=True,
        ),
        lax.all_to_all(
            grad_both.reshape(seq_count, portion, 2 * depth),
            "seq",
            split_axis=0,
            concat_axis=0,
            tiled=True,
        ),
    )
    attention = back_out.reshape(heads, tokens_here, depth)[None]
    grad_proj = back_grad.reshape(heads, tokens_here, 2 * depth)
    seq_grad = jnp.einsum(
        "htc,dhc->td", grad_proj, head_weights, preferred_element_type=jnp.float32
    ).astype(jnp.bfloat16)[None]
    if groups == 1:
        rows_out = width // (rec_count * seq_count)
        head_grad = lax.dot_general(
            placing, grad_both, (((0,), (0,)), ((), ())), preferred_element_type=jnp.float32
        ).astype(jnp.bfloat16)
        partial = jnp.einsum(
            "od,oc->dc", owned_all, head_grad, preferred_element_type=jnp.float32
        )
        summed = lax.psum_scatter(partial, "rec", scatter_dimension=0, tiled=True)
        spread = lax.all_to_all(
            summed.reshape(seq_count, rows_out, 2 * depth),
            "seq",
            split_axis=0,
            concat_axis=0,
            tiled=True,
        )
        weight_grad = jnp.transpose(spread, (1, 0, 2))
    else:
        weight_grad = lax.psum_scatter(
            jnp.einsum("td,htc->dhc", tokens, grad_proj, preferred_element_type=jnp.float32),
            ("rec", "seq"),
            scatter_dimension=0,
            tiled=True,
        )
    return (attention, seq_grad, weight_grad)


def solution(mesh):
    placed = (P("rec", "seq", None), P("rec", "seq"), P(), P(), P(), P("rec", None, "seq", None))
    return jax.shard_map(
        local,
        mesh=mesh,
        in_specs=placed,
        out_specs=(
            P("rec", None, "seq", None),
            P("rec", "seq", None),
            P(("rec", "seq"), None, None),
        ),
        check_vma=False,
    )
```

```python
import jax
import jax.numpy as jnp
from jax import lax
from jax.sharding import PartitionSpec as P
from jax.experimental import pallas as pl
from jax.experimental.pallas import tpu as pltpu

BLOCK = 128


def attention_kernel(lists_ref, counts_ref, both_ref, grad_ref, out_ref, back_ref, acc_ref):
    nblocks, listed = lists_ref.shape
    depth = grad_ref.shape[1]
    scale = depth ** (-0.5)
    acc_ref[...] = jnp.zeros(acc_ref.shape, jnp.float32)
    col_block = lax.broadcasted_iota(jnp.int32, (BLOCK, listed * BLOCK), 1) // BLOCK
    trans_a = (((0,), (0,)), ((), ()))
    trans_b = (((1,), (1,)), ((), ()))

    def one_block(a, carry):
        start = pl.multiple_of(a * BLOCK, BLOCK)
        query = both_ref[pl.ds(start, BLOCK), :][:, :depth]
        upstream = grad_ref[pl.ds(start, BLOCK), :]
        active = counts_ref[a]
        picks = [jnp.clip(lists_ref[a, j], 0, nblocks - 1) for j in range(listed)]
        near = jnp.concatenate(
            [both_ref[pl.ds(pl.multiple_of(b * BLOCK, BLOCK), BLOCK), :] for b in picks], axis=0
        )
        keys = near[:, :depth]
        values = near[:, depth:]
        scores = lax.dot_general(query, keys, trans_b, preferred_element_type=jnp.float32) * scale
        usable = col_block < active
        scores = jnp.where(usable, scores, -jnp.inf)
        peak = jnp.max(scores, axis=1, keepdims=True)
        weights = jnp.where(usable, jnp.exp(scores - peak), 0.0)
        probs = weights / jnp.sum(weights, axis=1, keepdims=True)
        probs_low = probs.astype(jnp.bfloat16)
        mixed = jnp.dot(probs_low, values, preferred_element_type=jnp.float32)
        out_ref[pl.ds(start, BLOCK), :] = mixed.astype(out_ref.dtype)
        dprobs = lax.dot_general(upstream, values, trans_b, preferred_element_type=jnp.float32)
        inner = jnp.sum(probs * dprobs, axis=1, keepdims=True)
        dscores = (scale * probs * (dprobs - inner)).astype(jnp.bfloat16)
        dquery = jnp.dot(dscores, keys, preferred_element_type=jnp.float32)
        dkeys = lax.dot_general(dscores, query, trans_a, preferred_element_type=jnp.float32)
        dvalues = lax.dot_general(probs_low, upstream, trans_a, preferred_element_type=jnp.float32)
        both_grads = jnp.concatenate([dkeys, dvalues], axis=1)
        for j in range(listed):
            part = both_grads[j * BLOCK:(j + 1) * BLOCK]
            if j == 0:
                part = part + jnp.concatenate([dquery, jnp.zeros_like(dquery)], axis=1)

            @pl.when(j < active)
            def _():
                rows = pl.ds(pl.multiple_of(picks[j] * BLOCK, BLOCK), BLOCK)
                acc_ref[rows, :] += part

        return carry

    lax.fori_loop(0, nblocks, one_block, 0)
    back_ref[...] = acc_ref[...].astype(back_ref.dtype)


def attend_group(both, grad_rows, lists, counts):
    total, width = both.shape
    depth = grad_rows.shape[1]
    smem = pltpu.MemorySpace.SMEM
    vmem = pltpu.MemorySpace.VMEM
    return pl.pallas_call(
        attention_kernel,
        out_shape=(
            jax.ShapeDtypeStruct((total, depth), jnp.bfloat16),
            jax.ShapeDtypeStruct((total, width), jnp.bfloat16),
        ),
        in_specs=[
            pl.BlockSpec(memory_space=smem),
            pl.BlockSpec(memory_space=smem),
            pl.BlockSpec(memory_space=vmem),
            pl.BlockSpec(memory_space=vmem),
        ],
        out_specs=(pl.BlockSpec(memory_space=vmem), pl.BlockSpec(memory_space=vmem)),
        scratch_shapes=[pltpu.VMEM((total, width), jnp.float32)],
    )(lists, counts, both, grad_rows)


def route_tokens(rows_here, targets, seq_count, my_index):
    tokens_here, width = rows_here.shape
    room = 2 * tokens_here // seq_count - 1
    holders = targets // tokens_here
    order_ids = jnp.arange(tokens_here)
    earlier = order_ids[None, :] < order_ids[:, None]
    same_holder = holders[:, None] == holders[None, :]
    ranked = jnp.sum((earlier & same_holder).astype(jnp.int32), axis=1)
    slot_ids = holders * room + ranked
    outgoing = jnp.zeros((seq_count * room, width), rows_here.dtype).at[slot_ids].set(rows_here)
    outgoing = outgoing.reshape(seq_count, room, width)
    labels = (
        jnp.full((seq_count * room,), -1, jnp.int32)
        .at[slot_ids]
        .set(targets)
        .reshape(seq_count, room)
    )
    arrived, arrived_pos = (
        lax.all_to_all(outgoing, "seq", split_axis=0, concat_axis=0, tiled=True),
        lax.all_to_all(labels, "seq", split_axis=0, concat_axis=0, tiled=True),
    )
    local_ids = jnp.where(
        arrived_pos >= 0, arrived_pos - my_index * tokens_here, tokens_here
    ).reshape(-1)
    return (
        jnp.zeros((tokens_here, width), rows_here.dtype)
        .at[local_ids]
        .set(arrived.reshape(-1, width), mode="drop")
    )


def local(owned_rows, seq_position, head_weights, key_blocks, key_counts, out_grad):
    seq_count = lax.axis_size("seq")
    rec_count = lax.axis_size("rec")
    my_index = lax.axis_index("seq")
    tokens_here = owned_rows.shape[1]
    width = owned_rows.shape[2]
    heads = head_weights.shape[1]
    depth = head_weights.shape[2] // 2
    groups = seq_count // heads
    portion = tokens_here // groups
    rows_here = owned_rows[0]
    targets = seq_position[0]
    group = my_index % groups
    upstream = out_grad[0].reshape(seq_count, portion, depth)
    if groups == 1:
        extra = ((2 * tokens_here + depth - 1) // depth + 15) // 16 * 16
        coded = jnp.concatenate([targets // 256, targets % 256]).astype(jnp.bfloat16)
        coded = jnp.pad(coded, (0, extra * depth - coded.shape[0])).reshape(extra, depth)
        sent = jnp.concatenate(
            [upstream, jnp.broadcast_to(coded[None], (seq_count, extra, depth))], axis=1
        )
        got_both = lax.all_to_all(sent, "seq", split_axis=0, concat_axis=0, tiled=True)
        grad_rows = got_both[:, :portion].reshape(seq_count * portion, depth)
        codes = got_both[:, portion:].reshape(seq_count, extra * depth).astype(jnp.float32)
        places_all = (
            codes[:, :tokens_here] * 256 + codes[:, tokens_here : 2 * tokens_here]
        ).astype(jnp.int32).reshape(-1)
        proj_mine = jnp.einsum(
            "td,dhc->htc", rows_here, head_weights, preferred_element_type=jnp.float32
        ).astype(jnp.bfloat16)
        proj_owned = lax.all_to_all(
            proj_mine, "seq", split_axis=0, concat_axis=0, tiled=True
        ).reshape(seq_count * tokens_here, 2 * depth)
        later_rows, proj_owned, grad_rows = lax.optimization_barrier(
            (rows_here, proj_owned, grad_rows)
        )
        owned_all = lax.all_gather(later_rows, "seq", axis=0, tiled=True)
        slots = jnp.arange(places_all.shape[0], dtype=places_all.dtype)
        placing = (slots[:, None] == places_all[None, :]).astype(jnp.bfloat16)
        gathered = jnp.dot(placing, proj_owned, preferred_element_type=jnp.float32).astype(
            jnp.bfloat16
        )
    else:
        got_grad = lax.all_to_all(upstream, "seq", split_axis=0, concat_axis=0, tiled=True)
        grad_rows = got_grad.reshape(seq_count * portion, depth)
        tokens = route_tokens(rows_here, targets, seq_count, my_index)
        proj = jnp.einsum(
            "td,dhc->htc", tokens, head_weights, preferred_element_type=jnp.float32
        ).astype(jnp.bfloat16)
        sending = proj.reshape(seq_count, portion * 2 * depth)
        got = lax.all_to_all(sending, "seq", split_axis=0, concat_axis=0, tiled=True)
        gathered = got.reshape(seq_count * portion, 2 * depth)
    mixed, grad_both = attend_group(gathered, grad_rows, key_blocks[group], key_counts[group])
    back_out, back_grad = (
        lax.all_to_all(
            mixed.reshape(seq_count, portion, depth),
            "seq",
            split_axis=0,
            concat_axis=0,
            tiled=True,
        ),
        lax.all_to_all(
            grad_both.reshape(seq_count, portion, 2 * depth),
            "seq",
            split_axis=0,
            concat_axis=0,
            tiled=True,
        ),
    )
    attention = back_out.reshape(heads, tokens_here, depth)[None]
    grad_proj = back_grad.reshape(heads, tokens_here, 2 * depth)
    seq_grad = jnp.einsum(
        "htc,dhc->td", grad_proj, head_weights, preferred_element_type=jnp.float32
    ).astype(jnp.bfloat16)[None]
    if groups == 1:
        rows_out = width // (rec_count * seq_count)
        head_grad = lax.dot_general(
            placing, grad_both, (((0,), (0,)), ((), ())), preferred_element_type=jnp.float32
        ).astype(jnp.bfloat16)
        partial = jnp.einsum(
            "od,oc->dc", owned_all, head_grad, preferred_element_type=jnp.float32
        )
        summed = lax.psum_scatter(partial, "rec", scatter_dimension=0, tiled=True)
        spread = lax.all_to_all(
            summed.reshape(seq_count, rows_out, 2 * depth),
            "seq",
            split_axis=0,
            concat_axis=0,
            tiled=True,
        )
        weight_grad = jnp.transpose(spread, (1, 0, 2))
    else:
        weight_grad = lax.psum_scatter(
            jnp.einsum("td,htc->dhc", tokens, grad_proj, preferred_element_type=jnp.float32),
            ("rec", "seq"),
            scatter_dimension=0,
            tiled=True,
        )
    return (attention, seq_grad, weight_grad)


def solution(mesh):
    placed = (P("rec", "seq", None), P("rec", "seq"), P(), P(), P(), P("rec", None, "seq", None))
    return jax.shard_map(
        local,
        mesh=mesh,
        in_specs=placed,
        out_specs=(
            P("rec", None, "seq", None),
            P("rec", "seq", None),
            P(("rec", "seq"), None, None),
        ),
        check_vma=False,
    )
```

```python
import jax
import jax.numpy as jnp
from jax import lax
from jax.sharding import PartitionSpec as P
from jax.experimental import pallas as pl
from jax.experimental.pallas import tpu as pltpu

BLOCK = 128


def attention_kernel(lists_ref, counts_ref, both_ref, grad_ref, out_ref, back_ref, acc_ref):
    nblocks, listed = lists_ref.shape
    depth = grad_ref.shape[1]
    scale = depth ** (-0.5)
    acc_ref[...] = jnp.zeros(acc_ref.shape, jnp.float32)
    col_block = lax.broadcasted_iota(jnp.int32, (BLOCK, listed * BLOCK), 1) // BLOCK
    trans_a = (((0,), (0,)), ((), ()))
    trans_b = (((1,), (1,)), ((), ()))

    def one_block(a, carry):
        start = pl.multiple_of(a * BLOCK, BLOCK)
        query = both_ref[pl.ds(start, BLOCK), :][:, :depth]
        upstream = grad_ref[pl.ds(start, BLOCK), :]
        active = counts_ref[a]
        picks = [jnp.clip(lists_ref[a, j], 0, nblocks - 1) for j in range(listed)]
        near = jnp.concatenate(
            [both_ref[pl.ds(pl.multiple_of(b * BLOCK, BLOCK), BLOCK), :] for b in picks], axis=0
        )
        keys = near[:, :depth]
        values = near[:, depth:]
        scores = lax.dot_general(query, keys, trans_b, preferred_element_type=jnp.float32) * scale
        usable = col_block < active
        scores = jnp.where(usable, scores, -jnp.inf)
        peak = jnp.max(scores, axis=1, keepdims=True)
        weights = jnp.where(usable, jnp.exp(scores - peak), 0.0)
        probs = weights / jnp.sum(weights, axis=1, keepdims=True)
        probs_low = probs.astype(jnp.bfloat16)
        mixed = jnp.dot(probs_low, values, preferred_element_type=jnp.float32)
        out_ref[pl.ds(start, BLOCK), :] = mixed.astype(out_ref.dtype)
        dprobs = lax.dot_general(upstream, values, trans_b, preferred_element_type=jnp.float32)
        inner = jnp.sum(probs * dprobs, axis=1, keepdims=True)
        dscores = (scale * probs * (dprobs - inner)).astype(jnp.bfloat16)
        dquery = jnp.dot(dscores, keys, preferred_element_type=jnp.float32)
        dkeys = lax.dot_general(dscores, query, trans_a, preferred_element_type=jnp.float32)
        dvalues = lax.dot_general(probs_low, upstream, trans_a, preferred_element_type=jnp.float32)
        both_grads = jnp.concatenate([dkeys, dvalues], axis=1)
        for j in range(listed):
            part = both_grads[j * BLOCK:(j + 1) * BLOCK]
            if j == 0:
                part = part + jnp.concatenate([dquery, jnp.zeros_like(dquery)], axis=1)

            @pl.when(j < active)
            def _():
                rows = pl.ds(pl.multiple_of(picks[j] * BLOCK, BLOCK), BLOCK)
                acc_ref[rows, :] += part

        return carry

    lax.fori_loop(0, nblocks, one_block, 0)
    back_ref[...] = acc_ref[...].astype(back_ref.dtype)


def attend_group(both, grad_rows, lists, counts):
    total, width = both.shape
    depth = grad_rows.shape[1]
    smem = pltpu.MemorySpace.SMEM
    vmem = pltpu.MemorySpace.VMEM
    return pl.pallas_call(
        attention_kernel,
        out_shape=(
            jax.ShapeDtypeStruct((total, depth), jnp.bfloat16),
            jax.ShapeDtypeStruct((total, width), jnp.bfloat16),
        ),
        in_specs=[
            pl.BlockSpec(memory_space=smem),
            pl.BlockSpec(memory_space=smem),
            pl.BlockSpec(memory_space=vmem),
            pl.BlockSpec(memory_space=vmem),
        ],
        out_specs=(pl.BlockSpec(memory_space=vmem), pl.BlockSpec(memory_space=vmem)),
        scratch_shapes=[pltpu.VMEM((total, width), jnp.float32)],
    )(lists, counts, both, grad_rows)


def route_tokens(rows_here, targets, seq_count, my_index):
    tokens_here, width = rows_here.shape
    room = 2 * tokens_here // seq_count - 1
    holders = targets // tokens_here
    order_ids = jnp.arange(tokens_here)
    earlier = order_ids[None, :] < order_ids[:, None]
    same_holder = holders[:, None] == holders[None, :]
    ranked = jnp.sum((earlier & same_holder).astype(jnp.int32), axis=1)
    slot_ids = holders * room + ranked
    outgoing = jnp.zeros((seq_count * room, width), rows_here.dtype).at[slot_ids].set(rows_here)
    outgoing = outgoing.reshape(seq_count, room, width)
    labels = (
        jnp.full((seq_count * room,), -1, jnp.int32)
        .at[slot_ids]
        .set(targets)
        .reshape(seq_count, room)
    )
    arrived, arrived_pos = (
        lax.all_to_all(outgoing, "seq", split_axis=0, concat_axis=0, tiled=True),
        lax.all_to_all(labels, "seq", split_axis=0, concat_axis=0, tiled=True),
    )
    local_ids = jnp.where(
        arrived_pos >= 0, arrived_pos - my_index * tokens_here, tokens_here
    ).reshape(-1)
    return (
        jnp.zeros((tokens_here, width), rows_here.dtype)
        .at[local_ids]
        .set(arrived.reshape(-1, width), mode="drop")
    )


def local(owned_rows, seq_position, head_weights, key_blocks, key_counts, out_grad):
    seq_count = lax.axis_size("seq")
    rec_count = lax.axis_size("rec")
    my_index = lax.axis_index("seq")
    tokens_here = owned_rows.shape[1]
    width = owned_rows.shape[2]
    heads = head_weights.shape[1]
    depth = head_weights.shape[2] // 2
    groups = seq_count // heads
    portion = tokens_here // groups
    rows_here = owned_rows[0]
    targets = seq_position[0]
    group = my_index % groups
    upstream = out_grad[0].reshape(seq_count, portion, depth)
    if groups == 1:
        extra = ((2 * tokens_here + depth - 1) // depth + 15) // 16 * 16
        coded = jnp.concatenate([targets // 256, targets % 256]).astype(jnp.bfloat16)
        coded = jnp.pad(coded, (0, extra * depth - coded.shape[0])).reshape(extra, depth)
        sent = jnp.concatenate(
            [upstream, jnp.broadcast_to(coded[None], (seq_count, extra, depth))], axis=1
        )
        got_both = lax.all_to_all(sent, "seq", split_axis=0, concat_axis=0, tiled=True)
        grad_rows = got_both[:, :portion].reshape(seq_count * portion, depth)
        codes = got_both[:, portion:].reshape(seq_count, extra * depth).astype(jnp.float32)
        places_all = (
            codes[:, :tokens_here] * 256 + codes[:, tokens_here : 2 * tokens_here]
        ).astype(jnp.int32).reshape(-1)
        proj_mine = jnp.einsum(
            "td,dhc->htc", rows_here, head_weights, preferred_element_type=jnp.float32
        ).astype(jnp.bfloat16)
        proj_owned = lax.all_to_all(
            proj_mine, "seq", split_axis=0, concat_axis=0, tiled=True
        ).reshape(seq_count * tokens_here, 2 * depth)
        later_rows, proj_owned, grad_rows = lax.optimization_barrier(
            (rows_here, proj_owned, grad_rows)
        )
        owned_all = lax.all_gather(later_rows, "seq", axis=0, tiled=True)
        slots = jnp.arange(places_all.shape[0], dtype=places_all.dtype)
        placing = (slots[:, None] == places_all[None, :]).astype(jnp.bfloat16)
        gathered = jnp.dot(placing, proj_owned, preferred_element_type=jnp.float32).astype(
            jnp.bfloat16
        )
    else:
        got_grad = lax.all_to_all(upstream, "seq", split_axis=0, concat_axis=0, tiled=True)
        grad_rows = got_grad.reshape(seq_count * portion, depth)
        tokens = route_tokens(rows_here, targets, seq_count, my_index)
        proj = jnp.einsum(
            "td,dhc->htc", tokens, head_weights, preferred_element_type=jnp.float32
        ).astype(jnp.bfloat16)
        sending = proj.reshape(seq_count, portion * 2 * depth)
        got = lax.all_to_all(sending, "seq", split_axis=0, concat_axis=0, tiled=True)
        gathered = got.reshape(seq_count * portion, 2 * depth)
    mixed, grad_both = attend_group(gathered, grad_rows, key_blocks[group], key_counts[group])
    back_out, back_grad = (
        lax.all_to_all(
            mixed.reshape(seq_count, portion, depth),
            "seq",
            split_axis=0,
            concat_axis=0,
            tiled=True,
        ),
        lax.all_to_all(
            grad_both.reshape(seq_count, portion, 2 * depth),
            "seq",
            split_axis=0,
            concat_axis=0,
            tiled=True,
        ),
    )
    if groups == 1:
        head_grad = lax.dot_general(
            placing, grad_both, (((0,), (0,)), ((), ())), preferred_element_type=jnp.float32
        ).astype(jnp.bfloat16)
        head_grad, back_out, back_grad = lax.optimization_barrier((head_grad, back_out, back_grad))
    attention = back_out.reshape(heads, tokens_here, depth)[None]
    grad_proj = back_grad.reshape(heads, tokens_here, 2 * depth)
    seq_grad = jnp.einsum(
        "htc,dhc->td", grad_proj, head_weights, preferred_element_type=jnp.float32
    ).astype(jnp.bfloat16)[None]
    if groups == 1:
        rows_out = width // (rec_count * seq_count)
        partial = jnp.einsum(
            "od,oc->dc", owned_all, head_grad, preferred_element_type=jnp.float32
        )
        pieces = lax.all_to_all(
            partial.reshape(rec_count, width // rec_count, 2 * depth),
            "rec",
            split_axis=0,
            concat_axis=0,
            tiled=True,
        )
        summed = jnp.sum(pieces, axis=0)
        spread = lax.all_to_all(
            summed.reshape(seq_count, rows_out, 2 * depth),
            "seq",
            split_axis=0,
            concat_axis=0,
            tiled=True,
        )
        weight_grad = jnp.transpose(spread, (1, 0, 2))
    else:
        weight_grad = lax.psum_scatter(
            jnp.einsum("td,htc->dhc", tokens, grad_proj, preferred_element_type=jnp.float32),
            ("rec", "seq"),
            scatter_dimension=0,
            tiled=True,
        )
    return (attention, seq_grad, weight_grad)


def solution(mesh):
    placed = (P("rec", "seq", None), P("rec", "seq"), P(), P(), P(), P("rec", None, "seq", None))
    return jax.shard_map(
        local,
        mesh=mesh,
        in_specs=placed,
        out_specs=(
            P("rec", None, "seq", None),
            P("rec", "seq", None),
            P(("rec", "seq"), None, None),
        ),
        check_vma=False,
    )
```

```python
import jax
import jax.numpy as jnp
from jax import lax
from jax.sharding import PartitionSpec as P
from jax.experimental import pallas as pl
from jax.experimental.pallas import tpu as pltpu

BLOCK = 128


def attention_kernel(lists_ref, counts_ref, both_ref, grad_ref, out_ref, back_ref, acc_ref):
    nblocks, listed = lists_ref.shape
    depth = grad_ref.shape[1]
    scale = depth ** (-0.5)
    acc_ref[...] = jnp.zeros(acc_ref.shape, jnp.float32)
    col_block = lax.broadcasted_iota(jnp.int32, (BLOCK, listed * BLOCK), 1) // BLOCK
    trans_a = (((0,), (0,)), ((), ()))
    trans_b = (((1,), (1,)), ((), ()))

    def one_block(a, carry):
        start = pl.multiple_of(a * BLOCK, BLOCK)
        query = both_ref[pl.ds(start, BLOCK), :][:, :depth]
        upstream = grad_ref[pl.ds(start, BLOCK), :]
        active = counts_ref[a]
        picks = [jnp.clip(lists_ref[a, j], 0, nblocks - 1) for j in range(listed)]
        near = jnp.concatenate(
            [both_ref[pl.ds(pl.multiple_of(b * BLOCK, BLOCK), BLOCK), :] for b in picks], axis=0
        )
        keys = near[:, :depth]
        values = near[:, depth:]
        scores = lax.dot_general(query, keys, trans_b, preferred_element_type=jnp.float32) * scale
        usable = col_block < active
        scores = jnp.where(usable, scores, -jnp.inf)
        peak = jnp.max(scores, axis=1, keepdims=True)
        weights = jnp.where(usable, jnp.exp(scores - peak), 0.0)
        probs = weights / jnp.sum(weights, axis=1, keepdims=True)
        probs_low = probs.astype(jnp.bfloat16)
        mixed = jnp.dot(probs_low, values, preferred_element_type=jnp.float32)
        out_ref[pl.ds(start, BLOCK), :] = mixed.astype(out_ref.dtype)
        dprobs = lax.dot_general(upstream, values, trans_b, preferred_element_type=jnp.float32)
        inner = jnp.sum(probs * dprobs, axis=1, keepdims=True)
        dscores = (scale * probs * (dprobs - inner)).astype(jnp.bfloat16)
        dquery = jnp.dot(dscores, keys, preferred_element_type=jnp.float32)
        dkeys = lax.dot_general(dscores, query, trans_a, preferred_element_type=jnp.float32)
        dvalues = lax.dot_general(probs_low, upstream, trans_a, preferred_element_type=jnp.float32)
        both_grads = jnp.concatenate([dkeys, dvalues], axis=1)
        for j in range(listed):
            part = both_grads[j * BLOCK:(j + 1) * BLOCK]
            if j == 0:
                part = part + jnp.concatenate([dquery, jnp.zeros_like(dquery)], axis=1)

            @pl.when(j < active)
            def _():
                rows = pl.ds(pl.multiple_of(picks[j] * BLOCK, BLOCK), BLOCK)
                acc_ref[rows, :] += part

        return carry

    lax.fori_loop(0, nblocks, one_block, 0)
    back_ref[...] = acc_ref[...].astype(back_ref.dtype)


def attend_group(both, grad_rows, lists, counts):
    total, width = both.shape
    depth = grad_rows.shape[1]
    smem = pltpu.MemorySpace.SMEM
    vmem = pltpu.MemorySpace.VMEM
    return pl.pallas_call(
        attention_kernel,
        out_shape=(
            jax.ShapeDtypeStruct((total, depth), jnp.bfloat16),
            jax.ShapeDtypeStruct((total, width), jnp.bfloat16),
        ),
        in_specs=[
            pl.BlockSpec(memory_space=smem),
            pl.BlockSpec(memory_space=smem),
            pl.BlockSpec(memory_space=vmem),
            pl.BlockSpec(memory_space=vmem),
        ],
        out_specs=(pl.BlockSpec(memory_space=vmem), pl.BlockSpec(memory_space=vmem)),
        scratch_shapes=[pltpu.VMEM((total, width), jnp.float32)],
    )(lists, counts, both, grad_rows)


def route_tokens(rows_here, targets, seq_count, my_index):
    tokens_here, width = rows_here.shape
    room = 2 * tokens_here // seq_count - 1
    holders = targets // tokens_here
    order_ids = jnp.arange(tokens_here)
    earlier = order_ids[None, :] < order_ids[:, None]
    same_holder = holders[:, None] == holders[None, :]
    ranked = jnp.sum((earlier & same_holder).astype(jnp.int32), axis=1)
    slot_ids = holders * room + ranked
    outgoing = jnp.zeros((seq_count * room, width), rows_here.dtype).at[slot_ids].set(rows_here)
    outgoing = outgoing.reshape(seq_count, room, width)
    labels = (
        jnp.full((seq_count * room,), -1, jnp.int32)
        .at[slot_ids]
        .set(targets)
        .reshape(seq_count, room)
    )
    arrived, arrived_pos = (
        lax.all_to_all(outgoing, "seq", split_axis=0, concat_axis=0, tiled=True),
        lax.all_to_all(labels, "seq", split_axis=0, concat_axis=0, tiled=True),
    )
    local_ids = jnp.where(
        arrived_pos >= 0, arrived_pos - my_index * tokens_here, tokens_here
    ).reshape(-1)
    return (
        jnp.zeros((tokens_here, width), rows_here.dtype)
        .at[local_ids]
        .set(arrived.reshape(-1, width), mode="drop")
    )


def local(owned_rows, seq_position, head_weights, key_blocks, key_counts, out_grad):
    seq_count = lax.axis_size("seq")
    rec_count = lax.axis_size("rec")
    my_index = lax.axis_index("seq")
    tokens_here = owned_rows.shape[1]
    width = owned_rows.shape[2]
    heads = head_weights.shape[1]
    depth = head_weights.shape[2] // 2
    groups = seq_count // heads
    portion = tokens_here // groups
    rows_here = owned_rows[0]
    targets = seq_position[0]
    group = my_index % groups
    upstream = out_grad[0].reshape(seq_count, portion, depth)
    got_grad = lax.all_to_all(upstream, "seq", split_axis=0, concat_axis=0, tiled=True)
    grad_rows = got_grad.reshape(seq_count * portion, depth)
    if groups == 1:
        places_all = lax.all_to_all(
            jnp.broadcast_to(targets[None], (seq_count, tokens_here)),
            "seq",
            split_axis=0,
            concat_axis=0,
            tiled=True,
        ).reshape(-1)
        proj_mine = jnp.einsum(
            "td,dhc->htc", rows_here, head_weights, preferred_element_type=jnp.float32
        ).astype(jnp.bfloat16)
        proj_owned = lax.all_to_all(
            proj_mine, "seq", split_axis=0, concat_axis=0, tiled=True
        ).reshape(seq_count * tokens_here, 2 * depth)
        later_rows, proj_owned, grad_rows = lax.optimization_barrier(
            (rows_here, proj_owned, grad_rows)
        )
        owned_all = lax.all_gather(later_rows, "seq", axis=0, tiled=True)
        slots = jnp.arange(places_all.shape[0], dtype=places_all.dtype)
        placing = (slots[:, None] == places_all[None, :]).astype(jnp.bfloat16)
        gathered = jnp.dot(placing, proj_owned, preferred_element_type=jnp.float32).astype(
            jnp.bfloat16
        )
    else:
        tokens = route_tokens(rows_here, targets, seq_count, my_index)
        proj = jnp.einsum(
            "td,dhc->htc", tokens, head_weights, preferred_element_type=jnp.float32
        ).astype(jnp.bfloat16)
        sending = proj.reshape(seq_count, portion * 2 * depth)
        got = lax.all_to_all(sending, "seq", split_axis=0, concat_axis=0, tiled=True)
        gathered = got.reshape(seq_count * portion, 2 * depth)
    mixed, grad_both = attend_group(gathered, grad_rows, key_blocks[group], key_counts[group])
    back_out, back_grad = (
        lax.all_to_all(
            mixed.reshape(seq_count, portion, depth),
            "seq",
            split_axis=0,
            concat_axis=0,
            tiled=True,
        ),
        lax.all_to_all(
            grad_both.reshape(seq_count, portion, 2 * depth),
            "seq",
            split_axis=0,
            concat_axis=0,
            tiled=True,
        ),
    )
    attention = back_out.reshape(heads, tokens_here, depth)[None]
    grad_proj = back_grad.reshape(heads, tokens_here, 2 * depth)
    seq_grad = jnp.einsum(
        "htc,dhc->td", grad_proj, head_weights, preferred_element_type=jnp.float32
    ).astype(jnp.bfloat16)[None]
    if groups == 1:
        rows_out = width // (rec_count * seq_count)
        head_grad = lax.optimization_barrier(
            lax.dot_general(
                placing, grad_both, (((0,), (0,)), ((), ())), preferred_element_type=jnp.float32
            ).astype(jnp.bfloat16)
        )
        partial = jnp.einsum(
            "od,oc->dc", owned_all, head_grad, preferred_element_type=jnp.float32
        )
        summed = lax.psum_scatter(partial, "rec", scatter_dimension=0, tiled=True)
        spread = lax.all_to_all(
            summed.reshape(seq_count, rows_out, 2 * depth),
            "seq",
            split_axis=0,
            concat_axis=0,
            tiled=True,
        )
        weight_grad = jnp.transpose(spread, (1, 0, 2))
    else:
        weight_grad = lax.psum_scatter(
            jnp.einsum("td,htc->dhc", tokens, grad_proj, preferred_element_type=jnp.float32),
            ("rec", "seq"),
            scatter_dimension=0,
            tiled=True,
        )
    return (attention, seq_grad, weight_grad)


def solution(mesh):
    placed = (P("rec", "seq", None), P("rec", "seq"), P(), P(), P(), P("rec", None, "seq", None))
    return jax.shard_map(
        local,
        mesh=mesh,
        in_specs=placed,
        out_specs=(
            P("rec", None, "seq", None),
            P("rec", "seq", None),
            P(("rec", "seq"), None, None),
        ),
        check_vma=False,
    )
```

```python
import functools

import jax
import jax.numpy as jnp
from jax import lax
from jax.sharding import PartitionSpec as P
from jax.experimental import pallas as pl
from jax.experimental.pallas import tpu as pltpu

BLOCK = 128


def attention_kernel(lists_ref, counts_ref, both_ref, grad_ref, out_ref, back_ref, acc_ref):
    nblocks, listed = lists_ref.shape
    depth = grad_ref.shape[1]
    scale = depth ** (-0.5)
    acc_ref[...] = jnp.zeros(acc_ref.shape, jnp.float32)
    trans_a = (((0,), (0,)), ((), ()))
    trans_b = (((1,), (1,)), ((), ()))

    def attend(a, used):
        start = pl.multiple_of(a * BLOCK, BLOCK)
        query = both_ref[pl.ds(start, BLOCK), :][:, :depth]
        upstream = grad_ref[pl.ds(start, BLOCK), :]
        picks = [jnp.clip(lists_ref[a, j], 0, nblocks - 1) for j in range(used)]
        tiles = [both_ref[pl.ds(pl.multiple_of(b * BLOCK, BLOCK), BLOCK), :] for b in picks]
        near = tiles[0] if used == 1 else jnp.concatenate(tiles, axis=0)
        keys = near[:, :depth]
        values = near[:, depth:]
        scores = lax.dot_general(query, keys, trans_b, preferred_element_type=jnp.float32) * scale
        peak = jnp.max(scores, axis=1, keepdims=True)
        weights = jnp.exp(scores - peak)
        probs = weights / jnp.sum(weights, axis=1, keepdims=True)
        probs_low = probs.astype(jnp.bfloat16)
        mixed = jnp.dot(probs_low, values, preferred_element_type=jnp.float32)
        out_ref[pl.ds(start, BLOCK), :] = mixed.astype(out_ref.dtype)
        dprobs = lax.dot_general(upstream, values, trans_b, preferred_element_type=jnp.float32)
        inner = jnp.sum(probs * dprobs, axis=1, keepdims=True)
        dscores = (scale * probs * (dprobs - inner)).astype(jnp.bfloat16)
        dquery = jnp.dot(dscores, keys, preferred_element_type=jnp.float32)
        dkeys = lax.dot_general(dscores, query, trans_a, preferred_element_type=jnp.float32)
        dvalues = lax.dot_general(probs_low, upstream, trans_a, preferred_element_type=jnp.float32)
        both_grads = jnp.concatenate([dkeys, dvalues], axis=1)
        for j in range(used):
            part = both_grads[j * BLOCK:(j + 1) * BLOCK]
            if j == 0:
                part = part + jnp.concatenate([dquery, jnp.zeros_like(dquery)], axis=1)
            rows = pl.ds(pl.multiple_of(picks[j] * BLOCK, BLOCK), BLOCK)
            acc_ref[rows, :] += part

    def one_block(a, carry):
        active = jnp.clip(counts_ref[a], 1, listed)
        lax.switch(active - 1, [functools.partial(attend, a, used) for used in range(1, listed + 1)])
        return carry

    lax.fori_loop(0, nblocks, one_block, 0)
    back_ref[...] = acc_ref[...].astype(back_ref.dtype)


def attend_group(both, grad_rows, lists, counts):
    total, width = both.shape
    depth = grad_rows.shape[1]
    smem = pltpu.MemorySpace.SMEM
    vmem = pltpu.MemorySpace.VMEM
    return pl.pallas_call(
        attention_kernel,
        out_shape=(
            jax.ShapeDtypeStruct((total, depth), jnp.bfloat16),
            jax.ShapeDtypeStruct((total, width), jnp.bfloat16),
        ),
        in_specs=[
            pl.BlockSpec(memory_space=smem),
            pl.BlockSpec(memory_space=smem),
            pl.BlockSpec(memory_space=vmem),
            pl.BlockSpec(memory_space=vmem),
        ],
        out_specs=(pl.BlockSpec(memory_space=vmem), pl.BlockSpec(memory_space=vmem)),
        scratch_shapes=[pltpu.VMEM((total, width), jnp.float32)],
    )(lists, counts, both, grad_rows)


def route_tokens(rows_here, targets, seq_count, my_index):
    tokens_here, width = rows_here.shape
    room = 2 * tokens_here // seq_count - 1
    holders = targets // tokens_here
    order_ids = jnp.arange(tokens_here)
    earlier = order_ids[None, :] < order_ids[:, None]
    same_holder = holders[:, None] == holders[None, :]
    ranked = jnp.sum((earlier & same_holder).astype(jnp.int32), axis=1)
    slot_ids = holders * room + ranked
    outgoing = jnp.zeros((seq_count * room, width), rows_here.dtype).at[slot_ids].set(rows_here)
    outgoing = outgoing.reshape(seq_count, room, width)
    labels = (
        jnp.full((seq_count * room,), -1, jnp.int32)
        .at[slot_ids]
        .set(targets)
        .reshape(seq_count, room)
    )
    arrived, arrived_pos = (
        lax.all_to_all(outgoing, "seq", split_axis=0, concat_axis=0, tiled=True),
        lax.all_to_all(labels, "seq", split_axis=0, concat_axis=0, tiled=True),
    )
    local_ids = jnp.where(
        arrived_pos >= 0, arrived_pos - my_index * tokens_here, tokens_here
    ).reshape(-1)
    return (
        jnp.zeros((tokens_here, width), rows_here.dtype)
        .at[local_ids]
        .set(arrived.reshape(-1, width), mode="drop")
    )


def local(owned_rows, seq_position, head_weights, key_blocks, key_counts, out_grad):
    seq_count = lax.axis_size("seq")
    rec_count = lax.axis_size("rec")
    my_index = lax.axis_index("seq")
    tokens_here = owned_rows.shape[1]
    width = owned_rows.shape[2]
    heads = head_weights.shape[1]
    depth = head_weights.shape[2] // 2
    groups = seq_count // heads
    portion = tokens_here // groups
    rows_here = owned_rows[0]
    targets = seq_position[0]
    group = my_index % groups
    upstream = out_grad[0].reshape(seq_count, portion, depth)
    got_grad = lax.all_to_all(upstream, "seq", split_axis=0, concat_axis=0, tiled=True)
    grad_rows = got_grad.reshape(seq_count * portion, depth)
    if groups == 1:
        places_all = lax.all_to_all(
            jnp.broadcast_to(targets[None], (seq_count, tokens_here)),
            "seq",
            split_axis=0,
            concat_axis=0,
            tiled=True,
        ).reshape(-1)
        proj_mine = jnp.einsum(
            "td,dhc->htc", rows_here, head_weights, preferred_element_type=jnp.float32
        ).astype(jnp.bfloat16)
        proj_owned = lax.all_to_all(
            proj_mine, "seq", split_axis=0, concat_axis=0, tiled=True
        ).reshape(seq_count * tokens_here, 2 * depth)
        later_rows, proj_owned, grad_rows = lax.optimization_barrier(
            (rows_here, proj_owned, grad_rows)
        )
        owned_all = lax.all_gather(later_rows, "seq", axis=0, tiled=True)
        slots = jnp.arange(places_all.shape[0], dtype=places_all.dtype)
        placing = (slots[:, None] == places_all[None, :]).astype(jnp.bfloat16)
        gathered = jnp.dot(placing, proj_owned, preferred_element_type=jnp.float32).astype(
            jnp.bfloat16
        )
    else:
        tokens = route_tokens(rows_here, targets, seq_count, my_index)
        proj = jnp.einsum(
            "td,dhc->htc", tokens, head_weights, preferred_element_type=jnp.float32
        ).astype(jnp.bfloat16)
        sending = proj.reshape(seq_count, portion * 2 * depth)
        got = lax.all_to_all(sending, "seq", split_axis=0, concat_axis=0, tiled=True)
        gathered = got.reshape(seq_count * portion, 2 * depth)
    mixed, grad_both = attend_group(gathered, grad_rows, key_blocks[group], key_counts[group])
    back_out, back_grad = (
        lax.all_to_all(
            mixed.reshape(seq_count, portion, depth),
            "seq",
            split_axis=0,
            concat_axis=0,
            tiled=True,
        ),
        lax.all_to_all(
            grad_both.reshape(seq_count, portion, 2 * depth),
            "seq",
            split_axis=0,
            concat_axis=0,
            tiled=True,
        ),
    )
    attention = back_out.reshape(heads, tokens_here, depth)[None]
    grad_proj = back_grad.reshape(heads, tokens_here, 2 * depth)
    seq_grad = jnp.einsum(
        "htc,dhc->td", grad_proj, head_weights, preferred_element_type=jnp.float32
    ).astype(jnp.bfloat16)[None]
    if groups == 1:
        rows_out = width // (rec_count * seq_count)
        head_grad = lax.optimization_barrier(
            lax.dot_general(
                placing, grad_both, (((0,), (0,)), ((), ())), preferred_element_type=jnp.float32
            ).astype(jnp.bfloat16)
        )
        partial = jnp.einsum(
            "od,oc->dc", owned_all, head_grad, preferred_element_type=jnp.float32
        )
        summed = lax.psum_scatter(partial, "rec", scatter_dimension=0, tiled=True)
        spread = lax.all_to_all(
            summed.reshape(seq_count, rows_out, 2 * depth),
            "seq",
            split_axis=0,
            concat_axis=0,
            tiled=True,
        )
        weight_grad = jnp.transpose(spread, (1, 0, 2))
    else:
        weight_grad = lax.psum_scatter(
            jnp.einsum("td,htc->dhc", tokens, grad_proj, preferred_element_type=jnp.float32),
            ("rec", "seq"),
            scatter_dimension=0,
            tiled=True,
        )
    return (attention, seq_grad, weight_grad)


def solution(mesh):
    placed = (P("rec", "seq", None), P("rec", "seq"), P(), P(), P(), P("rec", None, "seq", None))
    return jax.shard_map(
        local,
        mesh=mesh,
        in_specs=placed,
        out_specs=(
            P("rec", None, "seq", None),
            P("rec", "seq", None),
            P(("rec", "seq"), None, None),
        ),
        check_vma=False,
    )
```

```python
import functools

import jax
import jax.numpy as jnp
from jax import lax
from jax.sharding import PartitionSpec as P
from jax.experimental import pallas as pl
from jax.experimental.pallas import tpu as pltpu

BLOCK = 128


def attention_kernel(lists_ref, counts_ref, both_ref, grad_ref, out_ref, back_ref, acc_ref):
    nblocks, listed = lists_ref.shape
    depth = grad_ref.shape[1]
    scale = depth ** (-0.5)
    acc_ref[...] = jnp.zeros(acc_ref.shape, jnp.float32)
    trans_a = (((0,), (0,)), ((), ()))
    trans_b = (((1,), (1,)), ((), ()))

    def attend(a, used):
        start = pl.multiple_of(a * BLOCK, BLOCK)
        query = both_ref[pl.ds(start, BLOCK), :][:, :depth]
        upstream = grad_ref[pl.ds(start, BLOCK), :]
        picks = [jnp.clip(lists_ref[a, j], 0, nblocks - 1) for j in range(used)]
        tiles = [both_ref[pl.ds(pl.multiple_of(b * BLOCK, BLOCK), BLOCK), :] for b in picks]
        near = tiles[0] if used == 1 else jnp.concatenate(tiles, axis=0)
        keys = near[:, :depth]
        values = near[:, depth:]
        scores = lax.dot_general(query, keys, trans_b, preferred_element_type=jnp.float32) * scale
        peak = jnp.max(scores, axis=1, keepdims=True)
        weights = jnp.exp(scores - peak)
        probs = weights / jnp.sum(weights, axis=1, keepdims=True)
        probs_low = probs.astype(jnp.bfloat16)
        mixed = jnp.dot(probs_low, values, preferred_element_type=jnp.float32)
        out_ref[pl.ds(start, BLOCK), :] = mixed.astype(out_ref.dtype)
        dprobs = lax.dot_general(upstream, values, trans_b, preferred_element_type=jnp.float32)
        inner = jnp.sum(probs * dprobs, axis=1, keepdims=True)
        dscores = (scale * probs * (dprobs - inner)).astype(jnp.bfloat16)
        dquery = jnp.dot(dscores, keys, preferred_element_type=jnp.float32)
        dkeys = lax.dot_general(dscores, query, trans_a, preferred_element_type=jnp.float32)
        dvalues = lax.dot_general(probs_low, upstream, trans_a, preferred_element_type=jnp.float32)
        both_grads = jnp.concatenate([dkeys, dvalues], axis=1)
        for j in range(used):
            part = both_grads[j * BLOCK:(j + 1) * BLOCK]
            if j == 0:
                part = part + jnp.concatenate([dquery, jnp.zeros_like(dquery)], axis=1)
            rows = pl.ds(pl.multiple_of(picks[j] * BLOCK, BLOCK), BLOCK)
            acc_ref[rows, :] += part

    def one_block(a, carry):
        active = jnp.clip(counts_ref[a], 1, listed)
        lax.switch(active - 1, [functools.partial(attend, a, used) for used in range(1, listed + 1)])
        return carry

    lax.fori_loop(0, nblocks, one_block, 0)
    back_ref[...] = acc_ref[...].astype(back_ref.dtype)


def attend_group(both, grad_rows, lists, counts):
    total, width = both.shape
    depth = grad_rows.shape[1]
    smem = pltpu.MemorySpace.SMEM
    vmem = pltpu.MemorySpace.VMEM
    return pl.pallas_call(
        attention_kernel,
        out_shape=(
            jax.ShapeDtypeStruct((total, depth), jnp.bfloat16),
            jax.ShapeDtypeStruct((total, width), jnp.bfloat16),
        ),
        in_specs=[
            pl.BlockSpec(memory_space=smem),
            pl.BlockSpec(memory_space=smem),
            pl.BlockSpec(memory_space=vmem),
            pl.BlockSpec(memory_space=vmem),
        ],
        out_specs=(pl.BlockSpec(memory_space=vmem), pl.BlockSpec(memory_space=vmem)),
        scratch_shapes=[pltpu.VMEM((total, width), jnp.float32)],
    )(lists, counts, both, grad_rows)


def route_tokens(rows_here, targets, seq_count, my_index):
    tokens_here, width = rows_here.shape
    room = 2 * tokens_here // seq_count - 1
    holders = targets // tokens_here
    order_ids = jnp.arange(tokens_here)
    earlier = order_ids[None, :] < order_ids[:, None]
    same_holder = holders[:, None] == holders[None, :]
    ranked = jnp.sum((earlier & same_holder).astype(jnp.int32), axis=1)
    slot_ids = holders * room + ranked
    outgoing = jnp.zeros((seq_count * room, width), rows_here.dtype).at[slot_ids].set(rows_here)
    outgoing = outgoing.reshape(seq_count, room, width)
    labels = (
        jnp.full((seq_count * room,), -1, jnp.int32)
        .at[slot_ids]
        .set(targets)
        .reshape(seq_count, room)
    )
    arrived, arrived_pos = (
        lax.all_to_all(outgoing, "seq", split_axis=0, concat_axis=0, tiled=True),
        lax.all_to_all(labels, "seq", split_axis=0, concat_axis=0, tiled=True),
    )
    local_ids = jnp.where(
        arrived_pos >= 0, arrived_pos - my_index * tokens_here, tokens_here
    ).reshape(-1)
    return (
        jnp.zeros((tokens_here, width), rows_here.dtype)
        .at[local_ids]
        .set(arrived.reshape(-1, width), mode="drop")
    )


def local(owned_rows, seq_position, head_weights, key_blocks, key_counts, out_grad):
    seq_count = lax.axis_size("seq")
    rec_count = lax.axis_size("rec")
    my_index = lax.axis_index("seq")
    tokens_here = owned_rows.shape[1]
    width = owned_rows.shape[2]
    heads = head_weights.shape[1]
    depth = head_weights.shape[2] // 2
    groups = seq_count // heads
    portion = tokens_here // groups
    rows_here = owned_rows[0]
    targets = seq_position[0]
    group = my_index % groups
    upstream = out_grad[0].reshape(seq_count, portion, depth)
    got_grad = lax.all_to_all(upstream, "seq", split_axis=0, concat_axis=0, tiled=True)
    grad_rows = got_grad.reshape(seq_count * portion, depth)
    if groups == 1:
        places_all = lax.all_to_all(
            jnp.broadcast_to(targets[None], (seq_count, tokens_here)),
            "seq",
            split_axis=0,
            concat_axis=0,
            tiled=True,
        ).reshape(-1)
        proj_mine = jnp.einsum(
            "td,dhc->htc", rows_here, head_weights, preferred_element_type=jnp.float32
        ).astype(jnp.bfloat16)
        proj_owned = lax.all_to_all(
            proj_mine, "seq", split_axis=0, concat_axis=0, tiled=True
        ).reshape(seq_count * tokens_here, 2 * depth)
        later_rows, grad_rows = lax.optimization_barrier((rows_here, grad_rows))
        owned_all = lax.all_gather(later_rows, "seq", axis=0, tiled=True)
        slots = jnp.arange(places_all.shape[0], dtype=places_all.dtype)
        placing = (slots[:, None] == places_all[None, :]).astype(jnp.bfloat16)
        gathered = jnp.dot(placing, proj_owned, preferred_element_type=jnp.float32).astype(
            jnp.bfloat16
        )
    else:
        tokens = route_tokens(rows_here, targets, seq_count, my_index)
        proj = jnp.einsum(
            "td,dhc->htc", tokens, head_weights, preferred_element_type=jnp.float32
        ).astype(jnp.bfloat16)
        sending = proj.reshape(seq_count, portion * 2 * depth)
        got = lax.all_to_all(sending, "seq", split_axis=0, concat_axis=0, tiled=True)
        gathered = got.reshape(seq_count * portion, 2 * depth)
    mixed, grad_both = attend_group(gathered, grad_rows, key_blocks[group], key_counts[group])
    back_out, back_grad = (
        lax.all_to_all(
            mixed.reshape(seq_count, portion, depth),
            "seq",
            split_axis=0,
            concat_axis=0,
            tiled=True,
        ),
        lax.all_to_all(
            grad_both.reshape(seq_count, portion, 2 * depth),
            "seq",
            split_axis=0,
            concat_axis=0,
            tiled=True,
        ),
    )
    attention = back_out.reshape(heads, tokens_here, depth)[None]
    grad_proj = back_grad.reshape(heads, tokens_here, 2 * depth)
    seq_grad = jnp.einsum(
        "htc,dhc->td", grad_proj, head_weights, preferred_element_type=jnp.float32
    ).astype(jnp.bfloat16)[None]
    if groups == 1:
        rows_out = width // (rec_count * seq_count)
        head_grad = lax.optimization_barrier(
            lax.dot_general(
                placing, grad_both, (((0,), (0,)), ((), ())), preferred_element_type=jnp.float32
            ).astype(jnp.bfloat16)
        )
        partial = jnp.einsum(
            "od,oc->dc", owned_all, head_grad, preferred_element_type=jnp.float32
        )
        summed = lax.psum_scatter(partial, "rec", scatter_dimension=0, tiled=True)
        spread = lax.all_to_all(
            summed.reshape(seq_count, rows_out, 2 * depth),
            "seq",
            split_axis=0,
            concat_axis=0,
            tiled=True,
        )
        weight_grad = jnp.transpose(spread, (1, 0, 2))
    else:
        weight_grad = lax.psum_scatter(
            jnp.einsum("td,htc->dhc", tokens, grad_proj, preferred_element_type=jnp.float32),
            ("rec", "seq"),
            scatter_dimension=0,
            tiled=True,
        )
    return (attention, seq_grad, weight_grad)


def solution(mesh):
    placed = (P("rec", "seq", None), P("rec", "seq"), P(), P(), P(), P("rec", None, "seq", None))
    return jax.shard_map(
        local,
        mesh=mesh,
        in_specs=placed,
        out_specs=(
            P("rec", None, "seq", None),
            P("rec", "seq", None),
            P(("rec", "seq"), None, None),
        ),
        check_vma=False,
    )
```

```python
import functools

import jax
import jax.numpy as jnp
from jax import lax
from jax.sharding import PartitionSpec as P
from jax.experimental import pallas as pl
from jax.experimental.pallas import tpu as pltpu

BLOCK = 128


def attention_kernel(lists_ref, counts_ref, both_ref, grad_ref, out_ref, back_ref, acc_ref):
    nblocks, listed = lists_ref.shape
    depth = grad_ref.shape[1]
    scale = depth ** (-0.5)
    acc_ref[...] = jnp.zeros(acc_ref.shape, jnp.float32)
    trans_a = (((0,), (0,)), ((), ()))
    trans_b = (((1,), (1,)), ((), ()))

    def attend(a, used):
        start = pl.multiple_of(a * BLOCK, BLOCK)
        query = both_ref[pl.ds(start, BLOCK), :][:, :depth]
        upstream = grad_ref[pl.ds(start, BLOCK), :]
        picks = [jnp.clip(lists_ref[a, j], 0, nblocks - 1) for j in range(used)]
        tiles = [both_ref[pl.ds(pl.multiple_of(b * BLOCK, BLOCK), BLOCK), :] for b in picks]
        near = tiles[0] if used == 1 else jnp.concatenate(tiles, axis=0)
        keys = near[:, :depth]
        values = near[:, depth:]
        scores = lax.dot_general(query, keys, trans_b, preferred_element_type=jnp.float32) * scale
        peak = jnp.max(scores, axis=1, keepdims=True)
        weights = jnp.exp(scores - peak)
        probs = weights / jnp.sum(weights, axis=1, keepdims=True)
        probs_low = probs.astype(jnp.bfloat16)
        mixed = jnp.dot(probs_low, values, preferred_element_type=jnp.float32)
        out_ref[pl.ds(start, BLOCK), :] = mixed.astype(out_ref.dtype)
        dprobs = lax.dot_general(upstream, values, trans_b, preferred_element_type=jnp.float32)
        inner = jnp.sum(probs * dprobs, axis=1, keepdims=True)
        dscores = (scale * probs * (dprobs - inner)).astype(jnp.bfloat16)
        dquery = jnp.dot(dscores, keys, preferred_element_type=jnp.float32)
        dkeys = lax.dot_general(dscores, query, trans_a, preferred_element_type=jnp.float32)
        dvalues = lax.dot_general(probs_low, upstream, trans_a, preferred_element_type=jnp.float32)
        both_grads = jnp.concatenate([dkeys, dvalues], axis=1)
        for j in range(used):
            part = both_grads[j * BLOCK:(j + 1) * BLOCK]
            if j == 0:
                part = part + jnp.concatenate([dquery, jnp.zeros_like(dquery)], axis=1)
            rows = pl.ds(pl.multiple_of(picks[j] * BLOCK, BLOCK), BLOCK)
            acc_ref[rows, :] += part

    def one_block(a, carry):
        active = jnp.clip(counts_ref[a], 1, listed)
        lax.switch(active - 1, [functools.partial(attend, a, used) for used in range(1, listed + 1)])
        return carry

    lax.fori_loop(0, nblocks, one_block, 0)
    back_ref[...] = acc_ref[...].astype(back_ref.dtype)


def attend_group(both, grad_rows, lists, counts):
    total, width = both.shape
    depth = grad_rows.shape[1]
    smem = pltpu.MemorySpace.SMEM
    vmem = pltpu.MemorySpace.VMEM
    return pl.pallas_call(
        attention_kernel,
        out_shape=(
            jax.ShapeDtypeStruct((total, depth), jnp.bfloat16),
            jax.ShapeDtypeStruct((total, width), jnp.bfloat16),
        ),
        in_specs=[
            pl.BlockSpec(memory_space=smem),
            pl.BlockSpec(memory_space=smem),
            pl.BlockSpec(memory_space=vmem),
            pl.BlockSpec(memory_space=vmem),
        ],
        out_specs=(pl.BlockSpec(memory_space=vmem), pl.BlockSpec(memory_space=vmem)),
        scratch_shapes=[pltpu.VMEM((total, width), jnp.float32)],
    )(lists, counts, both, grad_rows)


def route_tokens(rows_here, targets, seq_count, my_index):
    tokens_here, width = rows_here.shape
    room = 2 * tokens_here // seq_count - 1
    holders = targets // tokens_here
    order_ids = jnp.arange(tokens_here)
    earlier = order_ids[None, :] < order_ids[:, None]
    same_holder = holders[:, None] == holders[None, :]
    ranked = jnp.sum((earlier & same_holder).astype(jnp.int32), axis=1)
    slot_ids = holders * room + ranked
    outgoing = jnp.zeros((seq_count * room, width), rows_here.dtype).at[slot_ids].set(rows_here)
    outgoing = outgoing.reshape(seq_count, room, width)
    labels = (
        jnp.full((seq_count * room,), -1, jnp.int32)
        .at[slot_ids]
        .set(targets)
        .reshape(seq_count, room)
    )
    arrived, arrived_pos = (
        lax.all_to_all(outgoing, "seq", split_axis=0, concat_axis=0, tiled=True),
        lax.all_to_all(labels, "seq", split_axis=0, concat_axis=0, tiled=True),
    )
    local_ids = jnp.where(
        arrived_pos >= 0, arrived_pos - my_index * tokens_here, tokens_here
    ).reshape(-1)
    return (
        jnp.zeros((tokens_here, width), rows_here.dtype)
        .at[local_ids]
        .set(arrived.reshape(-1, width), mode="drop")
    )


def local(owned_rows, seq_position, head_weights, key_blocks, key_counts, out_grad):
    seq_count = lax.axis_size("seq")
    rec_count = lax.axis_size("rec")
    my_index = lax.axis_index("seq")
    tokens_here = owned_rows.shape[1]
    width = owned_rows.shape[2]
    heads = head_weights.shape[1]
    depth = head_weights.shape[2] // 2
    groups = seq_count // heads
    portion = tokens_here // groups
    rows_here = owned_rows[0]
    targets = seq_position[0]
    group = my_index % groups
    upstream = out_grad[0].reshape(seq_count, portion, depth)
    got_grad = lax.all_to_all(upstream, "seq", split_axis=0, concat_axis=0, tiled=True)
    grad_rows = got_grad.reshape(seq_count * portion, depth)
    if groups == 1:
        places_all = lax.all_to_all(
            jnp.broadcast_to(targets[None], (seq_count, tokens_here)),
            "seq",
            split_axis=0,
            concat_axis=0,
            tiled=True,
        ).reshape(-1)
        proj_mine = jnp.einsum(
            "td,dhc->htc", rows_here, head_weights, preferred_element_type=jnp.float32
        ).astype(jnp.bfloat16)
        proj_owned = lax.all_to_all(
            proj_mine, "seq", split_axis=0, concat_axis=0, tiled=True
        ).reshape(seq_count * tokens_here, 2 * depth)
        later_rows, proj_owned, grad_rows = lax.optimization_barrier(
            (rows_here, proj_owned, grad_rows)
        )
        owned_all = lax.all_gather(later_rows, "seq", axis=0, tiled=True)
        slots = jnp.arange(places_all.shape[0], dtype=places_all.dtype)
        placing = (slots[:, None] == places_all[None, :]).astype(jnp.bfloat16)
        gathered = jnp.dot(placing, proj_owned, preferred_element_type=jnp.float32).astype(
            jnp.bfloat16
        )
    else:
        tokens = route_tokens(rows_here, targets, seq_count, my_index)
        proj = jnp.einsum(
            "td,dhc->htc", tokens, head_weights, preferred_element_type=jnp.float32
        ).astype(jnp.bfloat16)
        sending = proj.reshape(seq_count, portion * 2 * depth)
        got = lax.all_to_all(sending, "seq", split_axis=0, concat_axis=0, tiled=True)
        gathered = got.reshape(seq_count * portion, 2 * depth)
    mixed, grad_both = attend_group(gathered, grad_rows, key_blocks[group], key_counts[group])
    back = lax.all_to_all(
        jnp.concatenate([mixed, grad_both], axis=1).reshape(seq_count, portion, 3 * depth),
        "seq",
        split_axis=0,
        concat_axis=0,
        tiled=True,
    )
    back_out = back[:, :, :depth]
    back_grad = back[:, :, depth:]
    attention = back_out.reshape(heads, tokens_here, depth)[None]
    grad_proj = back_grad.reshape(heads, tokens_here, 2 * depth)
    seq_grad = jnp.einsum(
        "htc,dhc->td", grad_proj, head_weights, preferred_element_type=jnp.float32
    ).astype(jnp.bfloat16)[None]
    if groups == 1:
        rows_out = width // (rec_count * seq_count)
        head_grad = lax.optimization_barrier(
            lax.dot_general(
                placing, grad_both, (((0,), (0,)), ((), ())), preferred_element_type=jnp.float32
            ).astype(jnp.bfloat16)
        )
        partial = jnp.einsum(
            "od,oc->dc", owned_all, head_grad, preferred_element_type=jnp.float32
        )
        pieces = lax.all_to_all(
            partial.reshape(rec_count, width // rec_count, 2 * depth),
            "rec",
            split_axis=0,
            concat_axis=0,
            tiled=True,
        )
        summed = jnp.sum(pieces, axis=0)
        spread = lax.all_to_all(
            summed.reshape(seq_count, rows_out, 2 * depth),
            "seq",
            split_axis=0,
            concat_axis=0,
            tiled=True,
        )
        weight_grad = jnp.transpose(spread, (1, 0, 2))
    else:
        weight_grad = lax.psum_scatter(
            jnp.einsum("td,htc->dhc", tokens, grad_proj, preferred_element_type=jnp.float32),
            ("rec", "seq"),
            scatter_dimension=0,
            tiled=True,
        )
    return (attention, seq_grad, weight_grad)


def solution(mesh):
    placed = (P("rec", "seq", None), P("rec", "seq"), P(), P(), P(), P("rec", None, "seq", None))
    return jax.shard_map(
        local,
        mesh=mesh,
        in_specs=placed,
        out_specs=(
            P("rec", None, "seq", None),
            P("rec", "seq", None),
            P(("rec", "seq"), None, None),
        ),
        check_vma=False,
    )
```

```python
import functools

import jax
import jax.numpy as jnp
from jax import lax
from jax.sharding import PartitionSpec as P
from jax.experimental import pallas as pl
from jax.experimental.pallas import tpu as pltpu

BLOCK = 128


def attention_kernel(lists_ref, counts_ref, both_ref, grad_ref, out_ref, back_ref, acc_ref):
    nblocks, listed = lists_ref.shape
    depth = grad_ref.shape[1]
    scale = depth ** (-0.5)
    acc_ref[...] = jnp.zeros(acc_ref.shape, jnp.float32)
    trans_a = (((0,), (0,)), ((), ()))
    trans_b = (((1,), (1,)), ((), ()))

    def attend(a, used):
        start = pl.multiple_of(a * BLOCK, BLOCK)
        query = both_ref[pl.ds(start, BLOCK), :][:, :depth]
        upstream = grad_ref[pl.ds(start, BLOCK), :]
        picks = [jnp.clip(lists_ref[a, j], 0, nblocks - 1) for j in range(used)]
        tiles = [both_ref[pl.ds(pl.multiple_of(b * BLOCK, BLOCK), BLOCK), :] for b in picks]
        near = tiles[0] if used == 1 else jnp.concatenate(tiles, axis=0)
        keys = near[:, :depth]
        values = near[:, depth:]
        scores = lax.dot_general(query, keys, trans_b, preferred_element_type=jnp.float32) * scale
        peak = jnp.max(scores, axis=1, keepdims=True)
        weights = jnp.exp(scores - peak)
        probs = weights / jnp.sum(weights, axis=1, keepdims=True)
        probs_low = probs.astype(jnp.bfloat16)
        mixed = jnp.dot(probs_low, values, preferred_element_type=jnp.float32)
        out_ref[pl.ds(start, BLOCK), :] = mixed.astype(out_ref.dtype)
        dprobs = lax.dot_general(upstream, values, trans_b, preferred_element_type=jnp.float32)
        inner = jnp.sum(probs * dprobs, axis=1, keepdims=True)
        dscores = (scale * probs * (dprobs - inner)).astype(jnp.bfloat16)
        dquery = jnp.dot(dscores, keys, preferred_element_type=jnp.float32)
        dkeys = lax.dot_general(dscores, query, trans_a, preferred_element_type=jnp.float32)
        dvalues = lax.dot_general(probs_low, upstream, trans_a, preferred_element_type=jnp.float32)
        both_grads = jnp.concatenate([dkeys, dvalues], axis=1)
        for j in range(used):
            part = both_grads[j * BLOCK:(j + 1) * BLOCK]
            if j == 0:
                part = part + jnp.concatenate([dquery, jnp.zeros_like(dquery)], axis=1)
            rows = pl.ds(pl.multiple_of(picks[j] * BLOCK, BLOCK), BLOCK)
            acc_ref[rows, :] += part

    def one_block(a, carry):
        active = jnp.clip(counts_ref[a], 1, listed)
        lax.switch(active - 1, [functools.partial(attend, a, used) for used in range(1, listed + 1)])
        return carry

    lax.fori_loop(0, nblocks, one_block, 0)
    back_ref[...] = acc_ref[...].astype(back_ref.dtype)


def attend_group(both, grad_rows, lists, counts):
    total, width = both.shape
    depth = grad_rows.shape[1]
    smem = pltpu.MemorySpace.SMEM
    vmem = pltpu.MemorySpace.VMEM
    return pl.pallas_call(
        attention_kernel,
        out_shape=(
            jax.ShapeDtypeStruct((total, depth), jnp.bfloat16),
            jax.ShapeDtypeStruct((total, width), jnp.bfloat16),
        ),
        in_specs=[
            pl.BlockSpec(memory_space=smem),
            pl.BlockSpec(memory_space=smem),
            pl.BlockSpec(memory_space=vmem),
            pl.BlockSpec(memory_space=vmem),
        ],
        out_specs=(pl.BlockSpec(memory_space=vmem), pl.BlockSpec(memory_space=vmem)),
        scratch_shapes=[pltpu.VMEM((total, width), jnp.float32)],
    )(lists, counts, both, grad_rows)


def route_tokens(rows_here, targets, seq_count, my_index):
    tokens_here, width = rows_here.shape
    room = 2 * tokens_here // seq_count - 1
    holders = targets // tokens_here
    order_ids = jnp.arange(tokens_here)
    earlier = order_ids[None, :] < order_ids[:, None]
    same_holder = holders[:, None] == holders[None, :]
    ranked = jnp.sum((earlier & same_holder).astype(jnp.int32), axis=1)
    slot_ids = holders * room + ranked
    outgoing = jnp.zeros((seq_count * room, width), rows_here.dtype).at[slot_ids].set(rows_here)
    outgoing = outgoing.reshape(seq_count, room, width)
    labels = (
        jnp.full((seq_count * room,), -1, jnp.int32)
        .at[slot_ids]
        .set(targets)
        .reshape(seq_count, room)
    )
    arrived, arrived_pos = (
        lax.all_to_all(outgoing, "seq", split_axis=0, concat_axis=0, tiled=True),
        lax.all_to_all(labels, "seq", split_axis=0, concat_axis=0, tiled=True),
    )
    local_ids = jnp.where(
        arrived_pos >= 0, arrived_pos - my_index * tokens_here, tokens_here
    ).reshape(-1)
    return (
        jnp.zeros((tokens_here, width), rows_here.dtype)
        .at[local_ids]
        .set(arrived.reshape(-1, width), mode="drop")
    )


def local(owned_rows, seq_position, head_weights, key_blocks, key_counts, out_grad):
    seq_count = lax.axis_size("seq")
    rec_count = lax.axis_size("rec")
    my_index = lax.axis_index("seq")
    tokens_here = owned_rows.shape[1]
    width = owned_rows.shape[2]
    heads = head_weights.shape[1]
    depth = head_weights.shape[2] // 2
    groups = seq_count // heads
    portion = tokens_here // groups
    rows_here = owned_rows[0]
    targets = seq_position[0]
    group = my_index % groups
    upstream = out_grad[0].reshape(seq_count, portion, depth)
    if groups == 1:
        extra = ((2 * tokens_here + depth - 1) // depth + 15) // 16 * 16
        coded = jnp.concatenate([targets // 256, targets % 256]).astype(jnp.bfloat16)
        coded = jnp.pad(coded, (0, extra * depth - coded.shape[0])).reshape(extra, depth)
        sent = jnp.concatenate(
            [upstream, jnp.broadcast_to(coded[None], (seq_count, extra, depth))], axis=1
        )
        got_both = lax.all_to_all(sent, "seq", split_axis=0, concat_axis=0, tiled=True)
        grad_rows = got_both[:, :portion].reshape(seq_count * portion, depth)
        codes = got_both[:, portion:].reshape(seq_count, extra * depth).astype(jnp.float32)
        places_all = (
            codes[:, :tokens_here] * 256 + codes[:, tokens_here : 2 * tokens_here]
        ).astype(jnp.int32).reshape(-1)
        proj_mine = jnp.einsum(
            "td,dhc->htc", rows_here, head_weights, preferred_element_type=jnp.float32
        ).astype(jnp.bfloat16)
        proj_owned = lax.all_to_all(
            proj_mine, "seq", split_axis=0, concat_axis=0, tiled=True
        ).reshape(seq_count * tokens_here, 2 * depth)
        later_rows, proj_owned, grad_rows = lax.optimization_barrier(
            (rows_here, proj_owned, grad_rows)
        )
        owned_all = lax.all_gather(later_rows, "seq", axis=0, tiled=True)
        slots = jnp.arange(places_all.shape[0], dtype=places_all.dtype)
        placing = (slots[:, None] == places_all[None, :]).astype(jnp.bfloat16)
        gathered = jnp.dot(placing, proj_owned, preferred_element_type=jnp.float32).astype(
            jnp.bfloat16
        )
    else:
        got_grad = lax.all_to_all(upstream, "seq", split_axis=0, concat_axis=0, tiled=True)
        grad_rows = got_grad.reshape(seq_count * portion, depth)
        tokens = route_tokens(rows_here, targets, seq_count, my_index)
        proj = jnp.einsum(
            "td,dhc->htc", tokens, head_weights, preferred_element_type=jnp.float32
        ).astype(jnp.bfloat16)
        sending = proj.reshape(seq_count, portion * 2 * depth)
        got = lax.all_to_all(sending, "seq", split_axis=0, concat_axis=0, tiled=True)
        gathered = got.reshape(seq_count * portion, 2 * depth)
    mixed, grad_both = attend_group(gathered, grad_rows, key_blocks[group], key_counts[group])
    back = lax.all_to_all(
        jnp.concatenate([mixed, grad_both], axis=1).reshape(seq_count, portion, 3 * depth),
        "seq",
        split_axis=0,
        concat_axis=0,
        tiled=True,
    )
    back_out = back[:, :, :depth]
    back_grad = back[:, :, depth:]
    attention = back_out.reshape(heads, tokens_here, depth)[None]
    grad_proj = back_grad.reshape(heads, tokens_here, 2 * depth)
    seq_grad = jnp.einsum(
        "htc,dhc->td", grad_proj, head_weights, preferred_element_type=jnp.float32
    ).astype(jnp.bfloat16)[None]
    if groups == 1:
        rows_out = width // (rec_count * seq_count)
        head_grad = lax.optimization_barrier(
            lax.dot_general(
                placing, grad_both, (((0,), (0,)), ((), ())), preferred_element_type=jnp.float32
            ).astype(jnp.bfloat16)
        )
        partial = jnp.einsum(
            "od,oc->dc", owned_all, head_grad, preferred_element_type=jnp.float32
        )
        pieces = lax.all_to_all(
            partial.reshape(rec_count, width // rec_count, 2 * depth),
            "rec",
            split_axis=0,
            concat_axis=0,
            tiled=True,
        )
        summed = jnp.sum(pieces, axis=0)
        spread = lax.all_to_all(
            summed.reshape(seq_count, rows_out, 2 * depth),
            "seq",
            split_axis=0,
            concat_axis=0,
            tiled=True,
        )
        weight_grad = jnp.transpose(spread, (1, 0, 2))
    else:
        weight_grad = lax.psum_scatter(
            jnp.einsum("td,htc->dhc", tokens, grad_proj, preferred_element_type=jnp.float32),
            ("rec", "seq"),
            scatter_dimension=0,
            tiled=True,
        )
    return (attention, seq_grad, weight_grad)


def solution(mesh):
    placed = (P("rec", "seq", None), P("rec", "seq"), P(), P(), P(), P("rec", None, "seq", None))
    return jax.shard_map(
        local,
        mesh=mesh,
        in_specs=placed,
        out_specs=(
            P("rec", None, "seq", None),
            P("rec", "seq", None),
            P(("rec", "seq"), None, None),
        ),
        check_vma=False,
    )
```

```python
import functools

import jax
import jax.numpy as jnp
from jax import lax
from jax.sharding import PartitionSpec as P
from jax.experimental import pallas as pl
from jax.experimental.pallas import tpu as pltpu

BLOCK = 128


def attention_kernel(lists_ref, counts_ref, both_ref, grad_ref, out_ref, back_ref, acc_ref):
    nblocks, listed = lists_ref.shape
    depth = grad_ref.shape[1]
    scale = depth ** (-0.5)
    acc_ref[...] = jnp.zeros(acc_ref.shape, jnp.float32)
    trans_a = (((0,), (0,)), ((), ()))
    trans_b = (((1,), (1,)), ((), ()))

    def attend(a, used):
        start = pl.multiple_of(a * BLOCK, BLOCK)
        query = both_ref[pl.ds(start, BLOCK), :][:, :depth]
        upstream = grad_ref[pl.ds(start, BLOCK), :]
        picks = [jnp.clip(lists_ref[a, j], 0, nblocks - 1) for j in range(used)]
        tiles = [both_ref[pl.ds(pl.multiple_of(b * BLOCK, BLOCK), BLOCK), :] for b in picks]
        near = tiles[0] if used == 1 else jnp.concatenate(tiles, axis=0)
        keys = near[:, :depth]
        values = near[:, depth:]
        scores = lax.dot_general(query, keys, trans_b, preferred_element_type=jnp.float32) * scale
        peak = jnp.max(scores, axis=1, keepdims=True)
        weights = jnp.exp(scores - peak)
        probs = weights / jnp.sum(weights, axis=1, keepdims=True)
        probs_low = probs.astype(jnp.bfloat16)
        mixed = jnp.dot(probs_low, values, preferred_element_type=jnp.float32)
        out_ref[pl.ds(start, BLOCK), :] = mixed.astype(out_ref.dtype)
        dprobs = lax.dot_general(upstream, values, trans_b, preferred_element_type=jnp.float32)
        inner = jnp.sum(probs * dprobs, axis=1, keepdims=True)
        dscores = (scale * probs * (dprobs - inner)).astype(jnp.bfloat16)
        dquery = jnp.dot(dscores, keys, preferred_element_type=jnp.float32)
        dkeys = lax.dot_general(dscores, query, trans_a, preferred_element_type=jnp.float32)
        dvalues = lax.dot_general(probs_low, upstream, trans_a, preferred_element_type=jnp.float32)
        both_grads = jnp.concatenate([dkeys, dvalues], axis=1)
        for j in range(used):
            part = both_grads[j * BLOCK:(j + 1) * BLOCK]
            if j == 0:
                part = part + jnp.concatenate([dquery, jnp.zeros_like(dquery)], axis=1)
            rows = pl.ds(pl.multiple_of(picks[j] * BLOCK, BLOCK), BLOCK)
            acc_ref[rows, :] += part

    def one_block(a, carry):
        active = jnp.clip(counts_ref[a], 1, listed)
        lax.switch(active - 1, [functools.partial(attend, a, used) for used in range(1, listed + 1)])
        return carry

    lax.fori_loop(0, nblocks, one_block, 0)
    back_ref[...] = acc_ref[...].astype(back_ref.dtype)


def attend_group(both, grad_rows, lists, counts):
    total, width = both.shape
    depth = grad_rows.shape[1]
    smem = pltpu.MemorySpace.SMEM
    vmem = pltpu.MemorySpace.VMEM
    return pl.pallas_call(
        attention_kernel,
        out_shape=(
            jax.ShapeDtypeStruct((total, depth), jnp.bfloat16),
            jax.ShapeDtypeStruct((total, width), jnp.bfloat16),
        ),
        in_specs=[
            pl.BlockSpec(memory_space=smem),
            pl.BlockSpec(memory_space=smem),
            pl.BlockSpec(memory_space=vmem),
            pl.BlockSpec(memory_space=vmem),
        ],
        out_specs=(pl.BlockSpec(memory_space=vmem), pl.BlockSpec(memory_space=vmem)),
        scratch_shapes=[pltpu.VMEM((total, width), jnp.float32)],
    )(lists, counts, both, grad_rows)


def route_tokens(rows_here, targets, seq_count, my_index):
    tokens_here, width = rows_here.shape
    room = 2 * tokens_here // seq_count - 1
    holders = targets // tokens_here
    order_ids = jnp.arange(tokens_here)
    earlier = order_ids[None, :] < order_ids[:, None]
    same_holder = holders[:, None] == holders[None, :]
    ranked = jnp.sum((earlier & same_holder).astype(jnp.int32), axis=1)
    slot_ids = holders * room + ranked
    outgoing = jnp.zeros((seq_count * room, width), rows_here.dtype).at[slot_ids].set(rows_here)
    outgoing = outgoing.reshape(seq_count, room, width)
    labels = (
        jnp.full((seq_count * room,), -1, jnp.int32)
        .at[slot_ids]
        .set(targets)
        .reshape(seq_count, room)
    )
    arrived, arrived_pos = (
        lax.all_to_all(outgoing, "seq", split_axis=0, concat_axis=0, tiled=True),
        lax.all_to_all(labels, "seq", split_axis=0, concat_axis=0, tiled=True),
    )
    local_ids = jnp.where(
        arrived_pos >= 0, arrived_pos - my_index * tokens_here, tokens_here
    ).reshape(-1)
    return (
        jnp.zeros((tokens_here, width), rows_here.dtype)
        .at[local_ids]
        .set(arrived.reshape(-1, width), mode="drop")
    )


def local(owned_rows, seq_position, head_weights, key_blocks, key_counts, out_grad):
    seq_count = lax.axis_size("seq")
    rec_count = lax.axis_size("rec")
    my_index = lax.axis_index("seq")
    tokens_here = owned_rows.shape[1]
    width = owned_rows.shape[2]
    heads = head_weights.shape[1]
    depth = head_weights.shape[2] // 2
    groups = seq_count // heads
    portion = tokens_here // groups
    rows_here = owned_rows[0]
    targets = seq_position[0]
    group = my_index % groups
    upstream = out_grad[0].reshape(seq_count, portion, depth)
    got_grad = lax.all_to_all(upstream, "seq", split_axis=0, concat_axis=0, tiled=True)
    grad_rows = got_grad.reshape(seq_count * portion, depth)
    if groups == 1:
        places_all = lax.all_to_all(
            jnp.broadcast_to(targets[None], (seq_count, tokens_here)),
            "seq",
            split_axis=0,
            concat_axis=0,
            tiled=True,
        ).reshape(-1)
        proj_mine = jnp.einsum(
            "td,dhc->htc", rows_here, head_weights, preferred_element_type=jnp.float32
        ).astype(jnp.bfloat16)
        proj_owned = lax.all_to_all(
            proj_mine, "seq", split_axis=0, concat_axis=0, tiled=True
        ).reshape(seq_count * tokens_here, 2 * depth)
        later_rows, proj_owned, grad_rows = lax.optimization_barrier(
            (rows_here, proj_owned, grad_rows)
        )
        owned_all = lax.all_gather(later_rows, "seq", axis=0, tiled=True)
        slots = jnp.arange(places_all.shape[0], dtype=places_all.dtype)
        placing = (slots[:, None] == places_all[None, :]).astype(jnp.bfloat16)
        gathered = jnp.dot(placing, proj_owned, preferred_element_type=jnp.float32).astype(
            jnp.bfloat16
        )
    else:
        tokens = route_tokens(rows_here, targets, seq_count, my_index)
        proj = jnp.einsum(
            "td,dhc->htc", tokens, head_weights, preferred_element_type=jnp.float32
        ).astype(jnp.bfloat16)
        sending = proj.reshape(seq_count, portion * 2 * depth)
        got = lax.all_to_all(sending, "seq", split_axis=0, concat_axis=0, tiled=True)
        gathered = got.reshape(seq_count * portion, 2 * depth)
    mixed, grad_both = attend_group(gathered, grad_rows, key_blocks[group], key_counts[group])
    back = lax.all_to_all(
        jnp.concatenate([mixed, grad_both], axis=1).reshape(seq_count, portion, 3 * depth),
        "seq",
        split_axis=0,
        concat_axis=0,
        tiled=True,
    )
    back_out = back[:, :, :depth]
    back_grad = back[:, :, depth:]
    attention = back_out.reshape(heads, tokens_here, depth)[None]
    grad_proj = back_grad.reshape(heads, tokens_here, 2 * depth)
    seq_grad = jnp.einsum(
        "htc,dhc->td", grad_proj, head_weights, preferred_element_type=jnp.float32
    ).astype(jnp.bfloat16)[None]
    if groups == 1:
        rows_out = width // (rec_count * seq_count)
        head_grad = lax.optimization_barrier(
            lax.dot_general(
                placing, grad_both, (((0,), (0,)), ((), ())), preferred_element_type=jnp.float32
            ).astype(jnp.bfloat16)
        )
        partial = jnp.einsum(
            "od,oc->dc", owned_all, head_grad, preferred_element_type=jnp.float32
        )
        pieces = lax.all_to_all(
            partial.reshape(rec_count * seq_count, rows_out, 2 * depth),
            ("rec", "seq"),
            split_axis=0,
            concat_axis=0,
            tiled=True,
        )
        summed = jnp.sum(pieces.reshape(rec_count, heads, rows_out, 2 * depth), axis=0)
        weight_grad = jnp.transpose(summed, (1, 0, 2))
    else:
        weight_grad = lax.psum_scatter(
            jnp.einsum("td,htc->dhc", tokens, grad_proj, preferred_element_type=jnp.float32),
            ("rec", "seq"),
            scatter_dimension=0,
            tiled=True,
        )
    return (attention, seq_grad, weight_grad)


def solution(mesh):
    placed = (P("rec", "seq", None), P("rec", "seq"), P(), P(), P(), P("rec", None, "seq", None))
    return jax.shard_map(
        local,
        mesh=mesh,
        in_specs=placed,
        out_specs=(
            P("rec", None, "seq", None),
            P("rec", "seq", None),
            P(("rec", "seq"), None, None),
        ),
        check_vma=False,
    )
```

```python
import functools

import jax
import jax.numpy as jnp
from jax import lax
from jax.sharding import PartitionSpec as P
from jax.experimental import pallas as pl
from jax.experimental.pallas import tpu as pltpu

BLOCK = 128


def attention_kernel(lists_ref, counts_ref, both_ref, grad_ref, out_ref, back_ref, acc_ref):
    nblocks, listed = lists_ref.shape
    depth = grad_ref.shape[1]
    scale = depth ** (-0.5)
    acc_ref[...] = jnp.zeros(acc_ref.shape, jnp.float32)
    trans_a = (((0,), (0,)), ((), ()))
    trans_b = (((1,), (1,)), ((), ()))

    def attend(a, used):
        start = pl.multiple_of(a * BLOCK, BLOCK)
        query = both_ref[pl.ds(start, BLOCK), :][:, :depth]
        upstream = grad_ref[pl.ds(start, BLOCK), :]
        picks = [jnp.clip(lists_ref[a, j], 0, nblocks - 1) for j in range(used)]
        tiles = [both_ref[pl.ds(pl.multiple_of(b * BLOCK, BLOCK), BLOCK), :] for b in picks]
        near = tiles[0] if used == 1 else jnp.concatenate(tiles, axis=0)
        keys = near[:, :depth]
        values = near[:, depth:]
        scores = lax.dot_general(query, keys, trans_b, preferred_element_type=jnp.float32) * scale
        peak = jnp.max(scores, axis=1, keepdims=True)
        weights = jnp.exp(scores - peak)
        probs = weights / jnp.sum(weights, axis=1, keepdims=True)
        probs_low = probs.astype(jnp.bfloat16)
        mixed = jnp.dot(probs_low, values, preferred_element_type=jnp.float32)
        out_ref[pl.ds(start, BLOCK), :] = mixed.astype(out_ref.dtype)
        dprobs = lax.dot_general(upstream, values, trans_b, preferred_element_type=jnp.float32)
        inner = jnp.sum(probs * dprobs, axis=1, keepdims=True)
        dscores = (scale * probs * (dprobs - inner)).astype(jnp.bfloat16)
        dquery = jnp.dot(dscores, keys, preferred_element_type=jnp.float32)
        dkeys = lax.dot_general(dscores, query, trans_a, preferred_element_type=jnp.float32)
        dvalues = lax.dot_general(probs_low, upstream, trans_a, preferred_element_type=jnp.float32)
        both_grads = jnp.concatenate([dkeys, dvalues], axis=1)
        for j in range(used):
            part = both_grads[j * BLOCK:(j + 1) * BLOCK]
            if j == 0:
                part = part + jnp.concatenate([dquery, jnp.zeros_like(dquery)], axis=1)
            rows = pl.ds(pl.multiple_of(picks[j] * BLOCK, BLOCK), BLOCK)
            acc_ref[rows, :] += part

    def one_block(a, carry):
        active = jnp.clip(counts_ref[a], 1, listed)
        lax.switch(active - 1, [functools.partial(attend, a, used) for used in range(1, listed + 1)])
        return carry

    lax.fori_loop(0, nblocks, one_block, 0)
    back_ref[...] = acc_ref[...].astype(back_ref.dtype)


def attend_group(both, grad_rows, lists, counts):
    total, width = both.shape
    depth = grad_rows.shape[1]
    smem = pltpu.MemorySpace.SMEM
    vmem = pltpu.MemorySpace.VMEM
    return pl.pallas_call(
        attention_kernel,
        out_shape=(
            jax.ShapeDtypeStruct((total, depth), jnp.bfloat16),
            jax.ShapeDtypeStruct((total, width), jnp.bfloat16),
        ),
        in_specs=[
            pl.BlockSpec(memory_space=smem),
            pl.BlockSpec(memory_space=smem),
            pl.BlockSpec(memory_space=vmem),
            pl.BlockSpec(memory_space=vmem),
        ],
        out_specs=(pl.BlockSpec(memory_space=vmem), pl.BlockSpec(memory_space=vmem)),
        scratch_shapes=[pltpu.VMEM((total, width), jnp.float32)],
    )(lists, counts, both, grad_rows)


def route_tokens(rows_here, targets, seq_count, my_index):
    tokens_here, width = rows_here.shape
    room = 2 * tokens_here // seq_count - 1
    holders = targets // tokens_here
    order_ids = jnp.arange(tokens_here)
    earlier = order_ids[None, :] < order_ids[:, None]
    same_holder = holders[:, None] == holders[None, :]
    ranked = jnp.sum((earlier & same_holder).astype(jnp.int32), axis=1)
    slot_ids = holders * room + ranked
    outgoing = jnp.zeros((seq_count * room, width), rows_here.dtype).at[slot_ids].set(rows_here)
    outgoing = outgoing.reshape(seq_count, room, width)
    labels = (
        jnp.full((seq_count * room,), -1, jnp.int32)
        .at[slot_ids]
        .set(targets)
        .reshape(seq_count, room)
    )
    arrived, arrived_pos = (
        lax.all_to_all(outgoing, "seq", split_axis=0, concat_axis=0, tiled=True),
        lax.all_to_all(labels, "seq", split_axis=0, concat_axis=0, tiled=True),
    )
    local_ids = jnp.where(
        arrived_pos >= 0, arrived_pos - my_index * tokens_here, tokens_here
    ).reshape(-1)
    return (
        jnp.zeros((tokens_here, width), rows_here.dtype)
        .at[local_ids]
        .set(arrived.reshape(-1, width), mode="drop")
    )


def gather_pairs(rows, seq_count, my_index):
    if seq_count % 2:
        return lax.all_gather(rows, "seq", axis=0, tiled=True)
    chips = seq_count // 2
    core = my_index % 2
    chip = my_index // 2
    half = rows.shape[1] // 2
    swap = [(i, i ^ 1) for i in range(seq_count)]
    sibling = lax.ppermute(rows, "seq", swap)
    pair = jnp.where(core == 0, jnp.stack([rows, sibling]), jnp.stack([sibling, rows]))
    mine = lax.dynamic_slice_in_dim(pair, core * half, half, axis=2)
    held = [mine]
    for shift in range(1, chips):
        ring = [(i, (i + 2 * shift) % seq_count) for i in range(seq_count)]
        held.append(lax.ppermute(mine, "seq", ring))
    held = jnp.stack(held)
    order = (chip - jnp.arange(chips)) % chips
    cols = jnp.take(held, order, axis=0).reshape(-1, half)
    other = lax.ppermute(cols, "seq", swap)
    return jnp.where(
        core == 0,
        jnp.concatenate([cols, other], axis=1),
        jnp.concatenate([other, cols], axis=1),
    )


def local(owned_rows, seq_position, head_weights, key_blocks, key_counts, out_grad):
    seq_count = lax.axis_size("seq")
    rec_count = lax.axis_size("rec")
    my_index = lax.axis_index("seq")
    tokens_here = owned_rows.shape[1]
    width = owned_rows.shape[2]
    heads = head_weights.shape[1]
    depth = head_weights.shape[2] // 2
    groups = seq_count // heads
    portion = tokens_here // groups
    rows_here = owned_rows[0]
    targets = seq_position[0]
    group = my_index % groups
    upstream = out_grad[0].reshape(seq_count, portion, depth)
    got_grad = lax.all_to_all(upstream, "seq", split_axis=0, concat_axis=0, tiled=True)
    grad_rows = got_grad.reshape(seq_count * portion, depth)
    if groups == 1:
        places_all = lax.all_to_all(
            jnp.broadcast_to(targets[None], (seq_count, tokens_here)),
            "seq",
            split_axis=0,
            concat_axis=0,
            tiled=True,
        ).reshape(-1)
        proj_mine = jnp.einsum(
            "td,dhc->htc", rows_here, head_weights, preferred_element_type=jnp.float32
        ).astype(jnp.bfloat16)
        proj_owned = lax.all_to_all(
            proj_mine, "seq", split_axis=0, concat_axis=0, tiled=True
        ).reshape(seq_count * tokens_here, 2 * depth)
        later_rows, proj_owned, grad_rows = lax.optimization_barrier(
            (rows_here, proj_owned, grad_rows)
        )
        owned_all = gather_pairs(later_rows, seq_count, my_index)
        slots = jnp.arange(places_all.shape[0], dtype=places_all.dtype)
        placing = (slots[:, None] == places_all[None, :]).astype(jnp.bfloat16)
        gathered = jnp.dot(placing, proj_owned, preferred_element_type=jnp.float32).astype(
            jnp.bfloat16
        )
    else:
        tokens = route_tokens(rows_here, targets, seq_count, my_index)
        proj = jnp.einsum(
            "td,dhc->htc", tokens, head_weights, preferred_element_type=jnp.float32
        ).astype(jnp.bfloat16)
        sending = proj.reshape(seq_count, portion * 2 * depth)
        got = lax.all_to_all(sending, "seq", split_axis=0, concat_axis=0, tiled=True)
        gathered = got.reshape(seq_count * portion, 2 * depth)
    mixed, grad_both = attend_group(gathered, grad_rows, key_blocks[group], key_counts[group])
    back = lax.all_to_all(
        jnp.concatenate([mixed, grad_both], axis=1).reshape(seq_count, portion, 3 * depth),
        "seq",
        split_axis=0,
        concat_axis=0,
        tiled=True,
    )
    back_out = back[:, :, :depth]
    back_grad = back[:, :, depth:]
    attention = back_out.reshape(heads, tokens_here, depth)[None]
    grad_proj = back_grad.reshape(heads, tokens_here, 2 * depth)
    seq_grad = jnp.einsum(
        "htc,dhc->td", grad_proj, head_weights, preferred_element_type=jnp.float32
    ).astype(jnp.bfloat16)[None]
    if groups == 1:
        rows_out = width // (rec_count * seq_count)
        head_grad = lax.optimization_barrier(
            lax.dot_general(
                placing, grad_both, (((0,), (0,)), ((), ())), preferred_element_type=jnp.float32
            ).astype(jnp.bfloat16)
        )
        partial = jnp.einsum(
            "od,oc->dc", owned_all, head_grad, preferred_element_type=jnp.float32
        )
        pieces = lax.all_to_all(
            partial.reshape(rec_count * seq_count, rows_out, 2 * depth),
            ("rec", "seq"),
            split_axis=0,
            concat_axis=0,
            tiled=True,
        )
        summed = jnp.sum(pieces.reshape(rec_count, heads, rows_out, 2 * depth), axis=0)
        weight_grad = jnp.transpose(summed, (1, 0, 2))
    else:
        weight_grad = lax.psum_scatter(
            jnp.einsum("td,htc->dhc", tokens, grad_proj, preferred_element_type=jnp.float32),
            ("rec", "seq"),
            scatter_dimension=0,
            tiled=True,
        )
    return (attention, seq_grad, weight_grad)


def solution(mesh):
    placed = (P("rec", "seq", None), P("rec", "seq"), P(), P(), P(), P("rec", None, "seq", None))
    return jax.shard_map(
        local,
        mesh=mesh,
        in_specs=placed,
        out_specs=(
            P("rec", None, "seq", None),
            P("rec", "seq", None),
            P(("rec", "seq"), None, None),
        ),
        check_vma=False,
    )
```

```python
import functools

import jax
import jax.numpy as jnp
from jax import lax
from jax.sharding import PartitionSpec as P
from jax.experimental import pallas as pl
from jax.experimental.pallas import tpu as pltpu

BLOCK = 128


def attention_kernel(lists_ref, counts_ref, both_ref, grad_ref, out_ref, back_ref, acc_ref):
    nblocks, listed = lists_ref.shape
    depth = grad_ref.shape[1]
    scale = depth ** (-0.5)
    acc_ref[...] = jnp.zeros(acc_ref.shape, jnp.float32)
    trans_a = (((0,), (0,)), ((), ()))
    trans_b = (((1,), (1,)), ((), ()))

    def attend(a, used):
        start = pl.multiple_of(a * BLOCK, BLOCK)
        query = both_ref[pl.ds(start, BLOCK), :][:, :depth]
        upstream = grad_ref[pl.ds(start, BLOCK), :]
        picks = [jnp.clip(lists_ref[a, j], 0, nblocks - 1) for j in range(used)]
        tiles = [both_ref[pl.ds(pl.multiple_of(b * BLOCK, BLOCK), BLOCK), :] for b in picks]
        near = tiles[0] if used == 1 else jnp.concatenate(tiles, axis=0)
        keys = near[:, :depth]
        values = near[:, depth:]
        scores = lax.dot_general(query, keys, trans_b, preferred_element_type=jnp.float32) * scale
        peak = jnp.max(scores, axis=1, keepdims=True)
        weights = jnp.exp(scores - peak)
        probs = weights / jnp.sum(weights, axis=1, keepdims=True)
        probs_low = probs.astype(jnp.bfloat16)
        mixed = jnp.dot(probs_low, values, preferred_element_type=jnp.float32)
        out_ref[pl.ds(start, BLOCK), :] = mixed.astype(out_ref.dtype)
        dprobs = lax.dot_general(upstream, values, trans_b, preferred_element_type=jnp.float32)
        inner = jnp.sum(probs * dprobs, axis=1, keepdims=True)
        dscores = (scale * probs * (dprobs - inner)).astype(jnp.bfloat16)
        dquery = jnp.dot(dscores, keys, preferred_element_type=jnp.float32)
        dkeys = lax.dot_general(dscores, query, trans_a, preferred_element_type=jnp.float32)
        dvalues = lax.dot_general(probs_low, upstream, trans_a, preferred_element_type=jnp.float32)
        both_grads = jnp.concatenate([dkeys, dvalues], axis=1)
        for j in range(used):
            part = both_grads[j * BLOCK:(j + 1) * BLOCK]
            if j == 0:
                part = part + jnp.concatenate([dquery, jnp.zeros_like(dquery)], axis=1)
            rows = pl.ds(pl.multiple_of(picks[j] * BLOCK, BLOCK), BLOCK)
            acc_ref[rows, :] += part

    def one_block(a, carry):
        active = jnp.clip(counts_ref[a], 1, listed)
        lax.switch(active - 1, [functools.partial(attend, a, used) for used in range(1, listed + 1)])
        return carry

    lax.fori_loop(0, nblocks, one_block, 0)
    back_ref[...] = acc_ref[...].astype(back_ref.dtype)


def attend_group(both, grad_rows, lists, counts):
    total, width = both.shape
    depth = grad_rows.shape[1]
    smem = pltpu.MemorySpace.SMEM
    vmem = pltpu.MemorySpace.VMEM
    return pl.pallas_call(
        attention_kernel,
        out_shape=(
            jax.ShapeDtypeStruct((total, depth), jnp.bfloat16),
            jax.ShapeDtypeStruct((total, width), jnp.bfloat16),
        ),
        in_specs=[
            pl.BlockSpec(memory_space=smem),
            pl.BlockSpec(memory_space=smem),
            pl.BlockSpec(memory_space=vmem),
            pl.BlockSpec(memory_space=vmem),
        ],
        out_specs=(pl.BlockSpec(memory_space=vmem), pl.BlockSpec(memory_space=vmem)),
        scratch_shapes=[pltpu.VMEM((total, width), jnp.float32)],
    )(lists, counts, both, grad_rows)


def route_tokens(rows_here, targets, seq_count, my_index):
    tokens_here, width = rows_here.shape
    room = 2 * tokens_here // seq_count - 1
    holders = targets // tokens_here
    order_ids = jnp.arange(tokens_here)
    earlier = order_ids[None, :] < order_ids[:, None]
    same_holder = holders[:, None] == holders[None, :]
    ranked = jnp.sum((earlier & same_holder).astype(jnp.int32), axis=1)
    slot_ids = holders * room + ranked
    outgoing = jnp.zeros((seq_count * room, width), rows_here.dtype).at[slot_ids].set(rows_here)
    outgoing = outgoing.reshape(seq_count, room, width)
    labels = (
        jnp.full((seq_count * room,), -1, jnp.int32)
        .at[slot_ids]
        .set(targets)
        .reshape(seq_count, room)
    )
    arrived, arrived_pos = (
        lax.all_to_all(outgoing, "seq", split_axis=0, concat_axis=0, tiled=True),
        lax.all_to_all(labels, "seq", split_axis=0, concat_axis=0, tiled=True),
    )
    local_ids = jnp.where(
        arrived_pos >= 0, arrived_pos - my_index * tokens_here, tokens_here
    ).reshape(-1)
    return (
        jnp.zeros((tokens_here, width), rows_here.dtype)
        .at[local_ids]
        .set(arrived.reshape(-1, width), mode="drop")
    )


def local(owned_rows, seq_position, head_weights, key_blocks, key_counts, out_grad):
    seq_count = lax.axis_size("seq")
    rec_count = lax.axis_size("rec")
    my_index = lax.axis_index("seq")
    tokens_here = owned_rows.shape[1]
    width = owned_rows.shape[2]
    heads = head_weights.shape[1]
    depth = head_weights.shape[2] // 2
    groups = seq_count // heads
    portion = tokens_here // groups
    rows_here = owned_rows[0]
    targets = seq_position[0]
    group = my_index % groups
    upstream = out_grad[0].reshape(seq_count, portion, depth)
    got_grad = lax.all_to_all(upstream, "seq", split_axis=0, concat_axis=0, tiled=True)
    grad_rows = got_grad.reshape(seq_count * portion, depth)
    if groups == 1:
        places_all = lax.all_to_all(
            jnp.broadcast_to(targets[None], (seq_count, tokens_here)),
            "seq",
            split_axis=0,
            concat_axis=0,
            tiled=True,
        ).reshape(-1)
        proj_mine = jnp.einsum(
            "td,dhc->htc", rows_here, head_weights, preferred_element_type=jnp.float32
        ).astype(jnp.bfloat16)
        proj_owned = lax.all_to_all(
            proj_mine, "seq", split_axis=0, concat_axis=0, tiled=True
        ).reshape(seq_count * tokens_here, 2 * depth)
        later_rows, proj_owned, grad_rows = lax.optimization_barrier(
            (rows_here, proj_owned, grad_rows)
        )
        owned_all = lax.all_gather(later_rows, "seq", axis=0, tiled=True)
        slots = jnp.arange(places_all.shape[0], dtype=places_all.dtype)
        placing = (slots[:, None] == places_all[None, :]).astype(jnp.bfloat16)
        gathered = jnp.dot(placing, proj_owned, preferred_element_type=jnp.float32).astype(
            jnp.bfloat16
        )
    else:
        tokens = route_tokens(rows_here, targets, seq_count, my_index)
        proj = jnp.einsum(
            "td,dhc->htc", tokens, head_weights, preferred_element_type=jnp.float32
        ).astype(jnp.bfloat16)
        sending = proj.reshape(seq_count, portion * 2 * depth)
        got = lax.all_to_all(sending, "seq", split_axis=0, concat_axis=0, tiled=True)
        gathered = got.reshape(seq_count * portion, 2 * depth)
    mixed, grad_both = attend_group(gathered, grad_rows, key_blocks[group], key_counts[group])
    leaving = jnp.concatenate([mixed, grad_both], axis=1)
    if groups == 1:
        leaving, owned_all = lax.optimization_barrier((leaving, owned_all))
    back = lax.all_to_all(
        leaving.reshape(seq_count, portion, 3 * depth),
        "seq",
        split_axis=0,
        concat_axis=0,
        tiled=True,
    )
    back_out = back[:, :, :depth]
    back_grad = back[:, :, depth:]
    attention = back_out.reshape(heads, tokens_here, depth)[None]
    grad_proj = back_grad.reshape(heads, tokens_here, 2 * depth)
    seq_grad = jnp.einsum(
        "htc,dhc->td", grad_proj, head_weights, preferred_element_type=jnp.float32
    ).astype(jnp.bfloat16)[None]
    if groups == 1:
        rows_out = width // (rec_count * seq_count)
        head_grad = lax.optimization_barrier(
            lax.dot_general(
                placing, grad_both, (((0,), (0,)), ((), ())), preferred_element_type=jnp.float32
            ).astype(jnp.bfloat16)
        )
        partial = jnp.einsum(
            "od,oc->dc", owned_all, head_grad, preferred_element_type=jnp.float32
        )
        partial, back = lax.optimization_barrier((partial, back))
        pieces = lax.all_to_all(
            partial.reshape(rec_count * seq_count, rows_out, 2 * depth),
            ("rec", "seq"),
            split_axis=0,
            concat_axis=0,
            tiled=True,
        )
        summed = jnp.sum(pieces.reshape(rec_count, heads, rows_out, 2 * depth), axis=0)
        weight_grad = jnp.transpose(summed, (1, 0, 2))
    else:
        weight_grad = lax.psum_scatter(
            jnp.einsum("td,htc->dhc", tokens, grad_proj, preferred_element_type=jnp.float32),
            ("rec", "seq"),
            scatter_dimension=0,
            tiled=True,
        )
    return (attention, seq_grad, weight_grad)


def solution(mesh):
    placed = (P("rec", "seq", None), P("rec", "seq"), P(), P(), P(), P("rec", None, "seq", None))
    return jax.shard_map(
        local,
        mesh=mesh,
        in_specs=placed,
        out_specs=(
            P("rec", None, "seq", None),
            P("rec", "seq", None),
            P(("rec", "seq"), None, None),
        ),
        check_vma=False,
    )
```

```python
import functools

import jax
import jax.numpy as jnp
from jax import lax
from jax.sharding import PartitionSpec as P
from jax.experimental import pallas as pl
from jax.experimental.pallas import tpu as pltpu

BLOCK = 128


def attention_kernel(lists_ref, counts_ref, both_ref, grad_ref, out_ref, acc_ref):
    nblocks, listed = lists_ref.shape
    depth = grad_ref.shape[1]
    scale = depth ** (-0.5)
    acc_ref[...] = jnp.zeros(acc_ref.shape, jnp.float32)
    trans_a = (((0,), (0,)), ((), ()))
    trans_b = (((1,), (1,)), ((), ()))

    def attend(a, used):
        start = pl.multiple_of(a * BLOCK, BLOCK)
        query = both_ref[pl.ds(start, BLOCK), :][:, :depth]
        upstream = grad_ref[pl.ds(start, BLOCK), :]
        picks = [jnp.clip(lists_ref[a, j], 0, nblocks - 1) for j in range(used)]
        tiles = [both_ref[pl.ds(pl.multiple_of(b * BLOCK, BLOCK), BLOCK), :] for b in picks]
        near = tiles[0] if used == 1 else jnp.concatenate(tiles, axis=0)
        keys = near[:, :depth]
        values = near[:, depth:]
        scores = lax.dot_general(query, keys, trans_b, preferred_element_type=jnp.float32) * scale
        peak = jnp.max(scores, axis=1, keepdims=True)
        weights = jnp.exp(scores - peak)
        probs = weights / jnp.sum(weights, axis=1, keepdims=True)
        probs_low = probs.astype(jnp.bfloat16)
        mixed = jnp.dot(probs_low, values, preferred_element_type=jnp.float32)
        out_ref[pl.ds(start, BLOCK), :depth] = mixed.astype(out_ref.dtype)
        dprobs = lax.dot_general(upstream, values, trans_b, preferred_element_type=jnp.float32)
        inner = jnp.sum(probs * dprobs, axis=1, keepdims=True)
        dscores = (scale * probs * (dprobs - inner)).astype(jnp.bfloat16)
        dquery = jnp.dot(dscores, keys, preferred_element_type=jnp.float32)
        dkeys = lax.dot_general(dscores, query, trans_a, preferred_element_type=jnp.float32)
        dvalues = lax.dot_general(probs_low, upstream, trans_a, preferred_element_type=jnp.float32)
        both_grads = jnp.concatenate([dkeys, dvalues], axis=1)
        for j in range(used):
            part = both_grads[j * BLOCK:(j + 1) * BLOCK]
            if j == 0:
                part = part + jnp.concatenate([dquery, jnp.zeros_like(dquery)], axis=1)
            rows = pl.ds(pl.multiple_of(picks[j] * BLOCK, BLOCK), BLOCK)
            acc_ref[rows, :] += part

    def one_block(a, carry):
        active = jnp.clip(counts_ref[a], 1, listed)
        lax.switch(active - 1, [functools.partial(attend, a, used) for used in range(1, listed + 1)])
        return carry

    lax.fori_loop(0, nblocks, one_block, 0)
    out_ref[:, depth:] = acc_ref[...].astype(out_ref.dtype)


def attend_group(both, grad_rows, lists, counts):
    total, width = both.shape
    depth = grad_rows.shape[1]
    smem = pltpu.MemorySpace.SMEM
    vmem = pltpu.MemorySpace.VMEM
    return pl.pallas_call(
        attention_kernel,
        out_shape=jax.ShapeDtypeStruct((total, depth + width), jnp.bfloat16),
        in_specs=[
            pl.BlockSpec(memory_space=smem),
            pl.BlockSpec(memory_space=smem),
            pl.BlockSpec(memory_space=vmem),
            pl.BlockSpec(memory_space=vmem),
        ],
        out_specs=pl.BlockSpec(memory_space=vmem),
        scratch_shapes=[pltpu.VMEM((total, width), jnp.float32)],
    )(lists, counts, both, grad_rows)


def route_tokens(rows_here, targets, seq_count, my_index):
    tokens_here, width = rows_here.shape
    room = 2 * tokens_here // seq_count - 1
    holders = targets // tokens_here
    order_ids = jnp.arange(tokens_here)
    earlier = order_ids[None, :] < order_ids[:, None]
    same_holder = holders[:, None] == holders[None, :]
    ranked = jnp.sum((earlier & same_holder).astype(jnp.int32), axis=1)
    slot_ids = holders * room + ranked
    outgoing = jnp.zeros((seq_count * room, width), rows_here.dtype).at[slot_ids].set(rows_here)
    outgoing = outgoing.reshape(seq_count, room, width)
    labels = (
        jnp.full((seq_count * room,), -1, jnp.int32)
        .at[slot_ids]
        .set(targets)
        .reshape(seq_count, room)
    )
    arrived, arrived_pos = (
        lax.all_to_all(outgoing, "seq", split_axis=0, concat_axis=0, tiled=True),
        lax.all_to_all(labels, "seq", split_axis=0, concat_axis=0, tiled=True),
    )
    local_ids = jnp.where(
        arrived_pos >= 0, arrived_pos - my_index * tokens_here, tokens_here
    ).reshape(-1)
    return (
        jnp.zeros((tokens_here, width), rows_here.dtype)
        .at[local_ids]
        .set(arrived.reshape(-1, width), mode="drop")
    )


def local(owned_rows, seq_position, head_weights, key_blocks, key_counts, out_grad):
    seq_count = lax.axis_size("seq")
    rec_count = lax.axis_size("rec")
    my_index = lax.axis_index("seq")
    tokens_here = owned_rows.shape[1]
    width = owned_rows.shape[2]
    heads = head_weights.shape[1]
    depth = head_weights.shape[2] // 2
    groups = seq_count // heads
    portion = tokens_here // groups
    rows_here = owned_rows[0]
    targets = seq_position[0]
    group = my_index % groups
    upstream = out_grad[0].reshape(seq_count, portion, depth)
    got_grad = lax.all_to_all(upstream, "seq", split_axis=0, concat_axis=0, tiled=True)
    grad_rows = got_grad.reshape(seq_count * portion, depth)
    if groups == 1:
        places_all = lax.all_to_all(
            jnp.broadcast_to(targets[None], (seq_count, tokens_here)),
            "seq",
            split_axis=0,
            concat_axis=0,
            tiled=True,
        ).reshape(-1)
        proj_mine = jnp.einsum(
            "td,dhc->htc", rows_here, head_weights, preferred_element_type=jnp.float32
        ).astype(jnp.bfloat16)
        proj_owned = lax.all_to_all(
            proj_mine, "seq", split_axis=0, concat_axis=0, tiled=True
        ).reshape(seq_count * tokens_here, 2 * depth)
        later_rows, proj_owned, grad_rows = lax.optimization_barrier(
            (rows_here, proj_owned, grad_rows)
        )
        owned_all = lax.all_gather(later_rows, "seq", axis=0, tiled=True)
        slots = jnp.arange(places_all.shape[0], dtype=places_all.dtype)
        placing = (slots[:, None] == places_all[None, :]).astype(jnp.bfloat16)
        gathered = jnp.dot(placing, proj_owned, preferred_element_type=jnp.float32).astype(
            jnp.bfloat16
        )
    else:
        tokens = route_tokens(rows_here, targets, seq_count, my_index)
        proj = jnp.einsum(
            "td,dhc->htc", tokens, head_weights, preferred_element_type=jnp.float32
        ).astype(jnp.bfloat16)
        sending = proj.reshape(seq_count, portion * 2 * depth)
        got = lax.all_to_all(sending, "seq", split_axis=0, concat_axis=0, tiled=True)
        gathered = got.reshape(seq_count * portion, 2 * depth)
    leaving = attend_group(gathered, grad_rows, key_blocks[group], key_counts[group])
    grad_both = leaving[:, depth:]
    back = lax.all_to_all(
        leaving.reshape(seq_count, portion, 3 * depth),
        "seq",
        split_axis=0,
        concat_axis=0,
        tiled=True,
    )
    back_out = back[:, :, :depth]
    back_grad = back[:, :, depth:]
    attention = back_out.reshape(heads, tokens_here, depth)[None]
    grad_proj = back_grad.reshape(heads, tokens_here, 2 * depth)
    seq_grad = jnp.einsum(
        "htc,dhc->td", grad_proj, head_weights, preferred_element_type=jnp.float32
    ).astype(jnp.bfloat16)[None]
    if groups == 1:
        rows_out = width // (rec_count * seq_count)
        head_grad = lax.optimization_barrier(
            lax.dot_general(
                placing, grad_both, (((0,), (0,)), ((), ())), preferred_element_type=jnp.float32
            ).astype(jnp.bfloat16)
        )
        partial = jnp.einsum(
            "od,oc->dc", owned_all, head_grad, preferred_element_type=jnp.float32
        )
        pieces = lax.all_to_all(
            partial.reshape(rec_count * seq_count, rows_out, 2 * depth),
            ("rec", "seq"),
            split_axis=0,
            concat_axis=0,
            tiled=True,
        )
        summed = jnp.sum(pieces.reshape(rec_count, heads, rows_out, 2 * depth), axis=0)
        weight_grad = jnp.transpose(summed, (1, 0, 2))
    else:
        weight_grad = lax.psum_scatter(
            jnp.einsum("td,htc->dhc", tokens, grad_proj, preferred_element_type=jnp.float32),
            ("rec", "seq"),
            scatter_dimension=0,
            tiled=True,
        )
    return (attention, seq_grad, weight_grad)


def solution(mesh):
    placed = (P("rec", "seq", None), P("rec", "seq"), P(), P(), P(), P("rec", None, "seq", None))
    return jax.shard_map(
        local,
        mesh=mesh,
        in_specs=placed,
        out_specs=(
            P("rec", None, "seq", None),
            P("rec", "seq", None),
            P(("rec", "seq"), None, None),
        ),
        check_vma=False,
    )
```

```python
import functools

import jax
import jax.numpy as jnp
from jax import lax
from jax.sharding import PartitionSpec as P
from jax.experimental import pallas as pl
from jax.experimental.pallas import tpu as pltpu

BLOCK = 128


def attention_kernel(lists_ref, counts_ref, both_ref, grad_ref, out_ref, back_ref, acc_ref):
    nblocks, listed = lists_ref.shape
    depth = grad_ref.shape[1]
    scale = depth ** (-0.5)
    acc_ref[...] = jnp.zeros(acc_ref.shape, jnp.float32)
    trans_a = (((0,), (0,)), ((), ()))
    trans_b = (((1,), (1,)), ((), ()))

    def attend(a, used):
        start = pl.multiple_of(a * BLOCK, BLOCK)
        query = both_ref[pl.ds(start, BLOCK), :][:, :depth]
        upstream = grad_ref[pl.ds(start, BLOCK), :]
        picks = [jnp.clip(lists_ref[a, j], 0, nblocks - 1) for j in range(used)]
        tiles = [both_ref[pl.ds(pl.multiple_of(b * BLOCK, BLOCK), BLOCK), :] for b in picks]
        near = tiles[0] if used == 1 else jnp.concatenate(tiles, axis=0)
        keys = near[:, :depth]
        values = near[:, depth:]
        scores = lax.dot_general(query, keys, trans_b, preferred_element_type=jnp.float32) * scale
        peak = jnp.max(scores, axis=1, keepdims=True)
        weights = jnp.exp(scores - peak)
        probs = weights / jnp.sum(weights, axis=1, keepdims=True)
        probs_low = probs.astype(jnp.bfloat16)
        mixed = jnp.dot(probs_low, values, preferred_element_type=jnp.float32)
        out_ref[pl.ds(start, BLOCK), :] = mixed.astype(out_ref.dtype)
        dprobs = lax.dot_general(upstream, values, trans_b, preferred_element_type=jnp.float32)
        inner = jnp.sum(probs * dprobs, axis=1, keepdims=True)
        dscores = (scale * probs * (dprobs - inner)).astype(jnp.bfloat16)
        dquery = jnp.dot(dscores, keys, preferred_element_type=jnp.float32)
        dkeys = lax.dot_general(dscores, query, trans_a, preferred_element_type=jnp.float32)
        dvalues = lax.dot_general(probs_low, upstream, trans_a, preferred_element_type=jnp.float32)
        both_grads = jnp.concatenate([dkeys, dvalues], axis=1)
        for j in range(used):
            part = both_grads[j * BLOCK:(j + 1) * BLOCK]
            if j == 0:
                part = part + jnp.concatenate([dquery, jnp.zeros_like(dquery)], axis=1)
            rows = pl.ds(pl.multiple_of(picks[j] * BLOCK, BLOCK), BLOCK)
            acc_ref[rows, :] += part

    def one_block(a, carry):
        active = jnp.clip(counts_ref[a], 1, listed)
        lax.switch(active - 1, [functools.partial(attend, a, used) for used in range(1, listed + 1)])
        return carry

    lax.fori_loop(0, nblocks, one_block, 0)
    back_ref[...] = acc_ref[...].astype(back_ref.dtype)


def attend_group(both, grad_rows, lists, counts):
    total, width = both.shape
    depth = grad_rows.shape[1]
    smem = pltpu.MemorySpace.SMEM
    vmem = pltpu.MemorySpace.VMEM
    return pl.pallas_call(
        attention_kernel,
        out_shape=(
            jax.ShapeDtypeStruct((total, depth), jnp.bfloat16),
            jax.ShapeDtypeStruct((total, width), jnp.bfloat16),
        ),
        in_specs=[
            pl.BlockSpec(memory_space=smem),
            pl.BlockSpec(memory_space=smem),
            pl.BlockSpec(memory_space=vmem),
            pl.BlockSpec(memory_space=vmem),
        ],
        out_specs=(pl.BlockSpec(memory_space=vmem), pl.BlockSpec(memory_space=vmem)),
        scratch_shapes=[pltpu.VMEM((total, width), jnp.float32)],
    )(lists, counts, both, grad_rows)


def route_tokens(rows_here, targets, seq_count, my_index):
    tokens_here, width = rows_here.shape
    room = 2 * tokens_here // seq_count - 1
    holders = targets // tokens_here
    order_ids = jnp.arange(tokens_here)
    earlier = order_ids[None, :] < order_ids[:, None]
    same_holder = holders[:, None] == holders[None, :]
    ranked = jnp.sum((earlier & same_holder).astype(jnp.int32), axis=1)
    slot_ids = holders * room + ranked
    outgoing = jnp.zeros((seq_count * room, width), rows_here.dtype).at[slot_ids].set(rows_here)
    outgoing = outgoing.reshape(seq_count, room, width)
    labels = (
        jnp.full((seq_count * room,), -1, jnp.int32)
        .at[slot_ids]
        .set(targets)
        .reshape(seq_count, room)
    )
    arrived, arrived_pos = (
        lax.all_to_all(outgoing, "seq", split_axis=0, concat_axis=0, tiled=True),
        lax.all_to_all(labels, "seq", split_axis=0, concat_axis=0, tiled=True),
    )
    local_ids = jnp.where(
        arrived_pos >= 0, arrived_pos - my_index * tokens_here, tokens_here
    ).reshape(-1)
    return (
        jnp.zeros((tokens_here, width), rows_here.dtype)
        .at[local_ids]
        .set(arrived.reshape(-1, width), mode="drop")
    )


def local(owned_rows, seq_position, head_weights, key_blocks, key_counts, out_grad):
    seq_count = lax.axis_size("seq")
    rec_count = lax.axis_size("rec")
    my_index = lax.axis_index("seq")
    tokens_here = owned_rows.shape[1]
    width = owned_rows.shape[2]
    heads = head_weights.shape[1]
    depth = head_weights.shape[2] // 2
    groups = seq_count // heads
    portion = tokens_here // groups
    rows_here = owned_rows[0]
    targets = seq_position[0]
    group = my_index % groups
    upstream = out_grad[0].reshape(seq_count, portion, depth)
    got_grad = lax.all_to_all(upstream, "seq", split_axis=0, concat_axis=0, tiled=True)
    grad_rows = got_grad.reshape(seq_count * portion, depth)
    if groups == 1:
        places_all = lax.all_to_all(
            jnp.broadcast_to(targets[None], (seq_count, tokens_here)),
            "seq",
            split_axis=0,
            concat_axis=0,
            tiled=True,
        ).reshape(-1)
        proj_mine = jnp.einsum(
            "td,dhc->htc", rows_here, head_weights, preferred_element_type=jnp.float32
        ).astype(jnp.bfloat16)
        proj_owned = lax.all_to_all(
            proj_mine, "seq", split_axis=0, concat_axis=0, tiled=True
        ).reshape(seq_count * tokens_here, 2 * depth)
        later_rows, proj_owned, grad_rows = lax.optimization_barrier(
            (rows_here, proj_owned, grad_rows)
        )
        owned_all = lax.all_gather(later_rows, "seq", axis=0, tiled=True)
        slots = jnp.arange(places_all.shape[0], dtype=places_all.dtype)
        placing = (slots[:, None] == places_all[None, :]).astype(jnp.bfloat16)
        gathered = jnp.dot(placing, proj_owned, preferred_element_type=jnp.float32).astype(
            jnp.bfloat16
        )
    else:
        tokens = route_tokens(rows_here, targets, seq_count, my_index)
        proj = jnp.einsum(
            "td,dhc->htc", tokens, head_weights, preferred_element_type=jnp.float32
        ).astype(jnp.bfloat16)
        sending = proj.reshape(seq_count, portion * 2 * depth)
        got = lax.all_to_all(sending, "seq", split_axis=0, concat_axis=0, tiled=True)
        gathered = got.reshape(seq_count * portion, 2 * depth)
    mixed, grad_both = attend_group(gathered, grad_rows, key_blocks[group], key_counts[group])
    back = lax.all_to_all(
        jnp.concatenate([mixed, grad_both], axis=1).reshape(seq_count, portion, 3 * depth),
        "seq",
        split_axis=0,
        concat_axis=0,
        tiled=True,
    )
    back_out = back[:, :, :depth]
    back_grad = back[:, :, depth:]
    attention = back_out.reshape(heads, tokens_here, depth)[None]
    grad_proj = back_grad.reshape(heads, tokens_here, 2 * depth)
    seq_grad = jnp.einsum(
        "htc,dhc->td", grad_proj, head_weights, preferred_element_type=jnp.float32
    ).astype(jnp.bfloat16)[None]
    if groups == 1:
        rows_out = width // (rec_count * seq_count)
        head_grad = lax.optimization_barrier(
            lax.dot_general(
                placing, grad_both, (((0,), (0,)), ((), ())), preferred_element_type=jnp.float32
            ).astype(jnp.bfloat16)
        )
        partial = jnp.einsum(
            "oc,od->cd", head_grad, owned_all, preferred_element_type=jnp.float32
        ).T
        pieces = lax.all_to_all(
            partial.reshape(rec_count * seq_count, rows_out, 2 * depth),
            ("rec", "seq"),
            split_axis=0,
            concat_axis=0,
            tiled=True,
        )
        summed = jnp.sum(pieces.reshape(rec_count, heads, rows_out, 2 * depth), axis=0)
        weight_grad = jnp.transpose(summed, (1, 0, 2))
    else:
        weight_grad = lax.psum_scatter(
            jnp.einsum("td,htc->dhc", tokens, grad_proj, preferred_element_type=jnp.float32),
            ("rec", "seq"),
            scatter_dimension=0,
            tiled=True,
        )
    return (attention, seq_grad, weight_grad)


def solution(mesh):
    placed = (P("rec", "seq", None), P("rec", "seq"), P(), P(), P(), P("rec", None, "seq", None))
    return jax.shard_map(
        local,
        mesh=mesh,
        in_specs=placed,
        out_specs=(
            P("rec", None, "seq", None),
            P("rec", "seq", None),
            P(("rec", "seq"), None, None),
        ),
        check_vma=False,
    )
```
